128 devices in a mesh: tm: 16 (over y, z), rows: 8 (over x, core).
Axes of the slice: x: 4, y: 4, z: 4, core: 2. Of those that a mesh axis runs over, the one named last changes fastest.
Arguments:
- generator_latent_rows: bfloat16 [16, 64, 2560], P('tm', 'rows'), may hold values from -6 to 6
- slot_group_row: int32 [16, 64], P('tm', 'rows'), may hold values from 0 to 63, each once within a row
- frame_clip_number: int32 [64], replicated, may hold values from 0 to 4, never falling along the last dimension, each value on 1 to 21 neighbouring positions
- input_convolution_weight: bfloat16 [3, 3, 3, 16, 384], replicated, may hold values from -0.3125 to 0.3125
- first_norm_gain: float32 [384], replicated, may hold values from 0.5 to 1.5
- first_convolution_weight: bfloat16 [3, 3, 3, 384, 384], replicated, may hold values from -0.0625 to 0.0625
- second_norm_gain: float32 [384], replicated, may hold values from 0.5 to 1.5
- second_convolution_weight: bfloat16 [3, 3, 3, 384, 384], replicated, may hold values from -0.0625 to 0.0625
Outputs:
- decoded: bfloat16 [64, 16, 160, 384], P('tm', 'rows')
The draws below stay inside these ranges and needn't reach their ends.
Inputs may be any that keep to these rules, and one draw needn't show every extreme that they name: For each frame group, slot_group_row lists every row index of the group's 4 frames once: slot j holds the group's row (f % 4) * 16 + h.
All inputs are finite; a program needn't handle non-finite values.
Results may differ from the reference program's by a relative error of at most 0.0058.
Values may be sent and summed in bfloat16 or wider, within the bound.
No kernel may reach another device: no remote copies, remote signals or barrier semaphores. Data moves between devices by JAX's collectives and lax.ppermute only.
A program may use at most 128 MiB of HBM per device.

```python
import math
import jax
import jax.numpy as jnp
import numpy as np
from jax import lax

C = 384
LATENT_CHANNELS = 16
LATENT_COLUMNS = 160
F_DEV = 4
CLIP_MOST = 21
FRAME_GROUPS = 16
FRAMES = 64
H = 16
ROWS_PER_GROUP = 64
CLIPS = 5


def steps_of(stream_key, extent, cuts, low, top_value):
    factor_of, own = 1.0, jax.random.fold_in(stream_key, 6)
    for position, blocks in cuts:
        heights = jnp.exp(jax.random.uniform(jax.random.fold_in(own, position), (blocks,), jnp.float32, low / len(cuts), top_value / len(cuts)))
        factor_of = factor_of * jnp.repeat(heights, extent[position] // blocks).reshape([-1 if axis == position else 1 for axis in range(len(extent))])
    return factor_of


def split_up(number_of, total, reach, slope):
    loads = [(1 << 20) // math.isqrt(standing ** slope) + 1 for standing in range(2, number_of + 1)]
    rest, counts = total - reach - (number_of - 1), [1] * (number_of - 1)
    while rest > 0:
        movable = [i for i in range(number_of - 1) if counts[i] < reach]
        pool, budget = sum([loads[i] for i in movable]), rest
        for i in movable:
            extra = min(reach - counts[i], max(1, budget * loads[i] // pool), rest)
            counts[i] = counts[i] + extra
            rest = rest - extra
    return np.array([reach] + counts)


def uneven(rng, amount, total, limit, lean):
    if amount == 2:
        one = jax.random.randint(rng, (), max(1, total - limit), min(limit, total - 1) + 1)
        return jnp.stack([one, total - one])
    sizes = jnp.asarray(split_up(amount, total, limit, lean), jnp.int32)
    twos = (amount - 1) // 2
    donor, sink = sizes[1:1 + 2 * twos:2], sizes[2:2 + 2 * twos:2]
    room = jnp.minimum(donor - 1, limit - sink)
    passed = jax.random.randint(jax.random.fold_in(rng, 1), (twos,), 0, 1 << 20) % (room + 1)
    sizes = sizes.at[1:1 + 2 * twos:2].set(donor - passed).at[2:2 + 2 * twos:2].set(sink + passed)
    return sizes[jax.random.permutation(jax.random.fold_in(rng, 2), amount)]


def noise(rng, shape, deviation, most, pieces=(), held_as=jnp.bfloat16):
    loudness = steps_of(rng, shape, pieces, -0.22, 0.18) if pieces else 1.0
    array = jax.random.normal(rng, shape, jnp.float32) * deviation * loudness
    return jnp.minimum(jnp.maximum(array, -most), most).astype(held_as)


def setup_inputs(seed: int = 0) -> dict:
    seeds = jax.random.split(jax.random.key(seed), 9)
    generator_latent_rows = noise(seeds[0], (FRAME_GROUPS, ROWS_PER_GROUP, LATENT_COLUMNS * LATENT_CHANNELS), 1.0, 6.0, ((0, 16), (1, 8)))
    slot_group_row = jax.vmap(lambda own: jax.random.permutation(own, ROWS_PER_GROUP))(jax.random.split(seeds[1], FRAME_GROUPS)).reshape((FRAME_GROUPS, ROWS_PER_GROUP)).astype(jnp.int32)
    frame_clip_number = jnp.searchsorted(jnp.cumsum(uneven(seeds[2], CLIPS, FRAMES, CLIP_MOST, 2)), jnp.arange(FRAMES), side="right").astype(jnp.int32)
    input_convolution_weight = noise(seeds[3], (3, 3, 3, LATENT_CHANNELS, C), (27 * LATENT_CHANNELS) ** -0.5, 0.3125)
    first_norm_gain = jnp.clip(1.0 + 0.1 * jax.random.normal(seeds[4], (C,), jnp.float32), 0.5, 1.5)
    first_convolution_weight = noise(seeds[5], (3, 3, 3, C, C), (27 * C) ** -0.5, 0.0625)
    second_norm_gain = jnp.clip(1.0 + 0.1 * jax.random.normal(seeds[6], (C,), jnp.float32), 0.5, 1.5)
    second_convolution_weight = noise(seeds[7], (3, 3, 3, C, C), (27 * C) ** -0.5, 0.0625)
    return dict(generator_latent_rows=generator_latent_rows, slot_group_row=slot_group_row, frame_clip_number=frame_clip_number, input_convolution_weight=input_convolution_weight, first_norm_gain=first_norm_gain, first_convolution_weight=first_convolution_weight, second_norm_gain=second_norm_gain, second_convolution_weight=second_convolution_weight)


EPSILON = 1e-06

def clip_masks(frame_clip_number):
    frame_count = frame_clip_number.shape[0]
    padded = jnp.concatenate([jnp.full((2,), -1, jnp.int32), frame_clip_number.astype(jnp.int32)])
    current = padded[2:]
    return [padded[shift_at:shift_at + frame_count] == current for shift_at in range(3)]

def causal_conv(field, weight, keep_masks):
    frame_count, height, columns, channels = field.shape
    outputs = weight.shape[-1]
    padded = jnp.pad(field, ((2, 0), (1, 1), (1, 1), (0, 0)))
    running = jnp.zeros((frame_count, height, columns, outputs), jnp.float32)
    for tap_time in range(3):
        partial_value = jnp.zeros((frame_count * height * columns, outputs), jnp.float32)
        for tap_row in range(3):
            for tap_col in range(3):
                window = padded[tap_time:tap_time + frame_count, tap_row:tap_row + height, tap_col:tap_col + columns]
                partial_value = partial_value + jnp.dot(window.reshape(-1, channels), weight[tap_time, tap_row, tap_col], preferred_element_type=jnp.float32)
        partial_value = partial_value.reshape(frame_count, height, columns, outputs)
        running = running + jnp.where(keep_masks[tap_time][:, None, None, None], partial_value, jnp.float32(0.0))
    return running

def norm_act(field, gain_vec):
    values_f = field.astype(jnp.float32)
    inverse = lax.rsqrt(lax.optimization_barrier(jnp.mean(values_f * values_f, axis=-1, keepdims=True)) + EPSILON)
    return jax.nn.silu(values_f * inverse * gain_vec.astype(jnp.float32)).astype(jnp.bfloat16)

def reference(generator_latent_rows, slot_group_row, frame_clip_number, input_convolution_weight, first_norm_gain, first_convolution_weight, second_norm_gain, second_convolution_weight):
    frame_groups = generator_latent_rows.shape[0]
    frame_group_index = jnp.arange(frame_groups).astype(jnp.int32)[:, None]
    sorted_rows = jnp.zeros_like(generator_latent_rows).at[frame_group_index, slot_group_row.astype(jnp.int32)].set(generator_latent_rows)
    latent = sorted_rows.reshape(frame_groups * F_DEV, H, LATENT_COLUMNS, LATENT_CHANNELS)
    keep_masks = clip_masks(frame_clip_number)
    base_field = causal_conv(latent, input_convolution_weight, keep_masks).astype(jnp.bfloat16)
    base_field = lax.optimization_barrier(base_field)
    first_act = norm_act(base_field, first_norm_gain)
    middle = causal_conv(first_act, first_convolution_weight, keep_masks).astype(jnp.bfloat16)
    middle = lax.optimization_barrier(middle)
    second_act = norm_act(middle, second_norm_gain)
    decoded = base_field.astype(jnp.float32) + causal_conv(second_act, second_convolution_weight, keep_masks)
    return decoded.astype(jnp.bfloat16)
```

```python
import functools

import jax
import jax.numpy as jnp
from jax import lax
from jax.experimental import pallas as pl
from jax.experimental.pallas import tpu as pltpu
from jax.sharding import PartitionSpec as P

LATENT_CHANNELS = 16
F_DEV = 4
ID_LANES = 128

EPSILON = 1e-06


def shifted(x, axis, by):
    devices = lax.axis_size(axis)
    pairs = [(i, i + by) for i in range(devices) if 0 <= i + by < devices]
    return lax.ppermute(x, axis, pairs)


def diagonal(x, by_tm, by_rows):
    groups, parts = lax.axis_size("tm"), lax.axis_size("rows")
    pairs = []
    for g in range(groups):
        for r in range(parts):
            dg, dr = g + by_tm, r + by_rows
            if 0 <= dg < groups and 0 <= dr < parts:
                pairs.append((g * parts + r, dg * parts + dr))
    return lax.ppermute(x, ("tm", "rows"), pairs)


def norm_act(field, gain_vec):
    values_f = field.astype(jnp.float32)
    inverse = lax.rsqrt(jnp.mean(values_f * values_f, axis=-1, keepdims=True) + EPSILON)
    return jax.nn.silu(values_f * inverse * gain_vec).astype(jnp.bfloat16)


def local_conv(extended, weight, keep_masks):
    frame_count = extended.shape[0] - 2
    height = extended.shape[1] - 2
    columns = extended.shape[2]
    channels = extended.shape[3]
    outputs = weight.shape[-1]
    padded = jnp.pad(extended, ((0, 0), (0, 0), (1, 1), (0, 0)))
    running = jnp.zeros((frame_count, height, columns, outputs), jnp.float32)
    for tap_time in range(3):
        pieces = []
        for tap_row in range(3):
            for tap_col in range(3):
                pieces.append(
                    padded[
                        tap_time : tap_time + frame_count,
                        tap_row : tap_row + height,
                        tap_col : tap_col + columns,
                    ]
                )
        stacked = jnp.concatenate(pieces, axis=-1).reshape(-1, 9 * channels)
        partial_value = jnp.dot(
            stacked,
            weight[tap_time].reshape(9 * channels, outputs),
            preferred_element_type=jnp.float32,
        )
        partial_value = partial_value.reshape(frame_count, height, columns, outputs)
        running = running + jnp.where(
            keep_masks[tap_time][:, None, None, None], partial_value, jnp.float32(0.0)
        )
    return running


def conv_kernel(keep_ref, x_ref, w_ref, side_ref, o_ref, col_ref, *, mode):
    frames_in, rows_in, columns, channels = x_ref.shape
    frame_count, height = frames_in - 2, rows_in - 2
    band = height * columns
    cells = frame_count * band
    for f in range(frame_count):
        for k in range(3):
            kept = keep_ref[k * frame_count + f]
            for a in range(3):
                j = k * 3 + a
                rows_at = pl.ds(f * band, band)
                lanes_at = pl.ds(j * channels, channels)

                @pl.when(kept != 0)
                def _():
                    col_ref[rows_at, lanes_at] = x_ref[f + k, a : a + height].reshape(
                        band, channels
                    )

                @pl.when(kept == 0)
                def _():
                    col_ref[rows_at, lanes_at] = jnp.zeros((band, channels), col_ref.dtype)

    col = col_ref[...]
    outputs = w_ref.shape[-1]
    position = lax.broadcasted_iota(jnp.int32, (cells, outputs), 0) % columns
    running = None
    for b in (1, 0, 2):
        weight = w_ref[:, b].reshape(9 * channels, outputs)
        part = jnp.dot(col, weight, preferred_element_type=jnp.float32)
        if b == 0:
            part = jnp.where(position == 0, 0.0, pltpu.roll(part, 1, 0))
        elif b == 2:
            part = jnp.where(position == columns - 1, 0.0, pltpu.roll(part, cells - 1, 0))
        running = part if running is None else running + part
    if mode == "act":
        values_f = running.astype(jnp.bfloat16).astype(jnp.float32)
        inverse = lax.rsqrt(jnp.mean(values_f * values_f, axis=-1, keepdims=True) + EPSILON)
        scaled = values_f * inverse * side_ref[...]
        o_ref[...] = (scaled / (1.0 + jnp.exp(-scaled))).astype(o_ref.dtype)
    else:
        o_ref[...] = (side_ref[...].astype(jnp.float32) + running).astype(o_ref.dtype)


def conv_call(extended, weight, keep, side, mode):
    frames_in, rows_in, columns, channels = extended.shape
    frame_count, height = frames_in - 2, rows_in - 2
    outputs = weight.shape[-1]
    cells = frame_count * height * columns
    weight9 = weight.reshape(9, 3, channels, outputs)
    vmem = pltpu.MemorySpace.VMEM
    out = pl.pallas_call(
        functools.partial(conv_kernel, mode=mode),
        out_shape=jax.ShapeDtypeStruct((cells, outputs), jnp.bfloat16),
        in_specs=[
            pl.BlockSpec(memory_space=pltpu.SMEM),
            pl.BlockSpec(memory_space=vmem),
            pl.BlockSpec(memory_space=vmem),
            pl.BlockSpec(memory_space=vmem),
        ],
        out_specs=pl.BlockSpec(memory_space=vmem),
        scratch_shapes=[pltpu.VMEM((cells, 9 * channels), jnp.bfloat16)],
        compiler_params=pltpu.CompilerParams(vmem_limit_bytes=60 * 1024 * 1024),
    )(keep, extended, weight9, side)
    return out.reshape(frame_count, height, columns, outputs)


def on_device(
    generator_latent_rows,
    slot_group_row,
    frame_clip_number,
    input_convolution_weight,
    first_norm_gain,
    first_convolution_weight,
    second_norm_gain,
    second_convolution_weight,
):
    frame_count = F_DEV
    slots_here = generator_latent_rows.shape[1]
    packed_rows = generator_latent_rows.shape[2]
    parts_count = lax.axis_size("rows")
    rows_here = slots_here // frame_count
    height = rows_here * parts_count
    columns = packed_rows // LATENT_CHANNELS
    band_index = lax.axis_index("rows")
    frame_group_index = lax.axis_index("tm")

    ids = jnp.broadcast_to(
        slot_group_row.astype(jnp.bfloat16)[:, :, None], (1, slots_here, ID_LANES)
    )
    packed = jnp.concatenate([generator_latent_rows, ids], axis=-1)
    earlier = shifted(packed, "tm", 1)
    both = jnp.concatenate([earlier, packed], axis=0)
    gathered = lax.all_gather(both, "rows", axis=1, tiled=True)
    values = gathered[:, :, :packed_rows]
    slot_ids = gathered[:, :, packed_rows].astype(jnp.int32)

    window_rows = rows_here + 4
    frame_of = jnp.arange(frame_count, dtype=jnp.int32)[:, None]
    row_of = band_index * rows_here - 2 + jnp.arange(window_rows, dtype=jnp.int32)[None, :]
    wanted = (frame_of * height + row_of).reshape(-1)
    valid = jnp.broadcast_to((row_of >= 0) & (row_of < height), (frame_count, window_rows)).reshape(-1)
    selector = ((wanted[None, :, None] == slot_ids[:, None, :]) & valid[None, :, None]).astype(
        jnp.bfloat16
    )
    latent = jnp.einsum("qij,qjc->qic", selector, values, preferred_element_type=jnp.float32)
    latent = latent.astype(jnp.bfloat16).reshape(
        2 * frame_count, window_rows, columns, LATENT_CHANNELS
    )

    padded_clips = jnp.concatenate([jnp.full((4,), -1, jnp.int32), frame_clip_number])
    window = lax.dynamic_slice_in_dim(padded_clips, frame_group_index * frame_count, frame_count + 4)
    current_ext = window[2:]
    keep_ext = [window[k : k + frame_count + 2] == current_ext for k in range(3)]
    current = window[4:]
    keep_own = jnp.stack(
        [(window[k + 2 : k + 2 + frame_count] == current) for k in range(3)]
    ).astype(jnp.int32).reshape(-1)

    base_ext = local_conv(latent, input_convolution_weight, keep_ext).astype(jnp.bfloat16)
    first_act = norm_act(base_ext, first_norm_gain)
    ext_rows = band_index * rows_here - 1 + jnp.arange(rows_here + 2, dtype=jnp.int32)
    row_ok = (ext_rows >= 0) & (ext_rows < height)
    first_act = jnp.where(row_ok[None, :, None, None], first_act, jnp.zeros((), jnp.bfloat16))
    base_own = base_ext[2:, 1 : 1 + rows_here]

    second_act = conv_call(
        first_act, first_convolution_weight, keep_own, second_norm_gain.reshape(1, -1), "act"
    )

    last = second_act[frame_count - 2 :]
    from_above = shifted(second_act[:, rows_here - 1 :], "rows", 1)
    from_below = shifted(second_act[:, :1], "rows", -1)
    prev_mid = shifted(last, "tm", 1)
    prev_above = diagonal(last[:, rows_here - 1 :], 1, 1)
    prev_below = diagonal(last[:, :1], 1, -1)
    top = jnp.concatenate([prev_above, prev_mid, prev_below], axis=1)
    own = jnp.concatenate([from_above, second_act, from_below], axis=1)
    extended = jnp.concatenate([top, own], axis=0)

    decoded = conv_call(
        extended,
        second_convolution_weight,
        keep_own,
        base_own.reshape(frame_count * rows_here * columns, -1),
        "res",
    )
    return decoded


def solution(mesh):
    in_specs = (P("tm", "rows", None), P("tm", "rows"), P(), P(), P(), P(), P(), P())
    out_specs = P("tm", "rows", None, None)
    return jax.shard_map(
        on_device, mesh=mesh, in_specs=in_specs, out_specs=out_specs, check_vma=False
    )
```

```python
import functools

import jax
import jax.numpy as jnp
from jax import lax
from jax.experimental import pallas as pl
from jax.experimental.pallas import tpu as pltpu
from jax.sharding import PartitionSpec as P

LATENT_CHANNELS = 16
F_DEV = 4
ID_LANES = 128

EPSILON = 1e-06


def shifted(x, axis, by):
    devices = lax.axis_size(axis)
    pairs = [(i, i + by) for i in range(devices) if 0 <= i + by < devices]
    return lax.ppermute(x, axis, pairs)


def diagonal(x, by_tm, by_rows):
    groups, parts = lax.axis_size("tm"), lax.axis_size("rows")
    pairs = []
    for g in range(groups):
        for r in range(parts):
            dg, dr = g + by_tm, r + by_rows
            if 0 <= dg < groups and 0 <= dr < parts:
                pairs.append((g * parts + r, dg * parts + dr))
    return lax.ppermute(x, ("tm", "rows"), pairs)


def norm_act(field, gain_vec):
    values_f = field.astype(jnp.float32)
    inverse = lax.rsqrt(jnp.mean(values_f * values_f, axis=-1, keepdims=True) + EPSILON)
    return jax.nn.silu(values_f * inverse * gain_vec).astype(jnp.bfloat16)


def local_conv(extended, weight, keep_masks):
    frame_count = extended.shape[0] - 2
    height = extended.shape[1] - 2
    columns = extended.shape[2]
    channels = extended.shape[3]
    outputs = weight.shape[-1]
    padded = jnp.pad(extended, ((0, 0), (0, 0), (1, 1), (0, 0)))
    running = jnp.zeros((frame_count, height, columns, outputs), jnp.float32)
    for tap_time in range(3):
        pieces = []
        for tap_row in range(3):
            for tap_col in range(3):
                pieces.append(
                    padded[
                        tap_time : tap_time + frame_count,
                        tap_row : tap_row + height,
                        tap_col : tap_col + columns,
                    ]
                )
        stacked = jnp.concatenate(pieces, axis=-1).reshape(-1, 9 * channels)
        partial_value = jnp.dot(
            stacked,
            weight[tap_time].reshape(9 * channels, outputs),
            preferred_element_type=jnp.float32,
        )
        partial_value = partial_value.reshape(frame_count, height, columns, outputs)
        running = running + jnp.where(
            keep_masks[tap_time][:, None, None, None], partial_value, jnp.float32(0.0)
        )
    return running


def conv_kernel(keep_ref, x_ref, w_hbm, side_ref, *rest, x_first, keep_first, mode):
    o_ref, col_ref, w_ref, w_sem = rest[-4:]
    step = pl.program_id(0)
    rows_in, columns, channels = x_ref.shape[1:]
    height = rows_in - 2
    band = height * columns
    frames_total = keep_ref.shape[0] // 3
    own_frame = keep_first + step

    @pl.when(step == 0)
    def _():
        for b in range(3):
            pltpu.make_async_copy(w_hbm.at[:, b], w_ref.at[b], w_sem.at[b]).start()

    for k in range(3):
        kept = keep_ref[k * frames_total + own_frame] != 0
        for a in range(3):
            j = k * 3 + a
            piece = x_ref[x_first + step + k, a : a + height].reshape(band, channels)
            col_ref[:, j * channels : (j + 1) * channels] = jnp.where(
                kept, piece, jnp.zeros_like(piece)
            )

    col = col_ref[...]
    outputs = w_ref.shape[-1]
    position = lax.broadcasted_iota(jnp.int32, (band, outputs), 0) % columns
    running = None
    for b in (1, 0, 2):

        @pl.when(step == 0)
        def _():
            pltpu.make_async_copy(w_hbm.at[:, b], w_ref.at[b], w_sem.at[b]).wait()

        weight = w_ref[b].reshape(9 * channels, outputs)
        part = jnp.dot(col, weight, preferred_element_type=jnp.float32)
        if b == 0:
            part = jnp.where(position == 0, 0.0, pltpu.roll(part, 1, 0))
        elif b == 2:
            part = jnp.where(position == columns - 1, 0.0, pltpu.roll(part, band - 1, 0))
        running = part if running is None else running + part
    if mode == "act":
        values_f = running.astype(jnp.bfloat16).astype(jnp.float32)
        inverse = lax.rsqrt(jnp.mean(values_f * values_f, axis=-1, keepdims=True) + EPSILON)
        scaled = values_f * inverse * side_ref[...]
        o_ref[...] = (scaled / (1.0 + jnp.exp(-scaled))).astype(o_ref.dtype)
    else:
        residual = side_ref[2 + own_frame, 1 : 1 + height].reshape(band, outputs)
        o_ref[...] = (residual.astype(jnp.float32) + running).astype(o_ref.dtype)


def conv_call(extended, weight, keep, side, mode, x_first, keep_first, count, total,
              out_first=0, into=None):
    rows_in, columns, channels = extended.shape[1:]
    band = (rows_in - 2) * columns
    outputs = weight.shape[-1]
    weight9 = weight.reshape(9, 3, channels, outputs)
    in_specs = [
        pl.BlockSpec(memory_space=pltpu.SMEM),
        pl.BlockSpec(extended.shape, lambda step: (0,) * extended.ndim),
        pl.BlockSpec(memory_space=pl.ANY),
        pl.BlockSpec(side.shape, lambda step: (0,) * side.ndim),
    ]
    operands = [keep, extended, weight9, side]
    aliases = {}
    if into is not None:
        in_specs.append(pl.BlockSpec(memory_space=pl.ANY))
        operands.append(into)
        aliases = {4: 0}
    return pl.pallas_call(
        functools.partial(conv_kernel, x_first=x_first, keep_first=keep_first, mode=mode),
        grid=(count,),
        out_shape=jax.ShapeDtypeStruct((total * band, outputs), jnp.bfloat16),
        in_specs=in_specs,
        out_specs=pl.BlockSpec((band, outputs), lambda step: (step + out_first, 0)),
        scratch_shapes=[
            pltpu.VMEM((band, 9 * channels), jnp.bfloat16),
            pltpu.VMEM((3, 9, channels, outputs), jnp.bfloat16),
            pltpu.SemaphoreType.DMA((3,)),
        ],
        input_output_aliases=aliases,
        cost_estimate=pl.CostEstimate(
            flops=2 * count * band * 27 * channels * outputs,
            transcendentals=count * band * outputs,
            bytes_accessed=2 * (27 * channels * outputs + extended.size + 2 * count * band * outputs),
        ),
        compiler_params=pltpu.CompilerParams(vmem_limit_bytes=60 * 1024 * 1024),
    )(*operands)


def on_device(
    generator_latent_rows,
    slot_group_row,
    frame_clip_number,
    input_convolution_weight,
    first_norm_gain,
    first_convolution_weight,
    second_norm_gain,
    second_convolution_weight,
):
    frame_count = F_DEV
    slots_here = generator_latent_rows.shape[1]
    packed_rows = generator_latent_rows.shape[2]
    parts_count = lax.axis_size("rows")
    rows_here = slots_here // frame_count
    height = rows_here * parts_count
    columns = packed_rows // LATENT_CHANNELS
    band_index = lax.axis_index("rows")
    frame_group_index = lax.axis_index("tm")

    ids = jnp.broadcast_to(
        slot_group_row.astype(jnp.bfloat16)[:, :, None], (1, slots_here, ID_LANES)
    )
    packed = jnp.concatenate([generator_latent_rows, ids], axis=-1)
    earlier = shifted(packed, "tm", 1)
    both = jnp.concatenate([earlier, packed], axis=0)
    gathered = lax.all_gather(both, "rows", axis=1, tiled=True)
    values = gathered[:, :, :packed_rows]
    slot_ids = gathered[:, :, packed_rows].astype(jnp.int32)

    window_rows = rows_here + 4
    frame_of = jnp.arange(frame_count, dtype=jnp.int32)[:, None]
    row_of = band_index * rows_here - 2 + jnp.arange(window_rows, dtype=jnp.int32)[None, :]
    wanted = (frame_of * height + row_of).reshape(-1)
    valid = jnp.broadcast_to((row_of >= 0) & (row_of < height), (frame_count, window_rows)).reshape(-1)
    selector = ((wanted[None, :, None] == slot_ids[:, None, :]) & valid[None, :, None]).astype(
        jnp.bfloat16
    )
    latent = jnp.einsum("qij,qjc->qic", selector, values, preferred_element_type=jnp.float32)
    latent = latent.astype(jnp.bfloat16).reshape(
        2 * frame_count, window_rows, columns, LATENT_CHANNELS
    )

    padded_clips = jnp.concatenate([jnp.full((4,), -1, jnp.int32), frame_clip_number])
    window = lax.dynamic_slice_in_dim(padded_clips, frame_group_index * frame_count, frame_count + 4)
    current_ext = window[2:]
    keep_ext = [window[k : k + frame_count + 2] == current_ext for k in range(3)]
    current = window[4:]
    keep_own = jnp.stack(
        [(window[k + 2 : k + 2 + frame_count] == current) for k in range(3)]
    ).astype(jnp.int32).reshape(-1)

    base_ext = local_conv(latent, input_convolution_weight, keep_ext).astype(jnp.bfloat16)
    first_act = norm_act(base_ext, first_norm_gain)
    ext_rows = band_index * rows_here - 1 + jnp.arange(rows_here + 2, dtype=jnp.int32)
    row_ok = (ext_rows >= 0) & (ext_rows < height)
    first_act = jnp.where(row_ok[None, :, None, None], first_act, jnp.zeros((), jnp.bfloat16))

    gain = second_norm_gain.reshape(1, -1)
    late = conv_call(first_act, first_convolution_weight, keep_own, gain, "act", 2, 2, 2, 2)
    late = late.reshape(2, rows_here, columns, -1)
    prev_mid = shifted(late, "tm", 1)
    prev_above = diagonal(late[:, rows_here - 1 :], 1, 1)
    prev_below = diagonal(late[:, :1], 1, -1)
    late_above = shifted(late[:, rows_here - 1 :], "rows", 1)
    late_below = shifted(late[:, :1], "rows", -1)
    early = conv_call(first_act, first_convolution_weight, keep_own, gain, "act", 0, 0, 2, 2)
    early = early.reshape(2, rows_here, columns, -1)
    early_above = shifted(early[:, rows_here - 1 :], "rows", 1)
    early_below = shifted(early[:, :1], "rows", -1)

    early_ext = jnp.concatenate([early_above, early, early_below], axis=1)
    late_ext = jnp.concatenate([late_above, late, late_below], axis=1)
    prev_ext = jnp.concatenate([prev_above, prev_mid, prev_below], axis=1)
    own_ext = jnp.concatenate([early_ext, late_ext], axis=0)
    decoded = conv_call(
        own_ext, second_convolution_weight, keep_own, base_ext, "res", 0, 2, 2, 4, out_first=2
    )
    decoded, early_ext = lax.optimization_barrier((decoded, early_ext))
    before_ext = jnp.concatenate([prev_ext, early_ext], axis=0)
    decoded = conv_call(
        before_ext, second_convolution_weight, keep_own, base_ext, "res", 0, 0, 2, 4,
        out_first=0, into=decoded,
    )
    return decoded.reshape(frame_count, rows_here, columns, -1)


def solution(mesh):
    in_specs = (P("tm", "rows", None), P("tm", "rows"), P(), P(), P(), P(), P(), P())
    out_specs = P("tm", "rows", None, None)
    return jax.shard_map(
        on_device, mesh=mesh, in_specs=in_specs, out_specs=out_specs, check_vma=False
    )
```

```python
import functools

import jax
import jax.numpy as jnp
from jax import lax
from jax.experimental import pallas as pl
from jax.experimental.pallas import tpu as pltpu
from jax.sharding import PartitionSpec as P

LATENT_CHANNELS = 16
F_DEV = 4
ID_LANES = 128

EPSILON = 1e-06


def shifted(x, axis, by):
    devices = lax.axis_size(axis)
    pairs = [(i, i + by) for i in range(devices) if 0 <= i + by < devices]
    return lax.ppermute(x, axis, pairs)


def diagonal(x, by_tm, by_rows):
    groups, parts = lax.axis_size("tm"), lax.axis_size("rows")
    pairs = []
    for g in range(groups):
        for r in range(parts):
            dg, dr = g + by_tm, r + by_rows
            if 0 <= dg < groups and 0 <= dr < parts:
                pairs.append((g * parts + r, dg * parts + dr))
    return lax.ppermute(x, ("tm", "rows"), pairs)


def norm_act(field, gain_vec):
    values_f = field.astype(jnp.float32)
    inverse = lax.rsqrt(jnp.mean(values_f * values_f, axis=-1, keepdims=True) + EPSILON)
    return jax.nn.silu(values_f * inverse * gain_vec).astype(jnp.bfloat16)


def local_conv(extended, weight, keep_masks):
    frame_count = extended.shape[0] - 2
    height = extended.shape[1] - 2
    columns = extended.shape[2]
    channels = extended.shape[3]
    outputs = weight.shape[-1]
    padded = jnp.pad(extended, ((0, 0), (0, 0), (1, 1), (0, 0)))
    running = jnp.zeros((frame_count, height, columns, outputs), jnp.float32)
    for tap_time in range(3):
        pieces = []
        for tap_row in range(3):
            for tap_col in range(3):
                pieces.append(
                    padded[
                        tap_time : tap_time + frame_count,
                        tap_row : tap_row + height,
                        tap_col : tap_col + columns,
                    ]
                )
        stacked = jnp.concatenate(pieces, axis=-1).reshape(-1, 9 * channels)
        partial_value = jnp.dot(
            stacked,
            weight[tap_time].reshape(9 * channels, outputs),
            preferred_element_type=jnp.float32,
        )
        partial_value = partial_value.reshape(frame_count, height, columns, outputs)
        running = running + jnp.where(
            keep_masks[tap_time][:, None, None, None], partial_value, jnp.float32(0.0)
        )
    return running


def conv_kernel(keep_ref, *refs, layout, mode):
    sources = refs[: len(layout)]
    w_hbm, side_ref, o_ref, col_ref, w_ref, w_sem = refs[len(layout) :]
    columns, channels = sources[0].shape[-2:]
    frame_count = keep_ref.shape[0] // 3
    cells = col_ref.shape[0]
    band = cells // frame_count
    height = band // columns
    copies = [pltpu.make_async_copy(w_hbm.at[:, b], w_ref.at[b], w_sem.at[b]) for b in range(3)]
    for b in (1, 0, 2):
        copies[b].start()

    def row_of(ext_frame, ext_row):
        for name, (frame_lo, frame_hi, row_lo, row_hi) in layout.items():
            if frame_lo <= ext_frame < frame_hi and row_lo <= ext_row < row_hi:
                return sources[list(layout).index(name)][ext_frame - frame_lo, ext_row - row_lo]
        raise ValueError("no source")

    for f in range(frame_count):
        for k in range(3):
            kept = keep_ref[k * frame_count + f] != 0
            for a in range(3):
                j = k * 3 + a
                for i in range(height):
                    piece = row_of(f + k, a + i)
                    col_ref[pl.ds(f * band + i * columns, columns), pl.ds(j * channels, channels)] = (
                        jnp.where(kept, piece, jnp.zeros_like(piece))
                    )

    col = col_ref[...]
    outputs = w_ref.shape[-1]
    position = lax.broadcasted_iota(jnp.int32, (cells, outputs), 0) % columns
    running = None
    for b in (1, 0, 2):
        copies[b].wait()
        weight = w_ref[b].reshape(9 * channels, outputs)
        part = jnp.dot(col, weight, preferred_element_type=jnp.float32)
        if b == 0:
            part = jnp.where(position == 0, 0.0, pltpu.roll(part, 1, 0))
        elif b == 2:
            part = jnp.where(position == columns - 1, 0.0, pltpu.roll(part, cells - 1, 0))
        running = part if running is None else running + part
    if mode == "act":
        values_f = running.astype(jnp.bfloat16).astype(jnp.float32)
        inverse = lax.rsqrt(jnp.mean(values_f * values_f, axis=-1, keepdims=True) + EPSILON)
        scaled = values_f * inverse * side_ref[...]
        o_ref[...] = (scaled / (1.0 + jnp.exp(-scaled))).astype(o_ref.dtype)
    else:
        residual = side_ref[2 : 2 + frame_count, 1 : 1 + height].reshape(cells, outputs)
        o_ref[...] = (residual.astype(jnp.float32) + running).astype(o_ref.dtype)


def conv_call(layout, sources, weight, keep, side, mode):
    columns, channels = sources[0].shape[-2:]
    frame_count = keep.shape[0] // 3
    rows_in = max(hi for (_, _, _, hi) in layout.values())
    cells = frame_count * (rows_in - 2) * columns
    outputs = weight.shape[-1]
    weight9 = weight.reshape(9, 3, channels, outputs)
    vmem = pltpu.MemorySpace.VMEM
    out = pl.pallas_call(
        functools.partial(conv_kernel, layout=layout, mode=mode),
        out_shape=jax.ShapeDtypeStruct((cells, outputs), jnp.bfloat16),
        in_specs=[pl.BlockSpec(memory_space=pltpu.SMEM)]
        + [pl.BlockSpec(memory_space=vmem) for _ in sources]
        + [pl.BlockSpec(memory_space=pl.ANY), pl.BlockSpec(memory_space=vmem)],
        out_specs=pl.BlockSpec(memory_space=vmem),
        scratch_shapes=[
            pltpu.VMEM((cells, 9 * channels), jnp.bfloat16),
            pltpu.VMEM((3, 9, channels, outputs), jnp.bfloat16),
            pltpu.SemaphoreType.DMA((3,)),
        ],
        cost_estimate=pl.CostEstimate(
            flops=2 * cells * 27 * channels * outputs,
            transcendentals=cells * outputs,
            bytes_accessed=2 * (27 * channels * outputs + 3 * cells * outputs),
        ),
        compiler_params=pltpu.CompilerParams(vmem_limit_bytes=60 * 1024 * 1024),
    )(keep, *sources, weight9, side)
    return out.reshape(frame_count, rows_in - 2, columns, outputs)


def on_device(
    generator_latent_rows,
    slot_group_row,
    frame_clip_number,
    input_convolution_weight,
    first_norm_gain,
    first_convolution_weight,
    second_norm_gain,
    second_convolution_weight,
):
    frame_count = F_DEV
    slots_here = generator_latent_rows.shape[1]
    packed_rows = generator_latent_rows.shape[2]
    parts_count = lax.axis_size("rows")
    rows_here = slots_here // frame_count
    height = rows_here * parts_count
    columns = packed_rows // LATENT_CHANNELS
    band_index = lax.axis_index("rows")
    frame_group_index = lax.axis_index("tm")

    ids = jnp.broadcast_to(
        slot_group_row.astype(jnp.bfloat16)[:, :, None], (1, slots_here, ID_LANES)
    )
    packed = jnp.concatenate([generator_latent_rows, ids], axis=-1)
    earlier = shifted(packed, "tm", 1)
    both = jnp.concatenate([earlier, packed], axis=0)
    gathered = lax.all_gather(both, "rows", axis=1, tiled=True)
    values = gathered[:, :, :packed_rows]
    slot_ids = gathered[:, :, packed_rows].astype(jnp.int32)

    window_rows = rows_here + 4
    frame_of = jnp.arange(frame_count, dtype=jnp.int32)[:, None]
    row_of = band_index * rows_here - 2 + jnp.arange(window_rows, dtype=jnp.int32)[None, :]
    wanted = (frame_of * height + row_of).reshape(-1)
    valid = jnp.broadcast_to((row_of >= 0) & (row_of < height), (frame_count, window_rows)).reshape(-1)
    selector = ((wanted[None, :, None] == slot_ids[:, None, :]) & valid[None, :, None]).astype(
        jnp.bfloat16
    )
    latent = jnp.einsum("qij,qjc->qic", selector, values, preferred_element_type=jnp.float32)
    latent = latent.astype(jnp.bfloat16).reshape(
        2 * frame_count, window_rows, columns, LATENT_CHANNELS
    )

    padded_clips = jnp.concatenate([jnp.full((4,), -1, jnp.int32), frame_clip_number])
    window = lax.dynamic_slice_in_dim(padded_clips, frame_group_index * frame_count, frame_count + 4)
    current_ext = window[2:]
    keep_ext = [window[k : k + frame_count + 2] == current_ext for k in range(3)]
    current = window[4:]
    keep_own = jnp.stack(
        [(window[k + 2 : k + 2 + frame_count] == current) for k in range(3)]
    ).astype(jnp.int32).reshape(-1)

    base_ext = local_conv(latent, input_convolution_weight, keep_ext).astype(jnp.bfloat16)
    first_act = norm_act(base_ext, first_norm_gain)
    ext_rows = band_index * rows_here - 1 + jnp.arange(rows_here + 2, dtype=jnp.int32)
    row_ok = (ext_rows >= 0) & (ext_rows < height)
    first_act = jnp.where(row_ok[None, :, None, None], first_act, jnp.zeros((), jnp.bfloat16))

    gain = second_norm_gain.reshape(1, -1)
    ext_frames, ext_rows_n = first_act.shape[:2]
    second_act = conv_call(
        {"x": (0, ext_frames, 0, ext_rows_n)},
        [first_act],
        first_convolution_weight,
        keep_own,
        gain,
        "act",
    )

    last = second_act[frame_count - 2 :]
    from_above = shifted(second_act[:, rows_here - 1 :], "rows", 1)
    from_below = shifted(second_act[:, :1], "rows", -1)
    prev_mid = shifted(last, "tm", 1)
    prev_above = diagonal(last[:, rows_here - 1 :], 1, 1)
    prev_below = diagonal(last[:, :1], 1, -1)
    layout = {
        "own": (2, 2 + frame_count, 1, 1 + rows_here),
        "above": (2, 2 + frame_count, 0, 1),
        "below": (2, 2 + frame_count, 1 + rows_here, 2 + rows_here),
        "mid": (0, 2, 1, 1 + rows_here),
        "corner_above": (0, 2, 0, 1),
        "corner_below": (0, 2, 1 + rows_here, 2 + rows_here),
    }
    return conv_call(
        layout,
        [second_act, from_above, from_below, prev_mid, prev_above, prev_below],
        second_convolution_weight,
        keep_own,
        base_ext,
        "res",
    )


def solution(mesh):
    in_specs = (P("tm", "rows", None), P("tm", "rows"), P(), P(), P(), P(), P(), P())
    out_specs = P("tm", "rows", None, None)
    return jax.shard_map(
        on_device, mesh=mesh, in_specs=in_specs, out_specs=out_specs, check_vma=False
    )
```

```python
import functools

import jax
import jax.numpy as jnp
from jax import lax
from jax.experimental import pallas as pl
from jax.experimental.pallas import tpu as pltpu
from jax.sharding import PartitionSpec as P

LATENT_CHANNELS = 16
F_DEV = 4
ID_LANES = 128

EPSILON = 1e-06


def shifted(x, axis, by):
    devices = lax.axis_size(axis)
    pairs = [(i, i + by) for i in range(devices) if 0 <= i + by < devices]
    return lax.ppermute(x, axis, pairs)


def diagonal(x, by_tm, by_rows):
    groups, parts = lax.axis_size("tm"), lax.axis_size("rows")
    pairs = []
    for g in range(groups):
        for r in range(parts):
            dg, dr = g + by_tm, r + by_rows
            if 0 <= dg < groups and 0 <= dr < parts:
                pairs.append((g * parts + r, dg * parts + dr))
    return lax.ppermute(x, ("tm", "rows"), pairs)


def norm_act(field, gain_vec):
    values_f = field.astype(jnp.float32)
    inverse = lax.rsqrt(jnp.mean(values_f * values_f, axis=-1, keepdims=True) + EPSILON)
    return jax.nn.silu(values_f * inverse * gain_vec).astype(jnp.bfloat16)


def local_conv(extended, weight, keep_masks):
    frame_count = extended.shape[0] - 2
    height = extended.shape[1] - 2
    columns = extended.shape[2]
    channels = extended.shape[3]
    outputs = weight.shape[-1]
    padded = jnp.pad(extended, ((0, 0), (0, 0), (1, 1), (0, 0)))
    running = jnp.zeros((frame_count, height, columns, outputs), jnp.float32)
    for tap_time in range(3):
        pieces = []
        for tap_row in range(3):
            for tap_col in range(3):
                pieces.append(
                    padded[
                        tap_time : tap_time + frame_count,
                        tap_row : tap_row + height,
                        tap_col : tap_col + columns,
                    ]
                )
        stacked = jnp.concatenate(pieces, axis=-1).reshape(-1, 9 * channels)
        partial_value = jnp.dot(
            stacked,
            weight[tap_time].reshape(9 * channels, outputs),
            preferred_element_type=jnp.float32,
        )
        partial_value = partial_value.reshape(frame_count, height, columns, outputs)
        running = running + jnp.where(
            keep_masks[tap_time][:, None, None, None], partial_value, jnp.float32(0.0)
        )
    return running


def conv_kernel(keep_ref, *refs, layout, mode):
    sources = refs[: len(layout)]
    w_hbm, side_ref, o_ref, col_ref, w_ref, w_sem = refs[len(layout) :]
    columns, channels = sources[0].shape[-2:]
    frame_count = keep_ref.shape[0] // 3
    cells = col_ref.shape[0]
    band = cells // frame_count
    height = band // columns
    copies = [pltpu.make_async_copy(w_hbm.at[:, b], w_ref.at[b], w_sem.at[b]) for b in range(3)]
    for b in (1, 0, 2):
        copies[b].start()

    def row_of(ext_frame, ext_row):
        for name, (frame_lo, frame_hi, row_lo, row_hi) in layout.items():
            if frame_lo <= ext_frame < frame_hi and row_lo <= ext_row < row_hi:
                return sources[list(layout).index(name)][ext_frame - frame_lo, ext_row - row_lo]
        raise ValueError("no source")

    for f in range(frame_count):
        for k in range(3):
            kept = keep_ref[k * frame_count + f] != 0
            for a in range(3):
                j = k * 3 + a
                for i in range(height):
                    piece = row_of(f + k, a + i)
                    col_ref[pl.ds(f * band + i * columns, columns), pl.ds(j * channels, channels)] = (
                        jnp.where(kept, piece, jnp.zeros_like(piece))
                    )

    col = col_ref[...]
    outputs = w_ref.shape[-1]
    position = lax.broadcasted_iota(jnp.int32, (cells, outputs), 0) % columns
    running = None
    for b in (1, 0, 2):
        copies[b].wait()
        weight = w_ref[b].reshape(9 * channels, outputs)
        part = jnp.dot(col, weight, preferred_element_type=jnp.float32)
        if b == 0:
            part = jnp.where(position == 0, 0.0, pltpu.roll(part, 1, 0))
        elif b == 2:
            part = jnp.where(position == columns - 1, 0.0, pltpu.roll(part, cells - 1, 0))
        running = part if running is None else running + part
    if mode == "act":
        values_f = running.astype(jnp.bfloat16).astype(jnp.float32)
        inverse = lax.rsqrt(jnp.mean(values_f * values_f, axis=-1, keepdims=True) + EPSILON)
        scaled = values_f * inverse * side_ref[...]
        o_ref[...] = (scaled / (1.0 + jnp.exp(-scaled))).astype(o_ref.dtype)
    else:
        residual = side_ref[2 : 2 + frame_count, 1 : 1 + height].reshape(cells, outputs)
        o_ref[...] = (residual.astype(jnp.float32) + running).astype(o_ref.dtype)


def whole(x):
    return pl.BlockSpec(x.shape, lambda step: (0,) * x.ndim)


def conv_call(layout, sources, weight, keep, side, mode):
    columns, channels = sources[0].shape[-2:]
    frame_count = keep.shape[0] // 3
    rows_in = max(hi for (_, _, _, hi) in layout.values())
    cells = frame_count * (rows_in - 2) * columns
    outputs = weight.shape[-1]
    weight9 = weight.reshape(9, 3, channels, outputs)
    vmem = pltpu.MemorySpace.VMEM
    out = pl.pallas_call(
        functools.partial(conv_kernel, layout=layout, mode=mode),
        out_shape=jax.ShapeDtypeStruct((cells, outputs), jnp.bfloat16),
        in_specs=[pl.BlockSpec(memory_space=pltpu.SMEM)]
        + [whole(x) for x in sources]
        + [pl.BlockSpec(memory_space=pl.ANY), whole(side)],
        out_specs=pl.BlockSpec((cells, outputs), lambda step: (0, 0)),
        grid=(1,),
        scratch_shapes=[
            pltpu.VMEM((cells, 9 * channels), jnp.bfloat16),
            pltpu.VMEM((3, 9, channels, outputs), jnp.bfloat16),
            pltpu.SemaphoreType.DMA((3,)),
        ],
        cost_estimate=pl.CostEstimate(
            flops=2 * cells * 27 * channels * outputs,
            transcendentals=cells * outputs,
            bytes_accessed=2 * (27 * channels * outputs + 3 * cells * outputs),
        ),
        compiler_params=pltpu.CompilerParams(vmem_limit_bytes=60 * 1024 * 1024),
    )(keep, *sources, weight9, side)
    return out.reshape(frame_count, rows_in - 2, columns, outputs)


def on_device(
    generator_latent_rows,
    slot_group_row,
    frame_clip_number,
    input_convolution_weight,
    first_norm_gain,
    first_convolution_weight,
    second_norm_gain,
    second_convolution_weight,
):
    frame_count = F_DEV
    slots_here = generator_latent_rows.shape[1]
    packed_rows = generator_latent_rows.shape[2]
    parts_count = lax.axis_size("rows")
    rows_here = slots_here // frame_count
    height = rows_here * parts_count
    columns = packed_rows // LATENT_CHANNELS
    band_index = lax.axis_index("rows")
    frame_group_index = lax.axis_index("tm")

    ids = jnp.broadcast_to(
        slot_group_row.astype(jnp.bfloat16)[:, :, None], (1, slots_here, ID_LANES)
    )
    packed = jnp.concatenate([generator_latent_rows, ids], axis=-1)
    earlier = shifted(packed, "tm", 1)
    both = jnp.concatenate([earlier, packed], axis=0)
    parts_total = lax.axis_size("rows")
    pieces = [both]
    for by in range(1, parts_total):
        ring = [(i, (i + by) % parts_total) for i in range(parts_total)]
        pieces.append(lax.ppermute(both, "rows", ring))
    gathered = jnp.concatenate(pieces, axis=1)
    values = gathered[:, :, :packed_rows]
    slot_ids = gathered[:, :, packed_rows].astype(jnp.int32)

    window_rows = rows_here + 4
    frame_of = jnp.arange(frame_count, dtype=jnp.int32)[:, None]
    row_of = band_index * rows_here - 2 + jnp.arange(window_rows, dtype=jnp.int32)[None, :]
    wanted = (frame_of * height + row_of).reshape(-1)
    valid = jnp.broadcast_to((row_of >= 0) & (row_of < height), (frame_count, window_rows)).reshape(-1)
    selector = ((wanted[None, :, None] == slot_ids[:, None, :]) & valid[None, :, None]).astype(
        jnp.bfloat16
    )
    latent = jnp.einsum("qij,qjc->qic", selector, values, preferred_element_type=jnp.float32)
    latent = latent.astype(jnp.bfloat16).reshape(
        2 * frame_count, window_rows, columns, LATENT_CHANNELS
    )

    padded_clips = jnp.concatenate([jnp.full((4,), -1, jnp.int32), frame_clip_number])
    window = lax.dynamic_slice_in_dim(padded_clips, frame_group_index * frame_count, frame_count + 4)
    current_ext = window[2:]
    keep_ext = [window[k : k + frame_count + 2] == current_ext for k in range(3)]
    current = window[4:]
    keep_own = jnp.stack(
        [(window[k + 2 : k + 2 + frame_count] == current) for k in range(3)]
    ).astype(jnp.int32).reshape(-1)

    base_ext = local_conv(latent, input_convolution_weight, keep_ext).astype(jnp.bfloat16)
    first_act = norm_act(base_ext, first_norm_gain)
    ext_rows = band_index * rows_here - 1 + jnp.arange(rows_here + 2, dtype=jnp.int32)
    row_ok = (ext_rows >= 0) & (ext_rows < height)
    first_act = jnp.where(row_ok[None, :, None, None], first_act, jnp.zeros((), jnp.bfloat16))

    gain = second_norm_gain.reshape(1, -1)
    ext_frames, ext_rows_n = first_act.shape[:2]
    second_act = conv_call(
        {"x": (0, ext_frames, 0, ext_rows_n)},
        [first_act],
        first_convolution_weight,
        keep_own,
        gain,
        "act",
    )

    last = second_act[frame_count - 2 :]
    from_above = shifted(second_act[:, rows_here - 1 :], "rows", 1)
    from_below = shifted(second_act[:, :1], "rows", -1)
    prev_mid = shifted(last, "tm", 1)
    prev_above = diagonal(last[:, rows_here - 1 :], 1, 1)
    prev_below = diagonal(last[:, :1], 1, -1)
    layout = {
        "own": (2, 2 + frame_count, 1, 1 + rows_here),
        "above": (2, 2 + frame_count, 0, 1),
        "below": (2, 2 + frame_count, 1 + rows_here, 2 + rows_here),
        "mid": (0, 2, 1, 1 + rows_here),
        "corner_above": (0, 2, 0, 1),
        "corner_below": (0, 2, 1 + rows_here, 2 + rows_here),
    }
    return conv_call(
        layout,
        [second_act, from_above, from_below, prev_mid, prev_above, prev_below],
        second_convolution_weight,
        keep_own,
        base_ext,
        "res",
    )


def solution(mesh):
    in_specs = (P("tm", "rows", None), P("tm", "rows"), P(), P(), P(), P(), P(), P())
    out_specs = P("tm", "rows", None, None)
    return jax.shard_map(
        on_device, mesh=mesh, in_specs=in_specs, out_specs=out_specs, check_vma=False
    )
```

```python
import functools

import jax
import jax.numpy as jnp
from jax import lax
from jax.experimental import pallas as pl
from jax.experimental.pallas import tpu as pltpu
from jax.sharding import PartitionSpec as P

LATENT_CHANNELS = 16
F_DEV = 4
ID_LANES = 128

EPSILON = 1e-06


def shifted(x, axis, by):
    devices = lax.axis_size(axis)
    pairs = [(i, i + by) for i in range(devices) if 0 <= i + by < devices]
    return lax.ppermute(x, axis, pairs)


def diagonal(x, by_tm, by_rows):
    groups, parts = lax.axis_size("tm"), lax.axis_size("rows")
    pairs = []
    for g in range(groups):
        for r in range(parts):
            dg, dr = g + by_tm, r + by_rows
            if 0 <= dg < groups and 0 <= dr < parts:
                pairs.append((g * parts + r, dg * parts + dr))
    return lax.ppermute(x, ("tm", "rows"), pairs)


def norm_act(field, gain_vec):
    values_f = field.astype(jnp.float32)
    inverse = lax.rsqrt(jnp.mean(values_f * values_f, axis=-1, keepdims=True) + EPSILON)
    return jax.nn.silu(values_f * inverse * gain_vec).astype(jnp.bfloat16)


def local_conv(extended, weight, keep_masks):
    frame_count = extended.shape[0] - 2
    height = extended.shape[1] - 2
    columns = extended.shape[2]
    channels = extended.shape[3]
    outputs = weight.shape[-1]
    padded = jnp.pad(extended, ((0, 0), (0, 0), (1, 1), (0, 0)))
    running = jnp.zeros((frame_count, height, columns, outputs), jnp.float32)
    for tap_time in range(3):
        pieces = []
        for tap_row in range(3):
            for tap_col in range(3):
                pieces.append(
                    padded[
                        tap_time : tap_time + frame_count,
                        tap_row : tap_row + height,
                        tap_col : tap_col + columns,
                    ]
                )
        stacked = jnp.concatenate(pieces, axis=-1).reshape(-1, 9 * channels)
        partial_value = jnp.dot(
            stacked,
            weight[tap_time].reshape(9 * channels, outputs),
            preferred_element_type=jnp.float32,
        )
        partial_value = partial_value.reshape(frame_count, height, columns, outputs)
        running = running + jnp.where(
            keep_masks[tap_time][:, None, None, None], partial_value, jnp.float32(0.0)
        )
    return running


def conv_kernel(keep_ref, *refs, layout, mode, per_step):
    sources = refs[: len(layout)]
    w_hbm, side_ref, o_ref, col_ref, w_ref, w_sem = refs[len(layout) :]
    step = pl.program_id(0)
    steps = pl.num_programs(0)
    columns, channels = sources[0].shape[-2:]
    frame_count = keep_ref.shape[0] // 3
    cells = col_ref.shape[0]
    band = cells // per_step
    height = band // columns
    taps = 9 * channels

    def weight_copy(j, b):
        return pltpu.make_async_copy(
            w_hbm.at[pl.ds((j * 3 + b) * channels, channels)],
            w_ref.at[b, pl.ds(j * channels, channels)],
            w_sem.at[b],
        )

    def weight_wait(b):
        pltpu.make_async_copy(w_hbm.at[pl.ds(0, taps)], w_ref.at[b], w_sem.at[b]).wait()

    @pl.when(step == 0)
    def _():
        for b in (1, 0, 2):
            for j in range(9):
                weight_copy(j, b).start()

    def row_of(ext_frame, ext_row):
        for name, (frame_lo, frame_hi, row_lo, row_hi) in layout.items():
            if frame_lo <= ext_frame < frame_hi and row_lo <= ext_row < row_hi:
                return sources[list(layout).index(name)][ext_frame - frame_lo, ext_row - row_lo]
        raise ValueError("no source")

    for first in range(0, frame_count, per_step):

        @pl.when(step == first // per_step)
        def _():
            for fl in range(per_step):
                f = first + fl
                for k in range(3):
                    kept = keep_ref[k * frame_count + f] != 0
                    for a in range(3):
                        j = k * 3 + a
                        for i in range(height):
                            piece = row_of(f + k, a + i)
                            col_ref[
                                pl.ds(fl * band + i * columns, columns), pl.ds(j * channels, channels)
                            ] = jnp.where(kept, piece, jnp.zeros_like(piece))

    outputs = w_ref.shape[-1]
    position = lax.broadcasted_iota(jnp.int32, (cells, outputs), 0) % columns
    running = None
    for b in (1, 0, 2):

        @pl.when(step == 0)
        def _():
            weight_wait(b)

        part = jnp.dot(col_ref[...], w_ref[b], preferred_element_type=jnp.float32)
        if b == 0:
            part = jnp.where(position == 0, 0.0, pltpu.roll(part, 1, 0))
        elif b == 2:
            part = jnp.where(position == columns - 1, 0.0, pltpu.roll(part, cells - 1, 0))
        running = part if running is None else running + part
    if mode == "act":
        values_f = running.astype(jnp.bfloat16).astype(jnp.float32)
        inverse = lax.rsqrt(jnp.mean(values_f * values_f, axis=-1, keepdims=True) + EPSILON)
        scaled = values_f * inverse * side_ref[...]
        o_ref[...] = (scaled / (1.0 + jnp.exp(-scaled))).astype(o_ref.dtype)
    else:
        residual = side_ref[pl.ds(2 + step * per_step, per_step), 1 : 1 + height]
        o_ref[...] = (residual.reshape(cells, outputs).astype(jnp.float32) + running).astype(
            o_ref.dtype
        )


def whole(x):
    return pl.BlockSpec(x.shape, lambda step: (0,) * x.ndim)


def conv_call(layout, sources, weight, keep, side, mode, per_step=2):
    columns, channels = sources[0].shape[-2:]
    frame_count = keep.shape[0] // 3
    rows_in = max(hi for (_, _, _, hi) in layout.values())
    band = (rows_in - 2) * columns
    cells = frame_count * band
    outputs = weight.shape[-1]
    weight_rows = weight.reshape(27 * channels, outputs)
    out = pl.pallas_call(
        functools.partial(conv_kernel, layout=layout, mode=mode, per_step=per_step),
        out_shape=jax.ShapeDtypeStruct((cells, outputs), jnp.bfloat16),
        in_specs=[pl.BlockSpec(memory_space=pltpu.SMEM)]
        + [whole(x) for x in sources]
        + [pl.BlockSpec(memory_space=pl.ANY), whole(side)],
        out_specs=pl.BlockSpec((per_step * band, outputs), lambda step: (step, 0)),
        grid=(frame_count // per_step,),
        scratch_shapes=[
            pltpu.VMEM((per_step * band, 9 * channels), jnp.bfloat16),
            pltpu.VMEM((3, 9 * channels, outputs), jnp.bfloat16),
            pltpu.SemaphoreType.DMA((3,)),
        ],
        cost_estimate=pl.CostEstimate(
            flops=2 * cells * 27 * channels * outputs,
            transcendentals=cells * outputs,
            bytes_accessed=2 * (27 * channels * outputs + 3 * cells * outputs),
        ),
        compiler_params=pltpu.CompilerParams(vmem_limit_bytes=60 * 1024 * 1024),
    )(keep, *sources, weight_rows, side)
    return out.reshape(frame_count, rows_in - 2, columns, outputs)


def on_device(
    generator_latent_rows,
    slot_group_row,
    frame_clip_number,
    input_convolution_weight,
    first_norm_gain,
    first_convolution_weight,
    second_norm_gain,
    second_convolution_weight,
):
    frame_count = F_DEV
    slots_here = generator_latent_rows.shape[1]
    packed_rows = generator_latent_rows.shape[2]
    parts_count = lax.axis_size("rows")
    rows_here = slots_here // frame_count
    height = rows_here * parts_count
    columns = packed_rows // LATENT_CHANNELS
    band_index = lax.axis_index("rows")
    frame_group_index = lax.axis_index("tm")

    ids = jnp.broadcast_to(
        slot_group_row.astype(jnp.bfloat16)[:, :, None], (1, slots_here, ID_LANES)
    )
    packed = jnp.concatenate([generator_latent_rows, ids], axis=-1)
    earlier = shifted(packed, "tm", 1)
    both = jnp.concatenate([earlier, packed], axis=0)
    parts_total = lax.axis_size("rows")
    pieces = [both]
    for by in range(1, parts_total):
        ring = [(i, (i + by) % parts_total) for i in range(parts_total)]
        pieces.append(lax.ppermute(both, "rows", ring))
    gathered = jnp.concatenate(pieces, axis=1)
    values = gathered[:, :, :packed_rows]
    slot_ids = gathered[:, :, packed_rows].astype(jnp.int32)

    window_rows = rows_here + 4
    frame_of = jnp.arange(frame_count, dtype=jnp.int32)[:, None]
    row_of = band_index * rows_here - 2 + jnp.arange(window_rows, dtype=jnp.int32)[None, :]
    wanted = (frame_of * height + row_of).reshape(-1)
    valid = jnp.broadcast_to((row_of >= 0) & (row_of < height), (frame_count, window_rows)).reshape(-1)
    selector = ((wanted[None, :, None] == slot_ids[:, None, :]) & valid[None, :, None]).astype(
        jnp.bfloat16
    )
    latent = jnp.einsum("qij,qjc->qic", selector, values, preferred_element_type=jnp.float32)
    latent = latent.astype(jnp.bfloat16).reshape(
        2 * frame_count, window_rows, columns, LATENT_CHANNELS
    )

    padded_clips = jnp.concatenate([jnp.full((4,), -1, jnp.int32), frame_clip_number])
    window = lax.dynamic_slice_in_dim(padded_clips, frame_group_index * frame_count, frame_count + 4)
    current_ext = window[2:]
    keep_ext = [window[k : k + frame_count + 2] == current_ext for k in range(3)]
    current = window[4:]
    keep_own = jnp.stack(
        [(window[k + 2 : k + 2 + frame_count] == current) for k in range(3)]
    ).astype(jnp.int32).reshape(-1)

    base_ext = local_conv(latent, input_convolution_weight, keep_ext).astype(jnp.bfloat16)
    first_act = norm_act(base_ext, first_norm_gain)
    ext_rows = band_index * rows_here - 1 + jnp.arange(rows_here + 2, dtype=jnp.int32)
    row_ok = (ext_rows >= 0) & (ext_rows < height)
    first_act = jnp.where(row_ok[None, :, None, None], first_act, jnp.zeros((), jnp.bfloat16))

    gain = second_norm_gain.reshape(1, -1)
    ext_frames, ext_rows_n = first_act.shape[:2]
    second_act = conv_call(
        {"x": (0, ext_frames, 0, ext_rows_n)},
        [first_act],
        first_convolution_weight,
        keep_own,
        gain,
        "act",
    )

    last = second_act[frame_count - 2 :]
    from_above = shifted(second_act[:, rows_here - 1 :], "rows", 1)
    from_below = shifted(second_act[:, :1], "rows", -1)
    prev_mid = shifted(last, "tm", 1)
    prev_above = diagonal(last[:, rows_here - 1 :], 1, 1)
    prev_below = diagonal(last[:, :1], 1, -1)
    layout = {
        "own": (2, 2 + frame_count, 1, 1 + rows_here),
        "above": (2, 2 + frame_count, 0, 1),
        "below": (2, 2 + frame_count, 1 + rows_here, 2 + rows_here),
        "mid": (0, 2, 1, 1 + rows_here),
        "corner_above": (0, 2, 0, 1),
        "corner_below": (0, 2, 1 + rows_here, 2 + rows_here),
    }
    return conv_call(
        layout,
        [second_act, from_above, from_below, prev_mid, prev_above, prev_below],
        second_convolution_weight,
        keep_own,
        base_ext,
        "res",
    )


def solution(mesh):
    in_specs = (P("tm", "rows", None), P("tm", "rows"), P(), P(), P(), P(), P(), P())
    out_specs = P("tm", "rows", None, None)
    return jax.shard_map(
        on_device, mesh=mesh, in_specs=in_specs, out_specs=out_specs, check_vma=False
    )
```

```python
import functools

import jax
import jax.numpy as jnp
from jax import lax
from jax.experimental import pallas as pl
from jax.experimental.pallas import tpu as pltpu
from jax.sharding import PartitionSpec as P

LATENT_CHANNELS = 16
F_DEV = 4
ID_LANES = 128

EPSILON = 1e-06


def shifted(x, axis, by):
    devices = lax.axis_size(axis)
    pairs = [(i, i + by) for i in range(devices) if 0 <= i + by < devices]
    return lax.ppermute(x, axis, pairs)


def diagonal(x, by_tm, by_rows):
    groups, parts = lax.axis_size("tm"), lax.axis_size("rows")
    pairs = []
    for g in range(groups):
        for r in range(parts):
            dg, dr = g + by_tm, r + by_rows
            if 0 <= dg < groups and 0 <= dr < parts:
                pairs.append((g * parts + r, dg * parts + dr))
    return lax.ppermute(x, ("tm", "rows"), pairs)


def norm_act(field, gain_vec):
    values_f = field.astype(jnp.float32)
    inverse = lax.rsqrt(jnp.mean(values_f * values_f, axis=-1, keepdims=True) + EPSILON)
    return jax.nn.silu(values_f * inverse * gain_vec).astype(jnp.bfloat16)


def local_conv(extended, weight, keep_masks):
    frame_count = extended.shape[0] - 2
    height = extended.shape[1] - 2
    columns = extended.shape[2]
    channels = extended.shape[3]
    outputs = weight.shape[-1]
    padded = jnp.pad(extended, ((0, 0), (0, 0), (1, 1), (0, 0)))
    running = jnp.zeros((frame_count, height, columns, outputs), jnp.float32)
    for tap_time in range(3):
        pieces = []
        for tap_row in range(3):
            for tap_col in range(3):
                pieces.append(
                    padded[
                        tap_time : tap_time + frame_count,
                        tap_row : tap_row + height,
                        tap_col : tap_col + columns,
                    ]
                )
        stacked = jnp.concatenate(pieces, axis=-1).reshape(-1, 9 * channels)
        partial_value = jnp.dot(
            stacked,
            weight[tap_time].reshape(9 * channels, outputs),
            preferred_element_type=jnp.float32,
        )
        partial_value = partial_value.reshape(frame_count, height, columns, outputs)
        running = running + jnp.where(
            keep_masks[tap_time][:, None, None, None], partial_value, jnp.float32(0.0)
        )
    return running


def conv_kernel(keep_ref, *refs, layout, mode, per_step, firsts):
    sources = refs[: len(layout)]
    w_hbm, side_ref = refs[len(layout) : len(layout) + 2]
    o_ref, col_ref, w_ref, w_sem = refs[-4:]
    step = pl.program_id(0)
    steps = pl.num_programs(0)
    columns, channels = sources[0].shape[-2:]
    frame_count = keep_ref.shape[0] // 3
    cells = col_ref.shape[0]
    band = cells // per_step
    height = band // columns
    taps = 9 * channels

    def weight_copy(j, b):
        return pltpu.make_async_copy(
            w_hbm.at[pl.ds((j * 3 + b) * channels, channels)],
            w_ref.at[b, pl.ds(j * channels, channels)],
            w_sem.at[b],
        )

    def weight_wait(b):
        pltpu.make_async_copy(w_hbm.at[pl.ds(0, taps)], w_ref.at[b], w_sem.at[b]).wait()

    @pl.when(step == 0)
    def _():
        for b in (1, 0, 2):
            for j in range(9):
                weight_copy(j, b).start()

    def row_of(ext_frame, ext_row):
        for name, (frame_lo, frame_hi, row_lo, row_hi) in layout.items():
            if frame_lo <= ext_frame < frame_hi and row_lo <= ext_row < row_hi:
                return sources[list(layout).index(name)][ext_frame - frame_lo, ext_row - row_lo]
        raise ValueError("no source")

    for index, first in enumerate(firsts):

        @pl.when(step == index)
        def _():
            for fl in range(per_step):
                f = first + fl
                for k in range(3):
                    kept = keep_ref[k * frame_count + f] != 0
                    for a in range(3):
                        j = k * 3 + a
                        for i in range(height):
                            piece = row_of(f + k, a + i)
                            col_ref[
                                pl.ds(fl * band + i * columns, columns), pl.ds(j * channels, channels)
                            ] = jnp.where(kept, piece, jnp.zeros_like(piece))

    outputs = w_ref.shape[-1]
    position = lax.broadcasted_iota(jnp.int32, (cells, outputs), 0) % columns
    running = None
    for b in (1, 0, 2):

        @pl.when(step == 0)
        def _():
            weight_wait(b)

        part = jnp.dot(col_ref[...], w_ref[b], preferred_element_type=jnp.float32)
        if b == 0:
            part = jnp.where(position == 0, 0.0, pltpu.roll(part, 1, 0))
        elif b == 2:
            part = jnp.where(position == columns - 1, 0.0, pltpu.roll(part, cells - 1, 0))
        running = part if running is None else running + part
    if mode == "act":
        values_f = running.astype(jnp.bfloat16).astype(jnp.float32)
        inverse = lax.rsqrt(jnp.mean(values_f * values_f, axis=-1, keepdims=True) + EPSILON)
        scaled = values_f * inverse * side_ref[...]
        o_ref[...] = (scaled / (1.0 + jnp.exp(-scaled))).astype(o_ref.dtype)
    else:
        residual = side_ref[pl.ds(2 + firsts[0] + step * per_step, per_step), 1 : 1 + height]
        o_ref[...] = (residual.reshape(cells, outputs).astype(jnp.float32) + running).astype(
            o_ref.dtype
        )


def whole(x):
    return pl.BlockSpec(x.shape, lambda step: (0,) * x.ndim)


def conv_call(layout, sources, weight, keep, side, mode, per_step=2, firsts=None, into=None):
    columns, channels = sources[0].shape[-2:]
    frame_count = keep.shape[0] // 3
    rows_in = max(hi for (_, _, _, hi) in layout.values())
    band = (rows_in - 2) * columns
    cells = frame_count * band
    outputs = weight.shape[-1]
    weight_rows = weight.reshape(27 * channels, outputs)
    if firsts is None:
        firsts = tuple(range(0, frame_count, per_step))
    block_at = firsts[0] // per_step
    operands = [keep, *sources, weight_rows, side]
    extra_specs, aliases = [], {}
    if into is not None:
        extra_specs = [pl.BlockSpec(memory_space=pl.ANY)]
        aliases = {len(operands): 0}
        operands.append(into.reshape(cells, outputs))
    out = pl.pallas_call(
        functools.partial(conv_kernel, layout=layout, mode=mode, per_step=per_step, firsts=firsts),
        out_shape=jax.ShapeDtypeStruct((cells, outputs), jnp.bfloat16),
        in_specs=[pl.BlockSpec(memory_space=pltpu.SMEM)]
        + [whole(x) for x in sources]
        + [pl.BlockSpec(memory_space=pl.ANY), whole(side)]
        + extra_specs,
        out_specs=pl.BlockSpec((per_step * band, outputs), lambda step: (step + block_at, 0)),
        grid=(len(firsts),),
        input_output_aliases=aliases,
        scratch_shapes=[
            pltpu.VMEM((per_step * band, 9 * channels), jnp.bfloat16),
            pltpu.VMEM((3, 9 * channels, outputs), jnp.bfloat16),
            pltpu.SemaphoreType.DMA((3,)),
        ],
        cost_estimate=pl.CostEstimate(
            flops=2 * len(firsts) * per_step * band * 27 * channels * outputs,
            transcendentals=len(firsts) * per_step * band * outputs,
            bytes_accessed=2 * (27 * channels * outputs + 3 * len(firsts) * per_step * band * outputs),
        ),
        compiler_params=pltpu.CompilerParams(vmem_limit_bytes=60 * 1024 * 1024),
    )(*operands)
    return out.reshape(frame_count, rows_in - 2, columns, outputs)


def on_device(
    generator_latent_rows,
    slot_group_row,
    frame_clip_number,
    input_convolution_weight,
    first_norm_gain,
    first_convolution_weight,
    second_norm_gain,
    second_convolution_weight,
):
    frame_count = F_DEV
    slots_here = generator_latent_rows.shape[1]
    packed_rows = generator_latent_rows.shape[2]
    parts_count = lax.axis_size("rows")
    rows_here = slots_here // frame_count
    height = rows_here * parts_count
    columns = packed_rows // LATENT_CHANNELS
    band_index = lax.axis_index("rows")
    frame_group_index = lax.axis_index("tm")

    ids = jnp.broadcast_to(
        slot_group_row.astype(jnp.bfloat16)[:, :, None], (1, slots_here, ID_LANES)
    )
    packed = jnp.concatenate([generator_latent_rows, ids], axis=-1)
    earlier = shifted(packed, "tm", 1)
    both = jnp.concatenate([earlier, packed], axis=0)
    parts_total = lax.axis_size("rows")
    pieces = [both]
    for by in range(1, parts_total):
        ring = [(i, (i + by) % parts_total) for i in range(parts_total)]
        pieces.append(lax.ppermute(both, "rows", ring))
    gathered = jnp.concatenate(pieces, axis=1)
    values = gathered[:, :, :packed_rows]
    slot_ids = gathered[:, :, packed_rows].astype(jnp.int32)

    window_rows = rows_here + 4
    frame_of = jnp.arange(frame_count, dtype=jnp.int32)[:, None]
    row_of = band_index * rows_here - 2 + jnp.arange(window_rows, dtype=jnp.int32)[None, :]
    wanted = (frame_of * height + row_of).reshape(-1)
    valid = jnp.broadcast_to((row_of >= 0) & (row_of < height), (frame_count, window_rows)).reshape(-1)
    selector = ((wanted[None, :, None] == slot_ids[:, None, :]) & valid[None, :, None]).astype(
        jnp.bfloat16
    )
    latent = jnp.einsum("qij,qjc->qic", selector, values, preferred_element_type=jnp.float32)
    latent = latent.astype(jnp.bfloat16).reshape(
        2 * frame_count, window_rows, columns, LATENT_CHANNELS
    )

    padded_clips = jnp.concatenate([jnp.full((4,), -1, jnp.int32), frame_clip_number])
    window = lax.dynamic_slice_in_dim(padded_clips, frame_group_index * frame_count, frame_count + 4)
    current_ext = window[2:]
    keep_ext = [window[k : k + frame_count + 2] == current_ext for k in range(3)]
    current = window[4:]
    keep_own = jnp.stack(
        [(window[k + 2 : k + 2 + frame_count] == current) for k in range(3)]
    ).astype(jnp.int32).reshape(-1)

    base_ext = local_conv(latent, input_convolution_weight, keep_ext).astype(jnp.bfloat16)
    first_act = norm_act(base_ext, first_norm_gain)
    ext_rows = band_index * rows_here - 1 + jnp.arange(rows_here + 2, dtype=jnp.int32)
    row_ok = (ext_rows >= 0) & (ext_rows < height)
    first_act = jnp.where(row_ok[None, :, None, None], first_act, jnp.zeros((), jnp.bfloat16))

    gain = second_norm_gain.reshape(1, -1)
    ext_frames, ext_rows_n = first_act.shape[:2]
    second_act = conv_call(
        {"x": (0, ext_frames, 0, ext_rows_n)},
        [first_act],
        first_convolution_weight,
        keep_own,
        gain,
        "act",
    )

    last = second_act[frame_count - 2 :]
    from_above = shifted(second_act[:, rows_here - 1 :], "rows", 1)
    from_below = shifted(second_act[:, :1], "rows", -1)
    prev_mid = shifted(last, "tm", 1)
    prev_above = diagonal(last[:, rows_here - 1 :], 1, 1)
    prev_below = diagonal(last[:, :1], 1, -1)
    layout = {
        "own": (2, 2 + frame_count, 1, 1 + rows_here),
        "above": (2, 2 + frame_count, 0, 1),
        "below": (2, 2 + frame_count, 1 + rows_here, 2 + rows_here),
        "mid": (0, 2, 1, 1 + rows_here),
        "corner_above": (0, 2, 0, 1),
        "corner_below": (0, 2, 1 + rows_here, 2 + rows_here),
    }
    late_layout = {name: layout[name] for name in ("own", "above", "below")}
    late_sources = [second_act, from_above, from_below]
    decoded = conv_call(
        late_layout, late_sources, second_convolution_weight, keep_own, base_ext, "res",
        firsts=(frame_count - 2,),
    )
    return conv_call(
        layout,
        [second_act, from_above, from_below, prev_mid, prev_above, prev_below],
        second_convolution_weight,
        keep_own,
        base_ext,
        "res",
        firsts=(0,),
        into=decoded,
    )


def solution(mesh):
    in_specs = (P("tm", "rows", None), P("tm", "rows"), P(), P(), P(), P(), P(), P())
    out_specs = P("tm", "rows", None, None)
    return jax.shard_map(
        on_device, mesh=mesh, in_specs=in_specs, out_specs=out_specs, check_vma=False
    )
```

```python
import functools

import jax
import jax.numpy as jnp
from jax import lax
from jax.experimental import pallas as pl
from jax.experimental.pallas import tpu as pltpu
from jax.sharding import PartitionSpec as P

LATENT_CHANNELS = 16
F_DEV = 4
ID_LANES = 128

EPSILON = 1e-06


def shifted(x, axis, by):
    devices = lax.axis_size(axis)
    pairs = [(i, i + by) for i in range(devices) if 0 <= i + by < devices]
    return lax.ppermute(x, axis, pairs)


def diagonal(x, by_tm, by_rows):
    groups, parts = lax.axis_size("tm"), lax.axis_size("rows")
    pairs = []
    for g in range(groups):
        for r in range(parts):
            dg, dr = g + by_tm, r + by_rows
            if 0 <= dg < groups and 0 <= dr < parts:
                pairs.append((g * parts + r, dg * parts + dr))
    return lax.ppermute(x, ("tm", "rows"), pairs)


def norm_act(field, gain_vec):
    values_f = field.astype(jnp.float32)
    inverse = lax.rsqrt(jnp.mean(values_f * values_f, axis=-1, keepdims=True) + EPSILON)
    return jax.nn.silu(values_f * inverse * gain_vec).astype(jnp.bfloat16)


def local_conv(extended, weight, keep_masks):
    frame_count = extended.shape[0] - 2
    height = extended.shape[1] - 2
    columns = extended.shape[2]
    channels = extended.shape[3]
    outputs = weight.shape[-1]
    padded = jnp.pad(extended, ((0, 0), (0, 0), (1, 1), (0, 0)))
    running = jnp.zeros((frame_count, height, columns, outputs), jnp.float32)
    for tap_time in range(3):
        pieces = []
        for tap_row in range(3):
            for tap_col in range(3):
                pieces.append(
                    padded[
                        tap_time : tap_time + frame_count,
                        tap_row : tap_row + height,
                        tap_col : tap_col + columns,
                    ]
                )
        stacked = jnp.concatenate(pieces, axis=-1).reshape(-1, 9 * channels)
        partial_value = jnp.dot(
            stacked,
            weight[tap_time].reshape(9 * channels, outputs),
            preferred_element_type=jnp.float32,
        )
        partial_value = partial_value.reshape(frame_count, height, columns, outputs)
        running = running + jnp.where(
            keep_masks[tap_time][:, None, None, None], partial_value, jnp.float32(0.0)
        )
    return running


def conv_kernel(keep_ref, *refs, layout, mode, per_step, firsts):
    sources = refs[: len(layout)]
    w_hbm, side_ref = refs[len(layout) : len(layout) + 2]
    o_ref, col_ref, w_ref, w_sem = refs[-4:]
    step = pl.program_id(0)
    steps = pl.num_programs(0)
    columns, channels = sources[0].shape[-2:]
    frame_count = keep_ref.shape[0] // 3
    cells = col_ref.shape[0]
    band = cells // per_step
    height = band // columns
    taps = 9 * channels

    def weight_copy(j, b):
        return pltpu.make_async_copy(
            w_hbm.at[pl.ds((j * 3 + b) * channels, channels)],
            w_ref.at[b, pl.ds(j * channels, channels)],
            w_sem.at[b],
        )

    def weight_wait(b):
        pltpu.make_async_copy(w_hbm.at[pl.ds(0, taps)], w_ref.at[b], w_sem.at[b]).wait()

    @pl.when(step == 0)
    def _():
        for b in (1, 0, 2):
            for j in range(9):
                weight_copy(j, b).start()

    def row_of(ext_frame, ext_row):
        for name, (frame_lo, frame_hi, row_lo, row_hi) in layout.items():
            if frame_lo <= ext_frame < frame_hi and row_lo <= ext_row < row_hi:
                return sources[list(layout).index(name)][ext_frame - frame_lo, ext_row - row_lo]
        raise ValueError("no source")

    for index, first in enumerate(firsts):

        @pl.when(step == index)
        def _():
            for fl in range(per_step):
                f = first + fl
                for k in range(3):
                    kept = keep_ref[k * frame_count + f] != 0
                    for a in range(3):
                        j = k * 3 + a
                        for i in range(height):
                            piece = row_of(f + k, a + i)
                            col_ref[
                                pl.ds(fl * band + i * columns, columns), pl.ds(j * channels, channels)
                            ] = jnp.where(kept, piece, jnp.zeros_like(piece))

    outputs = w_ref.shape[-1]
    position = lax.broadcasted_iota(jnp.int32, (cells, outputs), 0) % columns
    running = None
    for b in (1, 0, 2):

        @pl.when(step == 0)
        def _():
            weight_wait(b)

        part = jnp.dot(col_ref[...], w_ref[b], preferred_element_type=jnp.float32)
        if b == 0:
            part = jnp.where(position == 0, 0.0, pltpu.roll(part, 1, 0))
        elif b == 2:
            part = jnp.where(position == columns - 1, 0.0, pltpu.roll(part, cells - 1, 0))
        running = part if running is None else running + part
    if mode == "act":
        values_f = running.astype(jnp.bfloat16).astype(jnp.float32)
        inverse = lax.rsqrt(jnp.mean(values_f * values_f, axis=-1, keepdims=True) + EPSILON)
        scaled = values_f * inverse * side_ref[...]
        o_ref[...] = (scaled / (1.0 + jnp.exp(-scaled))).astype(o_ref.dtype)
    else:
        residual = side_ref[pl.ds(2 + firsts[0] + step * per_step, per_step), 1 : 1 + height]
        o_ref[...] = (residual.reshape(cells, outputs).astype(jnp.float32) + running).astype(
            o_ref.dtype
        )


def whole(x):
    return pl.BlockSpec(x.shape, lambda step: (0,) * x.ndim)


def conv_call(layout, sources, weight, keep, side, mode, per_step=2, firsts=None, into=None):
    columns, channels = sources[0].shape[-2:]
    frame_count = keep.shape[0] // 3
    rows_in = max(hi for (_, _, _, hi) in layout.values())
    band = (rows_in - 2) * columns
    cells = frame_count * band
    outputs = weight.shape[-1]
    weight_rows = weight.reshape(27 * channels, outputs)
    if firsts is None:
        firsts = tuple(range(0, frame_count, per_step))
    block_at = firsts[0] // per_step
    operands = [keep, *sources, weight_rows, side]
    extra_specs, aliases = [], {}
    if into is not None:
        extra_specs = [pl.BlockSpec(memory_space=pl.ANY)]
        aliases = {len(operands): 0}
        operands.append(into.reshape(cells, outputs))
    out = pl.pallas_call(
        functools.partial(conv_kernel, layout=layout, mode=mode, per_step=per_step, firsts=firsts),
        out_shape=jax.ShapeDtypeStruct((cells, outputs), jnp.bfloat16),
        in_specs=[pl.BlockSpec(memory_space=pltpu.SMEM)]
        + [whole(x) for x in sources]
        + [pl.BlockSpec(memory_space=pl.ANY), whole(side)]
        + extra_specs,
        out_specs=pl.BlockSpec((per_step * band, outputs), lambda step: (step + block_at, 0)),
        grid=(len(firsts),),
        input_output_aliases=aliases,
        scratch_shapes=[
            pltpu.VMEM((per_step * band, 9 * channels), jnp.bfloat16),
            pltpu.VMEM((3, 9 * channels, outputs), jnp.bfloat16),
            pltpu.SemaphoreType.DMA((3,)),
        ],
        cost_estimate=pl.CostEstimate(
            flops=2 * len(firsts) * per_step * band * 27 * channels * outputs,
            transcendentals=len(firsts) * per_step * band * outputs,
            bytes_accessed=2 * (27 * channels * outputs + 3 * len(firsts) * per_step * band * outputs),
        ),
        compiler_params=pltpu.CompilerParams(vmem_limit_bytes=60 * 1024 * 1024),
    )(*operands)
    return out.reshape(frame_count, rows_in - 2, columns, outputs)


def on_device(
    generator_latent_rows,
    slot_group_row,
    frame_clip_number,
    input_convolution_weight,
    first_norm_gain,
    first_convolution_weight,
    second_norm_gain,
    second_convolution_weight,
):
    frame_count = F_DEV
    slots_here = generator_latent_rows.shape[1]
    packed_rows = generator_latent_rows.shape[2]
    parts_count = lax.axis_size("rows")
    rows_here = slots_here // frame_count
    height = rows_here * parts_count
    columns = packed_rows // LATENT_CHANNELS
    band_index = lax.axis_index("rows")
    frame_group_index = lax.axis_index("tm")

    ids = jnp.broadcast_to(
        slot_group_row.astype(jnp.bfloat16)[:, :, None], (1, slots_here, ID_LANES)
    )
    packed = jnp.concatenate([generator_latent_rows, ids], axis=-1)
    earlier = shifted(packed, "tm", 1)
    both = jnp.concatenate([earlier, packed], axis=0)
    parts_total = lax.axis_size("rows")
    gathered = both
    span = 1
    while span < parts_total:
        swap = [(i, i ^ span) for i in range(parts_total)]
        gathered = jnp.concatenate([gathered, lax.ppermute(gathered, "rows", swap)], axis=1)
        span *= 2
    values = gathered[:, :, :packed_rows]
    slot_ids = gathered[:, :, packed_rows].astype(jnp.int32)

    window_rows = rows_here + 4
    frame_of = jnp.arange(frame_count, dtype=jnp.int32)[:, None]
    row_of = band_index * rows_here - 2 + jnp.arange(window_rows, dtype=jnp.int32)[None, :]
    wanted = (frame_of * height + row_of).reshape(-1)
    valid = jnp.broadcast_to((row_of >= 0) & (row_of < height), (frame_count, window_rows)).reshape(-1)
    selector = ((wanted[None, :, None] == slot_ids[:, None, :]) & valid[None, :, None]).astype(
        jnp.bfloat16
    )
    latent = jnp.einsum("qij,qjc->qic", selector, values, preferred_element_type=jnp.float32)
    latent = latent.astype(jnp.bfloat16).reshape(
        2 * frame_count, window_rows, columns, LATENT_CHANNELS
    )

    padded_clips = jnp.concatenate([jnp.full((4,), -1, jnp.int32), frame_clip_number])
    window = lax.dynamic_slice_in_dim(padded_clips, frame_group_index * frame_count, frame_count + 4)
    current_ext = window[2:]
    keep_ext = [window[k : k + frame_count + 2] == current_ext for k in range(3)]
    current = window[4:]
    keep_own = jnp.stack(
        [(window[k + 2 : k + 2 + frame_count] == current) for k in range(3)]
    ).astype(jnp.int32).reshape(-1)

    base_ext = local_conv(latent, input_convolution_weight, keep_ext).astype(jnp.bfloat16)
    first_act = norm_act(base_ext, first_norm_gain)
    ext_rows = band_index * rows_here - 1 + jnp.arange(rows_here + 2, dtype=jnp.int32)
    row_ok = (ext_rows >= 0) & (ext_rows < height)
    first_act = jnp.where(row_ok[None, :, None, None], first_act, jnp.zeros((), jnp.bfloat16))

    gain = second_norm_gain.reshape(1, -1)
    ext_frames, ext_rows_n = first_act.shape[:2]
    second_act = conv_call(
        {"x": (0, ext_frames, 0, ext_rows_n)},
        [first_act],
        first_convolution_weight,
        keep_own,
        gain,
        "act",
    )

    last = second_act[frame_count - 2 :]
    from_above = shifted(second_act[:, rows_here - 1 :], "rows", 1)
    from_below = shifted(second_act[:, :1], "rows", -1)
    prev_mid = shifted(last, "tm", 1)
    prev_above = diagonal(last[:, rows_here - 1 :], 1, 1)
    prev_below = diagonal(last[:, :1], 1, -1)
    layout = {
        "own": (2, 2 + frame_count, 1, 1 + rows_here),
        "above": (2, 2 + frame_count, 0, 1),
        "below": (2, 2 + frame_count, 1 + rows_here, 2 + rows_here),
        "mid": (0, 2, 1, 1 + rows_here),
        "corner_above": (0, 2, 0, 1),
        "corner_below": (0, 2, 1 + rows_here, 2 + rows_here),
    }
    late_layout = {name: layout[name] for name in ("own", "above", "below")}
    late_sources = [second_act, from_above, from_below]
    decoded = conv_call(
        late_layout, late_sources, second_convolution_weight, keep_own, base_ext, "res",
        firsts=(frame_count - 2,),
    )
    return conv_call(
        layout,
        [second_act, from_above, from_below, prev_mid, prev_above, prev_below],
        second_convolution_weight,
        keep_own,
        base_ext,
        "res",
        firsts=(0,),
        into=decoded,
    )


def solution(mesh):
    in_specs = (P("tm", "rows", None), P("tm", "rows"), P(), P(), P(), P(), P(), P())
    out_specs = P("tm", "rows", None, None)
    return jax.shard_map(
        on_device, mesh=mesh, in_specs=in_specs, out_specs=out_specs, check_vma=False
    )
```

```python
import functools

import jax
import jax.numpy as jnp
from jax import lax
from jax.experimental import pallas as pl
from jax.experimental.pallas import tpu as pltpu
from jax.sharding import PartitionSpec as P

LATENT_CHANNELS = 16
F_DEV = 4
ID_LANES = 128

EPSILON = 1e-06


def shifted(x, axis, by):
    devices = lax.axis_size(axis)
    pairs = [(i, i + by) for i in range(devices) if 0 <= i + by < devices]
    return lax.ppermute(x, axis, pairs)


def diagonal(x, by_tm, by_rows):
    groups, parts = lax.axis_size("tm"), lax.axis_size("rows")
    pairs = []
    for g in range(groups):
        for r in range(parts):
            dg, dr = g + by_tm, r + by_rows
            if 0 <= dg < groups and 0 <= dr < parts:
                pairs.append((g * parts + r, dg * parts + dr))
    return lax.ppermute(x, ("tm", "rows"), pairs)


def norm_act(field, gain_vec):
    values_f = field.astype(jnp.float32)
    inverse = lax.rsqrt(jnp.mean(values_f * values_f, axis=-1, keepdims=True) + EPSILON)
    return jax.nn.silu(values_f * inverse * gain_vec).astype(jnp.bfloat16)


def local_conv(extended, weight, keep_masks):
    frame_count = extended.shape[0] - 2
    height = extended.shape[1] - 2
    columns = extended.shape[2]
    channels = extended.shape[3]
    outputs = weight.shape[-1]
    padded = jnp.pad(extended, ((0, 0), (0, 0), (1, 1), (0, 0)))
    running = jnp.zeros((frame_count, height, columns, outputs), jnp.float32)
    for tap_time in range(3):
        pieces = []
        for tap_row in range(3):
            for tap_col in range(3):
                pieces.append(
                    padded[
                        tap_time : tap_time + frame_count,
                        tap_row : tap_row + height,
                        tap_col : tap_col + columns,
                    ]
                )
        stacked = jnp.concatenate(pieces, axis=-1).reshape(-1, 9 * channels)
        partial_value = jnp.dot(
            stacked,
            weight[tap_time].reshape(9 * channels, outputs),
            preferred_element_type=jnp.float32,
        )
        partial_value = partial_value.reshape(frame_count, height, columns, outputs)
        running = running + jnp.where(
            keep_masks[tap_time][:, None, None, None], partial_value, jnp.float32(0.0)
        )
    return running


def conv_kernel(keep_ref, *refs, layout, mode, per_step, firsts):
    sources = refs[: len(layout)]
    w_hbm, side_ref = refs[len(layout) : len(layout) + 2]
    o_ref, col_ref, w_ref, w_sem = refs[-4:]
    step = pl.program_id(0)
    steps = pl.num_programs(0)
    columns, channels = sources[0].shape[-2:]
    frame_count = keep_ref.shape[0] // 3
    cells = col_ref.shape[0]
    band = cells // per_step
    height = band // columns
    taps = 9 * channels

    def weight_copy(j, b):
        return pltpu.make_async_copy(
            w_hbm.at[pl.ds((j * 3 + b) * channels, channels)],
            w_ref.at[b, pl.ds(j * channels, channels)],
            w_sem.at[b],
        )

    def weight_wait(b):
        pltpu.make_async_copy(w_hbm.at[pl.ds(0, taps)], w_ref.at[b], w_sem.at[b]).wait()

    @pl.when(step == 0)
    def _():
        for b in (1, 0, 2):
            for j in range(9):
                weight_copy(j, b).start()

    def row_of(ext_frame, ext_row):
        for name, (frame_lo, frame_hi, row_lo, row_hi) in layout.items():
            if frame_lo <= ext_frame < frame_hi and row_lo <= ext_row < row_hi:
                return sources[list(layout).index(name)][ext_frame - frame_lo, ext_row - row_lo]
        raise ValueError("no source")

    for index, first in enumerate(firsts):

        @pl.when(step == index)
        def _():
            for fl in range(per_step):
                f = first + fl
                for k in range(3):
                    kept = keep_ref[k * frame_count + f] != 0
                    for a in range(3):
                        j = k * 3 + a
                        for i in range(height):
                            piece = row_of(f + k, a + i)
                            col_ref[
                                pl.ds(fl * band + i * columns, columns), pl.ds(j * channels, channels)
                            ] = jnp.where(kept, piece, jnp.zeros_like(piece))

    outputs = w_ref.shape[-1]
    position = lax.broadcasted_iota(jnp.int32, (cells, outputs), 0) % columns
    running = None
    for b in (1, 0, 2):

        @pl.when(step == 0)
        def _():
            weight_wait(b)

        part = jnp.dot(col_ref[...], w_ref[b], preferred_element_type=jnp.float32)
        if b == 0:
            part = jnp.where(position == 0, 0.0, pltpu.roll(part, 1, 0))
        elif b == 2:
            part = jnp.where(position == columns - 1, 0.0, pltpu.roll(part, cells - 1, 0))
        running = part if running is None else running + part
    if mode == "act":
        values_f = running.astype(jnp.bfloat16).astype(jnp.float32)
        inverse = lax.rsqrt(jnp.mean(values_f * values_f, axis=-1, keepdims=True) + EPSILON)
        scaled = values_f * inverse * side_ref[...]
        o_ref[...] = (scaled / (1.0 + jnp.exp(-scaled))).astype(o_ref.dtype)
    else:
        residual = side_ref[pl.ds(2 + firsts[0] + step * per_step, per_step), 1 : 1 + height]
        o_ref[...] = (residual.reshape(cells, outputs).astype(jnp.float32) + running).astype(
            o_ref.dtype
        )


def whole(x):
    return pl.BlockSpec(x.shape, lambda step: (0,) * x.ndim)


def conv_call(layout, sources, weight, keep, side, mode, per_step=2, firsts=None, into=None):
    columns, channels = sources[0].shape[-2:]
    frame_count = keep.shape[0] // 3
    rows_in = max(hi for (_, _, _, hi) in layout.values())
    band = (rows_in - 2) * columns
    cells = frame_count * band
    outputs = weight.shape[-1]
    weight_rows = weight.reshape(27 * channels, outputs)
    if firsts is None:
        firsts = tuple(range(0, frame_count, per_step))
    block_at = firsts[0] // per_step
    operands = [keep, *sources, weight_rows, side]
    extra_specs, aliases = [], {}
    if into is not None:
        extra_specs = [pl.BlockSpec(memory_space=pl.ANY)]
        aliases = {len(operands): 0}
        operands.append(into.reshape(cells, outputs))
    out = pl.pallas_call(
        functools.partial(conv_kernel, layout=layout, mode=mode, per_step=per_step, firsts=firsts),
        out_shape=jax.ShapeDtypeStruct((cells, outputs), jnp.bfloat16),
        in_specs=[pl.BlockSpec(memory_space=pltpu.SMEM)]
        + [whole(x) for x in sources]
        + [pl.BlockSpec(memory_space=pl.ANY), whole(side)]
        + extra_specs,
        out_specs=pl.BlockSpec((per_step * band, outputs), lambda step: (step + block_at, 0)),
        grid=(len(firsts),),
        input_output_aliases=aliases,
        scratch_shapes=[
            pltpu.VMEM((per_step * band, 9 * channels), jnp.bfloat16),
            pltpu.VMEM((3, 9 * channels, outputs), jnp.bfloat16),
            pltpu.SemaphoreType.DMA((3,)),
        ],
        cost_estimate=pl.CostEstimate(
            flops=2 * len(firsts) * per_step * band * 27 * channels * outputs,
            transcendentals=len(firsts) * per_step * band * outputs,
            bytes_accessed=2 * (27 * channels * outputs + 3 * len(firsts) * per_step * band * outputs),
        ),
        compiler_params=pltpu.CompilerParams(vmem_limit_bytes=60 * 1024 * 1024),
    )(*operands)
    return out.reshape(frame_count, rows_in - 2, columns, outputs)


def on_device(
    generator_latent_rows,
    slot_group_row,
    frame_clip_number,
    input_convolution_weight,
    first_norm_gain,
    first_convolution_weight,
    second_norm_gain,
    second_convolution_weight,
):
    frame_count = F_DEV
    slots_here = generator_latent_rows.shape[1]
    packed_rows = generator_latent_rows.shape[2]
    parts_count = lax.axis_size("rows")
    rows_here = slots_here // frame_count
    height = rows_here * parts_count
    columns = packed_rows // LATENT_CHANNELS
    band_index = lax.axis_index("rows")
    frame_group_index = lax.axis_index("tm")

    ids = jnp.broadcast_to(
        slot_group_row.astype(jnp.bfloat16)[:, :, None], (1, slots_here, ID_LANES)
    )
    packed = jnp.concatenate([generator_latent_rows, ids], axis=-1)
    parts_total = lax.axis_size("rows")
    pieces = [packed]
    for by in range(1, parts_total):
        ring = [(i, (i + by) % parts_total) for i in range(parts_total)]
        pieces.append(lax.ppermute(packed, "rows", ring))
    gathered = jnp.concatenate(pieces, axis=1)[0]
    values = gathered[:, :packed_rows]
    slot_ids = gathered[:, packed_rows].astype(jnp.int32)

    window_rows = rows_here + 4
    frame_of = jnp.arange(frame_count, dtype=jnp.int32)[:, None]
    row_of = band_index * rows_here - 2 + jnp.arange(window_rows, dtype=jnp.int32)[None, :]
    wanted = (frame_of * height + row_of).reshape(-1)
    valid = jnp.broadcast_to((row_of >= 0) & (row_of < height), (frame_count, window_rows)).reshape(-1)
    selector = ((wanted[:, None] == slot_ids[None, :]) & valid[:, None]).astype(jnp.bfloat16)
    own_window = jnp.dot(selector, values, preferred_element_type=jnp.float32).astype(jnp.bfloat16)
    prev_window = shifted(own_window, "tm", 1)
    latent = jnp.concatenate([prev_window, own_window], axis=0).reshape(
        2 * frame_count, window_rows, columns, LATENT_CHANNELS
    )

    padded_clips = jnp.concatenate([jnp.full((4,), -1, jnp.int32), frame_clip_number])
    window = lax.dynamic_slice_in_dim(padded_clips, frame_group_index * frame_count, frame_count + 4)
    current_ext = window[2:]
    keep_ext = [window[k : k + frame_count + 2] == current_ext for k in range(3)]
    current = window[4:]
    keep_own = jnp.stack(
        [(window[k + 2 : k + 2 + frame_count] == current) for k in range(3)]
    ).astype(jnp.int32).reshape(-1)

    base_ext = local_conv(latent, input_convolution_weight, keep_ext).astype(jnp.bfloat16)
    first_act = norm_act(base_ext, first_norm_gain)
    ext_rows = band_index * rows_here - 1 + jnp.arange(rows_here + 2, dtype=jnp.int32)
    row_ok = (ext_rows >= 0) & (ext_rows < height)
    first_act = jnp.where(row_ok[None, :, None, None], first_act, jnp.zeros((), jnp.bfloat16))

    gain = second_norm_gain.reshape(1, -1)
    ext_frames, ext_rows_n = first_act.shape[:2]
    second_act = conv_call(
        {"x": (0, ext_frames, 0, ext_rows_n)},
        [first_act],
        first_convolution_weight,
        keep_own,
        gain,
        "act",
    )

    last = second_act[frame_count - 2 :]
    from_above = shifted(second_act[:, rows_here - 1 :], "rows", 1)
    from_below = shifted(second_act[:, :1], "rows", -1)
    prev_mid = shifted(last, "tm", 1)
    prev_above = diagonal(last[:, rows_here - 1 :], 1, 1)
    prev_below = diagonal(last[:, :1], 1, -1)
    layout = {
        "own": (2, 2 + frame_count, 1, 1 + rows_here),
        "above": (2, 2 + frame_count, 0, 1),
        "below": (2, 2 + frame_count, 1 + rows_here, 2 + rows_here),
        "mid": (0, 2, 1, 1 + rows_here),
        "corner_above": (0, 2, 0, 1),
        "corner_below": (0, 2, 1 + rows_here, 2 + rows_here),
    }
    late_layout = {name: layout[name] for name in ("own", "above", "below")}
    late_sources = [second_act, from_above, from_below]
    decoded = conv_call(
        late_layout, late_sources, second_convolution_weight, keep_own, base_ext, "res",
        firsts=(frame_count - 2,),
    )
    return conv_call(
        layout,
        [second_act, from_above, from_below, prev_mid, prev_above, prev_below],
        second_convolution_weight,
        keep_own,
        base_ext,
        "res",
        firsts=(0,),
        into=decoded,
    )


def solution(mesh):
    in_specs = (P("tm", "rows", None), P("tm", "rows"), P(), P(), P(), P(), P(), P())
    out_specs = P("tm", "rows", None, None)
    return jax.shard_map(
        on_device, mesh=mesh, in_specs=in_specs, out_specs=out_specs, check_vma=False
    )
```

```python
import functools

import jax
import jax.numpy as jnp
from jax import lax
from jax.experimental import pallas as pl
from jax.experimental.pallas import tpu as pltpu
from jax.sharding import PartitionSpec as P

LATENT_CHANNELS = 16
F_DEV = 4
ID_LANES = 128

EPSILON = 1e-06


def shifted(x, axis, by):
    devices = lax.axis_size(axis)
    pairs = [(i, i + by) for i in range(devices) if 0 <= i + by < devices]
    return lax.ppermute(x, axis, pairs)


def diagonal(x, by_tm, by_rows):
    groups, parts = lax.axis_size("tm"), lax.axis_size("rows")
    pairs = []
    for g in range(groups):
        for r in range(parts):
            dg, dr = g + by_tm, r + by_rows
            if 0 <= dg < groups and 0 <= dr < parts:
                pairs.append((g * parts + r, dg * parts + dr))
    return lax.ppermute(x, ("tm", "rows"), pairs)


def norm_act(field, gain_vec):
    values_f = field.astype(jnp.float32)
    inverse = lax.rsqrt(jnp.mean(values_f * values_f, axis=-1, keepdims=True) + EPSILON)
    return jax.nn.silu(values_f * inverse * gain_vec).astype(jnp.bfloat16)


def local_conv(extended, weight, keep_masks):
    frame_count = extended.shape[0] - 2
    height = extended.shape[1] - 2
    columns = extended.shape[2]
    channels = extended.shape[3]
    outputs = weight.shape[-1]
    padded = jnp.pad(extended, ((0, 0), (0, 0), (1, 1), (0, 0)))
    running = jnp.zeros((frame_count, height, columns, outputs), jnp.float32)
    for tap_time in range(3):
        pieces = []
        for tap_row in range(3):
            for tap_col in range(3):
                pieces.append(
                    padded[
                        tap_time : tap_time + frame_count,
                        tap_row : tap_row + height,
                        tap_col : tap_col + columns,
                    ]
                )
        stacked = jnp.concatenate(pieces, axis=-1).reshape(-1, 9 * channels)
        partial_value = jnp.dot(
            stacked,
            weight[tap_time].reshape(9 * channels, outputs),
            preferred_element_type=jnp.float32,
        )
        partial_value = partial_value.reshape(frame_count, height, columns, outputs)
        running = running + jnp.where(
            keep_masks[tap_time][:, None, None, None], partial_value, jnp.float32(0.0)
        )
    return running


def input_conv(extended, weight, keep_masks):
    frame_count = extended.shape[0] - 2
    height = extended.shape[1] - 2
    columns = extended.shape[2]
    channels = extended.shape[3]
    outputs = weight.shape[-1]
    padded = jnp.pad(extended, ((0, 0), (0, 0), (1, 1), (0, 0)))
    pieces = []
    for tap_time in range(3):
        kept = keep_masks[tap_time][:, None, None, None]
        for tap_row in range(3):
            for tap_col in range(3):
                window = padded[
                    tap_time : tap_time + frame_count,
                    tap_row : tap_row + height,
                    tap_col : tap_col + columns,
                ]
                pieces.append(jnp.where(kept, window, jnp.zeros((), window.dtype)))
    stacked = jnp.concatenate(pieces, axis=-1).reshape(-1, 27 * channels)
    total = jnp.dot(
        stacked, weight.reshape(27 * channels, outputs), preferred_element_type=jnp.float32
    )
    return total.astype(jnp.bfloat16).reshape(frame_count, height, columns, outputs)


def conv_kernel(keep_ref, *refs, layout, mode, per_step, firsts):
    sources = refs[: len(layout)]
    w_hbm, side_ref = refs[len(layout) : len(layout) + 2]
    o_ref, col_ref, w_ref, w_sem = refs[-4:]
    step = pl.program_id(0)
    steps = pl.num_programs(0)
    columns, channels = sources[0].shape[-2:]
    frame_count = keep_ref.shape[0] // 3
    cells = col_ref.shape[0]
    band = cells // per_step
    height = band // columns
    taps = 9 * channels

    def weight_copy(j, b):
        return pltpu.make_async_copy(
            w_hbm.at[pl.ds((j * 3 + b) * channels, channels)],
            w_ref.at[b, pl.ds(j * channels, channels)],
            w_sem.at[b],
        )

    def weight_wait(b):
        pltpu.make_async_copy(w_hbm.at[pl.ds(0, taps)], w_ref.at[b], w_sem.at[b]).wait()

    @pl.when(step == 0)
    def _():
        for b in (1, 0, 2):
            for j in range(9):
                weight_copy(j, b).start()

    def row_of(ext_frame, ext_row):
        for name, (frame_lo, frame_hi, row_lo, row_hi) in layout.items():
            if frame_lo <= ext_frame < frame_hi and row_lo <= ext_row < row_hi:
                return sources[list(layout).index(name)][ext_frame - frame_lo, ext_row - row_lo]
        raise ValueError("no source")

    for index, first in enumerate(firsts):

        @pl.when(step == index)
        def _():
            for fl in range(per_step):
                f = first + fl
                for k in range(3):
                    kept = keep_ref[k * frame_count + f] != 0
                    for a in range(3):
                        j = k * 3 + a
                        for i in range(height):
                            piece = row_of(f + k, a + i)
                            col_ref[
                                pl.ds(fl * band + i * columns, columns), pl.ds(j * channels, channels)
                            ] = jnp.where(kept, piece, jnp.zeros_like(piece))

    outputs = w_ref.shape[-1]
    position = lax.broadcasted_iota(jnp.int32, (cells, outputs), 0) % columns
    running = None
    for b in (1, 0, 2):

        @pl.when(step == 0)
        def _():
            weight_wait(b)

        part = jnp.dot(col_ref[...], w_ref[b], preferred_element_type=jnp.float32)
        if b == 0:
            part = jnp.where(position == 0, 0.0, pltpu.roll(part, 1, 0))
        elif b == 2:
            part = jnp.where(position == columns - 1, 0.0, pltpu.roll(part, cells - 1, 0))
        running = part if running is None else running + part
    if mode == "act":
        values_f = running.astype(jnp.bfloat16).astype(jnp.float32)
        inverse = lax.rsqrt(jnp.mean(values_f * values_f, axis=-1, keepdims=True) + EPSILON)
        scaled = values_f * inverse * side_ref[...]
        o_ref[...] = (scaled / (1.0 + jnp.exp(-scaled))).astype(o_ref.dtype)
    else:
        residual = side_ref[pl.ds(2 + firsts[0] + step * per_step, per_step), 1 : 1 + height]
        o_ref[...] = (residual.reshape(cells, outputs).astype(jnp.float32) + running).astype(
            o_ref.dtype
        )


def whole(x):
    return pl.BlockSpec(x.shape, lambda step: (0,) * x.ndim)


def conv_call(layout, sources, weight, keep, side, mode, per_step=2, firsts=None, into=None):
    columns, channels = sources[0].shape[-2:]
    frame_count = keep.shape[0] // 3
    rows_in = max(hi for (_, _, _, hi) in layout.values())
    band = (rows_in - 2) * columns
    cells = frame_count * band
    outputs = weight.shape[-1]
    weight_rows = weight.reshape(27 * channels, outputs)
    if firsts is None:
        firsts = tuple(range(0, frame_count, per_step))
    block_at = firsts[0] // per_step
    operands = [keep, *sources, weight_rows, side]
    extra_specs, aliases = [], {}
    if into is not None:
        extra_specs = [pl.BlockSpec(memory_space=pl.ANY)]
        aliases = {len(operands): 0}
        operands.append(into.reshape(cells, outputs))
    out = pl.pallas_call(
        functools.partial(conv_kernel, layout=layout, mode=mode, per_step=per_step, firsts=firsts),
        out_shape=jax.ShapeDtypeStruct((cells, outputs), jnp.bfloat16),
        in_specs=[pl.BlockSpec(memory_space=pltpu.SMEM)]
        + [whole(x) for x in sources]
        + [pl.BlockSpec(memory_space=pl.ANY), whole(side)]
        + extra_specs,
        out_specs=pl.BlockSpec((per_step * band, outputs), lambda step: (step + block_at, 0)),
        grid=(len(firsts),),
        input_output_aliases=aliases,
        scratch_shapes=[
            pltpu.VMEM((per_step * band, 9 * channels), jnp.bfloat16),
            pltpu.VMEM((3, 9 * channels, outputs), jnp.bfloat16),
            pltpu.SemaphoreType.DMA((3,)),
        ],
        cost_estimate=pl.CostEstimate(
            flops=2 * len(firsts) * per_step * band * 27 * channels * outputs,
            transcendentals=len(firsts) * per_step * band * outputs,
            bytes_accessed=2 * (27 * channels * outputs + 3 * len(firsts) * per_step * band * outputs),
        ),
        compiler_params=pltpu.CompilerParams(vmem_limit_bytes=60 * 1024 * 1024),
    )(*operands)
    return out.reshape(frame_count, rows_in - 2, columns, outputs)


def on_device(
    generator_latent_rows,
    slot_group_row,
    frame_clip_number,
    input_convolution_weight,
    first_norm_gain,
    first_convolution_weight,
    second_norm_gain,
    second_convolution_weight,
):
    frame_count = F_DEV
    slots_here = generator_latent_rows.shape[1]
    packed_rows = generator_latent_rows.shape[2]
    parts_count = lax.axis_size("rows")
    rows_here = slots_here // frame_count
    height = rows_here * parts_count
    columns = packed_rows // LATENT_CHANNELS
    band_index = lax.axis_index("rows")
    frame_group_index = lax.axis_index("tm")

    ids = jnp.broadcast_to(
        slot_group_row.astype(jnp.bfloat16)[:, :, None], (1, slots_here, ID_LANES)
    )
    packed = jnp.concatenate([generator_latent_rows, ids], axis=-1)
    parts_total = lax.axis_size("rows")
    pieces = [packed]
    for by in range(1, parts_total):
        ring = [(i, (i + by) % parts_total) for i in range(parts_total)]
        pieces.append(lax.ppermute(packed, "rows", ring))
    gathered = jnp.concatenate(pieces, axis=1)[0]
    values = gathered[:, :packed_rows]
    slot_ids = gathered[:, packed_rows].astype(jnp.int32)

    window_rows = rows_here + 4
    frame_of = jnp.arange(frame_count, dtype=jnp.int32)[:, None]
    row_of = band_index * rows_here - 2 + jnp.arange(window_rows, dtype=jnp.int32)[None, :]
    wanted = (frame_of * height + row_of).reshape(-1)
    valid = jnp.broadcast_to((row_of >= 0) & (row_of < height), (frame_count, window_rows)).reshape(-1)
    selector = ((wanted[:, None] == slot_ids[None, :]) & valid[:, None]).astype(jnp.bfloat16)
    own_window = jnp.dot(selector, values, preferred_element_type=jnp.float32).astype(jnp.bfloat16)
    prev_window = shifted(own_window, "tm", 1)
    latent = jnp.concatenate([prev_window, own_window], axis=0).reshape(
        2 * frame_count, window_rows, columns, LATENT_CHANNELS
    )

    padded_clips = jnp.concatenate([jnp.full((4,), -1, jnp.int32), frame_clip_number])
    window = lax.dynamic_slice_in_dim(padded_clips, frame_group_index * frame_count, frame_count + 4)
    current_ext = window[2:]
    keep_ext = [window[k : k + frame_count + 2] == current_ext for k in range(3)]
    current = window[4:]
    keep_own = jnp.stack(
        [(window[k + 2 : k + 2 + frame_count] == current) for k in range(3)]
    ).astype(jnp.int32).reshape(-1)

    base_ext = input_conv(latent, input_convolution_weight, keep_ext)
    first_act = norm_act(base_ext, first_norm_gain)
    ext_rows = band_index * rows_here - 1 + jnp.arange(rows_here + 2, dtype=jnp.int32)
    row_ok = (ext_rows >= 0) & (ext_rows < height)
    first_act = jnp.where(row_ok[None, :, None, None], first_act, jnp.zeros((), jnp.bfloat16))

    gain = second_norm_gain.reshape(1, -1)
    ext_frames, ext_rows_n = first_act.shape[:2]
    second_act = conv_call(
        {"x": (0, ext_frames, 0, ext_rows_n)},
        [first_act],
        first_convolution_weight,
        keep_own,
        gain,
        "act",
    )

    last = second_act[frame_count - 2 :]
    from_above = shifted(second_act[:, rows_here - 1 :], "rows", 1)
    from_below = shifted(second_act[:, :1], "rows", -1)
    prev_mid = shifted(last, "tm", 1)
    prev_above = diagonal(last[:, rows_here - 1 :], 1, 1)
    prev_below = diagonal(last[:, :1], 1, -1)
    layout = {
        "own": (2, 2 + frame_count, 1, 1 + rows_here),
        "above": (2, 2 + frame_count, 0, 1),
        "below": (2, 2 + frame_count, 1 + rows_here, 2 + rows_here),
        "mid": (0, 2, 1, 1 + rows_here),
        "corner_above": (0, 2, 0, 1),
        "corner_below": (0, 2, 1 + rows_here, 2 + rows_here),
    }
    late_layout = {name: layout[name] for name in ("own", "above", "below")}
    late_sources = [second_act, from_above, from_below]
    decoded = conv_call(
        late_layout, late_sources, second_convolution_weight, keep_own, base_ext, "res",
        firsts=(frame_count - 2,),
    )
    return conv_call(
        layout,
        [second_act, from_above, from_below, prev_mid, prev_above, prev_below],
        second_convolution_weight,
        keep_own,
        base_ext,
        "res",
        firsts=(0,),
        into=decoded,
    )


def solution(mesh):
    in_specs = (P("tm", "rows", None), P("tm", "rows"), P(), P(), P(), P(), P(), P())
    out_specs = P("tm", "rows", None, None)
    return jax.shard_map(
        on_device, mesh=mesh, in_specs=in_specs, out_specs=out_specs, check_vma=False
    )
```

```python
import functools

import jax
import jax.numpy as jnp
from jax import lax
from jax.experimental import pallas as pl
from jax.experimental.pallas import tpu as pltpu
from jax.sharding import PartitionSpec as P

LATENT_CHANNELS = 16
F_DEV = 4
ID_LANES = 128

EPSILON = 1e-06


def shifted(x, axis, by):
    devices = lax.axis_size(axis)
    pairs = [(i, i + by) for i in range(devices) if 0 <= i + by < devices]
    return lax.ppermute(x, axis, pairs)


def diagonal(x, by_tm, by_rows):
    groups, parts = lax.axis_size("tm"), lax.axis_size("rows")
    pairs = []
    for g in range(groups):
        for r in range(parts):
            dg, dr = g + by_tm, r + by_rows
            if 0 <= dg < groups and 0 <= dr < parts:
                pairs.append((g * parts + r, dg * parts + dr))
    return lax.ppermute(x, ("tm", "rows"), pairs)


def norm_act(field, gain_vec):
    values_f = field.astype(jnp.float32)
    inverse = lax.rsqrt(jnp.mean(values_f * values_f, axis=-1, keepdims=True) + EPSILON)
    return jax.nn.silu(values_f * inverse * gain_vec).astype(jnp.bfloat16)


def local_conv(extended, weight, keep_masks):
    frame_count = extended.shape[0] - 2
    height = extended.shape[1] - 2
    columns = extended.shape[2]
    channels = extended.shape[3]
    outputs = weight.shape[-1]
    padded = jnp.pad(extended, ((0, 0), (0, 0), (1, 1), (0, 0)))
    running = jnp.zeros((frame_count, height, columns, outputs), jnp.float32)
    for tap_time in range(3):
        pieces = []
        for tap_row in range(3):
            for tap_col in range(3):
                pieces.append(
                    padded[
                        tap_time : tap_time + frame_count,
                        tap_row : tap_row + height,
                        tap_col : tap_col + columns,
                    ]
                )
        stacked = jnp.concatenate(pieces, axis=-1).reshape(-1, 9 * channels)
        partial_value = jnp.dot(
            stacked,
            weight[tap_time].reshape(9 * channels, outputs),
            preferred_element_type=jnp.float32,
        )
        partial_value = partial_value.reshape(frame_count, height, columns, outputs)
        running = running + jnp.where(
            keep_masks[tap_time][:, None, None, None], partial_value, jnp.float32(0.0)
        )
    return running


def conv_kernel(keep_ref, *refs, layout, mode, per_step, firsts):
    sources = refs[: len(layout)]
    w_hbm, side_ref = refs[len(layout) : len(layout) + 2]
    o_ref, col_ref, w_ref, w_sem = refs[-4:]
    step = pl.program_id(0)
    steps = pl.num_programs(0)
    columns, channels = sources[0].shape[-2:]
    frame_count = keep_ref.shape[0] // 3
    cells = col_ref.shape[0]
    band = cells // per_step
    height = band // columns
    taps = 9 * channels

    def weight_copy(j, b):
        return pltpu.make_async_copy(
            w_hbm.at[pl.ds((j * 3 + b) * channels, channels)],
            w_ref.at[b, pl.ds(j * channels, channels)],
            w_sem.at[b],
        )

    def weight_wait(b):
        pltpu.make_async_copy(w_hbm.at[pl.ds(0, taps)], w_ref.at[b], w_sem.at[b]).wait()

    @pl.when(step == 0)
    def _():
        for b in (1, 0, 2):
            for j in range(9):
                weight_copy(j, b).start()

    def row_of(ext_frame, ext_row):
        for name, (frame_lo, frame_hi, row_lo, row_hi) in layout.items():
            if frame_lo <= ext_frame < frame_hi and row_lo <= ext_row < row_hi:
                return sources[list(layout).index(name)][ext_frame - frame_lo, ext_row - row_lo]
        raise ValueError("no source")

    for index, first in enumerate(firsts):

        @pl.when(step == index)
        def _():
            for fl in range(per_step):
                f = first + fl
                for k in range(3):
                    kept = keep_ref[k * frame_count + f] != 0
                    for a in range(3):
                        j = k * 3 + a
                        for i in range(height):
                            piece = row_of(f + k, a + i)
                            col_ref[
                                pl.ds(fl * band + i * columns, columns), pl.ds(j * channels, channels)
                            ] = jnp.where(kept, piece, jnp.zeros_like(piece))

    outputs = w_ref.shape[-1]
    position = lax.broadcasted_iota(jnp.int32, (cells, outputs), 0) % columns
    running = None
    for b in (1, 0, 2):

        @pl.when(step == 0)
        def _():
            weight_wait(b)

        part = jnp.dot(col_ref[...], w_ref[b], preferred_element_type=jnp.float32)
        if b == 0:
            part = jnp.where(position == 0, 0.0, pltpu.roll(part, 1, 0))
        elif b == 2:
            part = jnp.where(position == columns - 1, 0.0, pltpu.roll(part, cells - 1, 0))
        running = part if running is None else running + part
    if mode == "act":
        values_f = running.astype(jnp.bfloat16).astype(jnp.float32)
        inverse = lax.rsqrt(jnp.mean(values_f * values_f, axis=-1, keepdims=True) + EPSILON)
        scaled = values_f * inverse * side_ref[...]
        o_ref[...] = (scaled / (1.0 + jnp.exp(-scaled))).astype(o_ref.dtype)
    else:
        residual = side_ref[pl.ds(2 + firsts[0] + step * per_step, per_step), 1 : 1 + height]
        o_ref[...] = (residual.reshape(cells, outputs).astype(jnp.float32) + running).astype(
            o_ref.dtype
        )


def whole(x):
    return pl.BlockSpec(x.shape, lambda step: (0,) * x.ndim)


def conv_call(layout, sources, weight, keep, side, mode, per_step=2, firsts=None, into=None):
    columns, channels = sources[0].shape[-2:]
    frame_count = keep.shape[0] // 3
    rows_in = max(hi for (_, _, _, hi) in layout.values())
    band = (rows_in - 2) * columns
    cells = frame_count * band
    outputs = weight.shape[-1]
    weight_rows = weight.reshape(27 * channels, outputs)
    if firsts is None:
        firsts = tuple(range(0, frame_count, per_step))
    block_at = firsts[0] // per_step
    operands = [keep, *sources, weight_rows, side]
    extra_specs, aliases = [], {}
    if into is not None:
        extra_specs = [pl.BlockSpec(memory_space=pl.ANY)]
        aliases = {len(operands): 0}
        operands.append(into.reshape(cells, outputs))
    out = pl.pallas_call(
        functools.partial(conv_kernel, layout=layout, mode=mode, per_step=per_step, firsts=firsts),
        out_shape=jax.ShapeDtypeStruct((cells, outputs), jnp.bfloat16),
        in_specs=[pl.BlockSpec(memory_space=pltpu.SMEM)]
        + [whole(x) for x in sources]
        + [pl.BlockSpec(memory_space=pl.ANY), whole(side)]
        + extra_specs,
        out_specs=pl.BlockSpec((per_step * band, outputs), lambda step: (step + block_at, 0)),
        grid=(len(firsts),),
        input_output_aliases=aliases,
        scratch_shapes=[
            pltpu.VMEM((per_step * band, 9 * channels), jnp.bfloat16),
            pltpu.VMEM((3, 9 * channels, outputs), jnp.bfloat16),
            pltpu.SemaphoreType.DMA((3,)),
        ],
        cost_estimate=pl.CostEstimate(
            flops=2 * len(firsts) * per_step * band * 27 * channels * outputs,
            transcendentals=len(firsts) * per_step * band * outputs,
            bytes_accessed=2 * (27 * channels * outputs + 3 * len(firsts) * per_step * band * outputs),
        ),
        compiler_params=pltpu.CompilerParams(vmem_limit_bytes=60 * 1024 * 1024),
    )(*operands)
    return out.reshape(frame_count, rows_in - 2, columns, outputs)


def on_device(
    generator_latent_rows,
    slot_group_row,
    frame_clip_number,
    input_convolution_weight,
    first_norm_gain,
    first_convolution_weight,
    second_norm_gain,
    second_convolution_weight,
):
    frame_count = F_DEV
    slots_here = generator_latent_rows.shape[1]
    packed_rows = generator_latent_rows.shape[2]
    parts_count = lax.axis_size("rows")
    rows_here = slots_here // frame_count
    height = rows_here * parts_count
    columns = packed_rows // LATENT_CHANNELS
    band_index = lax.axis_index("rows")
    frame_group_index = lax.axis_index("tm")

    ids = jnp.broadcast_to(
        slot_group_row.astype(jnp.bfloat16)[:, :, None], (1, slots_here, ID_LANES)
    )
    packed = jnp.concatenate([generator_latent_rows, ids], axis=-1)
    parts_total = lax.axis_size("rows")
    pieces = [packed]
    for by in range(1, parts_total):
        ring = [(i, (i + by) % parts_total) for i in range(parts_total)]
        pieces.append(lax.ppermute(packed, "rows", ring))
    gathered = jnp.concatenate(pieces, axis=1)[0]
    values = gathered[:, :packed_rows]
    slot_ids = gathered[:, packed_rows].astype(jnp.int32)

    window_rows = rows_here + 4
    frame_of = jnp.arange(frame_count, dtype=jnp.int32)[:, None]
    row_of = band_index * rows_here - 2 + jnp.arange(window_rows, dtype=jnp.int32)[None, :]
    wanted = (frame_of * height + row_of).reshape(-1)
    valid = jnp.broadcast_to((row_of >= 0) & (row_of < height), (frame_count, window_rows)).reshape(-1)
    selector = ((wanted[:, None] == slot_ids[None, :]) & valid[:, None]).astype(jnp.bfloat16)
    own_window = jnp.dot(selector, values, preferred_element_type=jnp.float32).astype(jnp.bfloat16)
    prev_window = shifted(own_window, "tm", 1)
    latent = jnp.concatenate([prev_window, own_window], axis=0).reshape(
        2 * frame_count, window_rows, columns, LATENT_CHANNELS
    )

    padded_clips = jnp.concatenate([jnp.full((4,), -1, jnp.int32), frame_clip_number])
    window = lax.dynamic_slice_in_dim(padded_clips, frame_group_index * frame_count, frame_count + 4)
    current_ext = window[2:]
    keep_ext = [window[k : k + frame_count + 2] == current_ext for k in range(3)]
    current = window[4:]
    keep_own = jnp.stack(
        [(window[k + 2 : k + 2 + frame_count] == current) for k in range(3)]
    ).astype(jnp.int32).reshape(-1)

    base_ext = local_conv(latent, input_convolution_weight, keep_ext).astype(jnp.bfloat16)
    first_act = norm_act(base_ext, first_norm_gain)
    ext_rows = band_index * rows_here - 1 + jnp.arange(rows_here + 2, dtype=jnp.int32)
    row_ok = (ext_rows >= 0) & (ext_rows < height)
    first_act = jnp.where(row_ok[None, :, None, None], first_act, jnp.zeros((), jnp.bfloat16))

    gain = second_norm_gain.reshape(1, -1)
    ext_frames, ext_rows_n = first_act.shape[:2]
    second_act = conv_call(
        {"x": (0, ext_frames, 0, ext_rows_n)},
        [first_act],
        first_convolution_weight,
        keep_own,
        gain,
        "act",
    )

    last = second_act[frame_count - 2 :]
    from_above = shifted(second_act[:, rows_here - 1 :], "rows", 1)
    from_below = shifted(second_act[:, :1], "rows", -1)
    prev_mid = shifted(last, "tm", 1)
    layout = {
        "own": (2, 2 + frame_count, 1, 1 + rows_here),
        "above": (2, 2 + frame_count, 0, 1),
        "below": (2, 2 + frame_count, 1 + rows_here, 2 + rows_here),
        "mid": (0, 2, 1, 1 + rows_here),
        "corner_above": (0, 2, 0, 1),
        "corner_below": (0, 2, 1 + rows_here, 2 + rows_here),
    }
    late_layout = {name: layout[name] for name in ("own", "above", "below")}
    late_sources = [second_act, from_above, from_below]
    decoded = conv_call(
        late_layout, late_sources, second_convolution_weight, keep_own, base_ext, "res",
        firsts=(frame_count - 2,),
    )
    decoded, prev_mid = lax.optimization_barrier((decoded, prev_mid))
    prev_above = shifted(prev_mid[:, rows_here - 1 :], "rows", 1)
    prev_below = shifted(prev_mid[:, :1], "rows", -1)
    return conv_call(
        layout,
        [second_act, from_above, from_below, prev_mid, prev_above, prev_below],
        second_convolution_weight,
        keep_own,
        base_ext,
        "res",
        firsts=(0,),
        into=decoded,
    )


def solution(mesh):
    in_specs = (P("tm", "rows", None), P("tm", "rows"), P(), P(), P(), P(), P(), P())
    out_specs = P("tm", "rows", None, None)
    return jax.shard_map(
        on_device, mesh=mesh, in_specs=in_specs, out_specs=out_specs, check_vma=False
    )
```

```python
import functools

import jax
import jax.numpy as jnp
from jax import lax
from jax.experimental import pallas as pl
from jax.experimental.pallas import tpu as pltpu
from jax.sharding import PartitionSpec as P

LATENT_CHANNELS = 16
F_DEV = 4
ID_LANES = 128

EPSILON = 1e-06


def shifted(x, axis, by):
    devices = lax.axis_size(axis)
    pairs = [(i, i + by) for i in range(devices) if 0 <= i + by < devices]
    return lax.ppermute(x, axis, pairs)


def diagonal(x, by_tm, by_rows):
    groups, parts = lax.axis_size("tm"), lax.axis_size("rows")
    pairs = []
    for g in range(groups):
        for r in range(parts):
            dg, dr = g + by_tm, r + by_rows
            if 0 <= dg < groups and 0 <= dr < parts:
                pairs.append((g * parts + r, dg * parts + dr))
    return lax.ppermute(x, ("tm", "rows"), pairs)


def norm_act(field, gain_vec):
    values_f = field.astype(jnp.float32)
    inverse = lax.rsqrt(jnp.mean(values_f * values_f, axis=-1, keepdims=True) + EPSILON)
    return jax.nn.silu(values_f * inverse * gain_vec).astype(jnp.bfloat16)


def local_conv(extended, weight, keep_masks):
    frame_count = extended.shape[0] - 2
    height = extended.shape[1] - 2
    columns = extended.shape[2]
    channels = extended.shape[3]
    outputs = weight.shape[-1]
    padded = jnp.pad(extended, ((0, 0), (0, 0), (1, 1), (0, 0)))
    running = jnp.zeros((frame_count, height, columns, outputs), jnp.float32)
    for tap_time in range(3):
        pieces = []
        for tap_row in range(3):
            for tap_col in range(3):
                pieces.append(
                    padded[
                        tap_time : tap_time + frame_count,
                        tap_row : tap_row + height,
                        tap_col : tap_col + columns,
                    ]
                )
        stacked = jnp.concatenate(pieces, axis=-1).reshape(-1, 9 * channels)
        partial_value = jnp.dot(
            stacked,
            weight[tap_time].reshape(9 * channels, outputs),
            preferred_element_type=jnp.float32,
        )
        partial_value = partial_value.reshape(frame_count, height, columns, outputs)
        running = running + jnp.where(
            keep_masks[tap_time][:, None, None, None], partial_value, jnp.float32(0.0)
        )
    return running


def conv_kernel(keep_ref, *refs, layout, mode, per_step, firsts):
    sources = refs[: len(layout)]
    w_hbm, side_ref = refs[len(layout) : len(layout) + 2]
    o_ref, col_ref, w_ref, w_sem = refs[-4:]
    step = pl.program_id(0)
    steps = pl.num_programs(0)
    columns, channels = sources[0].shape[-2:]
    frame_count = keep_ref.shape[0] // 3
    cells = col_ref.shape[0]
    band = cells // per_step
    height = band // columns
    taps = 9 * channels

    outputs = w_ref.shape[-1] // 3

    def weight_copy(j, b):
        return pltpu.make_async_copy(
            w_hbm.at[pl.ds((j * 3 + b) * channels, channels)],
            w_ref.at[pl.ds(j * channels, channels), pl.ds(b * outputs, outputs)],
            w_sem.at[b],
        )

    def weight_wait(b):
        pltpu.make_async_copy(
            w_hbm.at[pl.ds(0, taps)], w_ref.at[:, pl.ds(b * outputs, outputs)], w_sem.at[b]
        ).wait()

    @pl.when(step == 0)
    def _():
        for b in (1, 0, 2):
            for j in range(9):
                weight_copy(j, b).start()

    def row_of(ext_frame, ext_row):
        for name, (frame_lo, frame_hi, row_lo, row_hi) in layout.items():
            if frame_lo <= ext_frame < frame_hi and row_lo <= ext_row < row_hi:
                return sources[list(layout).index(name)][ext_frame - frame_lo, ext_row - row_lo]
        raise ValueError("no source")

    for index, first in enumerate(firsts):

        @pl.when(step == index)
        def _():
            for fl in range(per_step):
                f = first + fl
                for k in range(3):
                    kept = keep_ref[k * frame_count + f] != 0
                    for a in range(3):
                        j = k * 3 + a
                        for i in range(height):
                            piece = row_of(f + k, a + i)
                            col_ref[
                                pl.ds(fl * band + i * columns, columns), pl.ds(j * channels, channels)
                            ] = jnp.where(kept, piece, jnp.zeros_like(piece))

    position = lax.broadcasted_iota(jnp.int32, (cells, outputs), 0) % columns

    @pl.when(step == 0)
    def _():
        for b in (1, 0, 2):
            weight_wait(b)

    product = jnp.dot(col_ref[...], w_ref[...], preferred_element_type=jnp.float32)
    running = None
    for b in (1, 0, 2):
        part = product[:, b * outputs : (b + 1) * outputs]
        if b == 0:
            part = jnp.where(position == 0, 0.0, pltpu.roll(part, 1, 0))
        elif b == 2:
            part = jnp.where(position == columns - 1, 0.0, pltpu.roll(part, cells - 1, 0))
        running = part if running is None else running + part
    if mode == "act":
        values_f = running.astype(jnp.bfloat16).astype(jnp.float32)
        inverse = lax.rsqrt(jnp.mean(values_f * values_f, axis=-1, keepdims=True) + EPSILON)
        scaled = values_f * inverse * side_ref[...]
        o_ref[...] = (scaled / (1.0 + jnp.exp(-scaled))).astype(o_ref.dtype)
    else:
        residual = side_ref[pl.ds(2 + firsts[0] + step * per_step, per_step), 1 : 1 + height]
        o_ref[...] = (residual.reshape(cells, outputs).astype(jnp.float32) + running).astype(
            o_ref.dtype
        )


def whole(x):
    return pl.BlockSpec(x.shape, lambda step: (0,) * x.ndim)


def conv_call(layout, sources, weight, keep, side, mode, per_step=2, firsts=None, into=None):
    columns, channels = sources[0].shape[-2:]
    frame_count = keep.shape[0] // 3
    rows_in = max(hi for (_, _, _, hi) in layout.values())
    band = (rows_in - 2) * columns
    cells = frame_count * band
    outputs = weight.shape[-1]
    weight_rows = weight.reshape(27 * channels, outputs)
    if firsts is None:
        firsts = tuple(range(0, frame_count, per_step))
    block_at = firsts[0] // per_step
    operands = [keep, *sources, weight_rows, side]
    extra_specs, aliases = [], {}
    if into is not None:
        extra_specs = [pl.BlockSpec(memory_space=pl.ANY)]
        aliases = {len(operands): 0}
        operands.append(into.reshape(cells, outputs))
    out = pl.pallas_call(
        functools.partial(conv_kernel, layout=layout, mode=mode, per_step=per_step, firsts=firsts),
        out_shape=jax.ShapeDtypeStruct((cells, outputs), jnp.bfloat16),
        in_specs=[pl.BlockSpec(memory_space=pltpu.SMEM)]
        + [whole(x) for x in sources]
        + [pl.BlockSpec(memory_space=pl.ANY), whole(side)]
        + extra_specs,
        out_specs=pl.BlockSpec((per_step * band, outputs), lambda step: (step + block_at, 0)),
        grid=(len(firsts),),
        input_output_aliases=aliases,
        scratch_shapes=[
            pltpu.VMEM((per_step * band, 9 * channels), jnp.bfloat16),
            pltpu.VMEM((9 * channels, 3 * outputs), jnp.bfloat16),
            pltpu.SemaphoreType.DMA((3,)),
        ],
        cost_estimate=pl.CostEstimate(
            flops=2 * len(firsts) * per_step * band * 27 * channels * outputs,
            transcendentals=len(firsts) * per_step * band * outputs,
            bytes_accessed=2 * (27 * channels * outputs + 3 * len(firsts) * per_step * band * outputs),
        ),
        compiler_params=pltpu.CompilerParams(vmem_limit_bytes=60 * 1024 * 1024),
    )(*operands)
    return out.reshape(frame_count, rows_in - 2, columns, outputs)


def on_device(
    generator_latent_rows,
    slot_group_row,
    frame_clip_number,
    input_convolution_weight,
    first_norm_gain,
    first_convolution_weight,
    second_norm_gain,
    second_convolution_weight,
):
    frame_count = F_DEV
    slots_here = generator_latent_rows.shape[1]
    packed_rows = generator_latent_rows.shape[2]
    parts_count = lax.axis_size("rows")
    rows_here = slots_here // frame_count
    height = rows_here * parts_count
    columns = packed_rows // LATENT_CHANNELS
    band_index = lax.axis_index("rows")
    frame_group_index = lax.axis_index("tm")

    ids = jnp.broadcast_to(
        slot_group_row.astype(jnp.bfloat16)[:, :, None], (1, slots_here, ID_LANES)
    )
    packed = jnp.concatenate([generator_latent_rows, ids], axis=-1)
    parts_total = lax.axis_size("rows")
    pieces = [packed]
    for by in range(1, parts_total):
        ring = [(i, (i + by) % parts_total) for i in range(parts_total)]
        pieces.append(lax.ppermute(packed, "rows", ring))
    gathered = jnp.concatenate(pieces, axis=1)[0]
    values = gathered[:, :packed_rows]
    slot_ids = gathered[:, packed_rows].astype(jnp.int32)

    window_rows = rows_here + 4
    frame_of = jnp.arange(frame_count, dtype=jnp.int32)[:, None]
    row_of = band_index * rows_here - 2 + jnp.arange(window_rows, dtype=jnp.int32)[None, :]
    wanted = (frame_of * height + row_of).reshape(-1)
    valid = jnp.broadcast_to((row_of >= 0) & (row_of < height), (frame_count, window_rows)).reshape(-1)
    selector = ((wanted[:, None] == slot_ids[None, :]) & valid[:, None]).astype(jnp.bfloat16)
    own_window = jnp.dot(selector, values, preferred_element_type=jnp.float32).astype(jnp.bfloat16)
    prev_window = shifted(own_window, "tm", 1)
    latent = jnp.concatenate([prev_window, own_window], axis=0).reshape(
        2 * frame_count, window_rows, columns, LATENT_CHANNELS
    )

    padded_clips = jnp.concatenate([jnp.full((4,), -1, jnp.int32), frame_clip_number])
    window = lax.dynamic_slice_in_dim(padded_clips, frame_group_index * frame_count, frame_count + 4)
    current_ext = window[2:]
    keep_ext = [window[k : k + frame_count + 2] == current_ext for k in range(3)]
    current = window[4:]
    keep_own = jnp.stack(
        [(window[k + 2 : k + 2 + frame_count] == current) for k in range(3)]
    ).astype(jnp.int32).reshape(-1)

    base_ext = local_conv(latent, input_convolution_weight, keep_ext).astype(jnp.bfloat16)
    first_act = norm_act(base_ext, first_norm_gain)
    ext_rows = band_index * rows_here - 1 + jnp.arange(rows_here + 2, dtype=jnp.int32)
    row_ok = (ext_rows >= 0) & (ext_rows < height)
    first_act = jnp.where(row_ok[None, :, None, None], first_act, jnp.zeros((), jnp.bfloat16))

    gain = second_norm_gain.reshape(1, -1)
    ext_frames, ext_rows_n = first_act.shape[:2]
    second_act = conv_call(
        {"x": (0, ext_frames, 0, ext_rows_n)},
        [first_act],
        first_convolution_weight,
        keep_own,
        gain,
        "act",
    )

    last = second_act[frame_count - 2 :]
    from_above = shifted(second_act[:, rows_here - 1 :], "rows", 1)
    from_below = shifted(second_act[:, :1], "rows", -1)
    prev_mid = shifted(last, "tm", 1)
    prev_above = diagonal(last[:, rows_here - 1 :], 1, 1)
    prev_below = diagonal(last[:, :1], 1, -1)
    layout = {
        "own": (2, 2 + frame_count, 1, 1 + rows_here),
        "above": (2, 2 + frame_count, 0, 1),
        "below": (2, 2 + frame_count, 1 + rows_here, 2 + rows_here),
        "mid": (0, 2, 1, 1 + rows_here),
        "corner_above": (0, 2, 0, 1),
        "corner_below": (0, 2, 1 + rows_here, 2 + rows_here),
    }
    late_layout = {name: layout[name] for name in ("own", "above", "below")}
    late_sources = [second_act, from_above, from_below]
    decoded = conv_call(
        late_layout, late_sources, second_convolution_weight, keep_own, base_ext, "res",
        firsts=(frame_count - 2,),
    )
    return conv_call(
        layout,
        [second_act, from_above, from_below, prev_mid, prev_above, prev_below],
        second_convolution_weight,
        keep_own,
        base_ext,
        "res",
        firsts=(0,),
        into=decoded,
    )


def solution(mesh):
    in_specs = (P("tm", "rows", None), P("tm", "rows"), P(), P(), P(), P(), P(), P())
    out_specs = P("tm", "rows", None, None)
    return jax.shard_map(
        on_device, mesh=mesh, in_specs=in_specs, out_specs=out_specs, check_vma=False
    )
```

```python
import functools

import jax
import jax.numpy as jnp
from jax import lax
from jax.experimental import pallas as pl
from jax.experimental.pallas import tpu as pltpu
from jax.sharding import PartitionSpec as P

LATENT_CHANNELS = 16
F_DEV = 4
ID_LANES = 128

EPSILON = 1e-06


def shifted(x, axis, by):
    devices = lax.axis_size(axis)
    pairs = [(i, i + by) for i in range(devices) if 0 <= i + by < devices]
    return lax.ppermute(x, axis, pairs)


def diagonal(x, by_tm, by_rows):
    groups, parts = lax.axis_size("tm"), lax.axis_size("rows")
    pairs = []
    for g in range(groups):
        for r in range(parts):
            dg, dr = g + by_tm, r + by_rows
            if 0 <= dg < groups and 0 <= dr < parts:
                pairs.append((g * parts + r, dg * parts + dr))
    return lax.ppermute(x, ("tm", "rows"), pairs)


def norm_act(field, gain_vec):
    values_f = field.astype(jnp.float32)
    inverse = lax.rsqrt(jnp.mean(values_f * values_f, axis=-1, keepdims=True) + EPSILON)
    return jax.nn.silu(values_f * inverse * gain_vec).astype(jnp.bfloat16)


def local_conv(extended, weight, keep_masks):
    frame_count = extended.shape[0] - 2
    height = extended.shape[1] - 2
    columns = extended.shape[2]
    channels = extended.shape[3]
    outputs = weight.shape[-1]
    padded = jnp.pad(extended, ((0, 0), (0, 0), (1, 1), (0, 0)))
    running = jnp.zeros((frame_count, height, columns, outputs), jnp.float32)
    for tap_time in range(3):
        pieces = []
        for tap_row in range(3):
            for tap_col in range(3):
                pieces.append(
                    padded[
                        tap_time : tap_time + frame_count,
                        tap_row : tap_row + height,
                        tap_col : tap_col + columns,
                    ]
                )
        stacked = jnp.concatenate(pieces, axis=-1).reshape(-1, 9 * channels)
        partial_value = jnp.dot(
            stacked,
            weight[tap_time].reshape(9 * channels, outputs),
            preferred_element_type=jnp.float32,
        )
        partial_value = partial_value.reshape(frame_count, height, columns, outputs)
        running = running + jnp.where(
            keep_masks[tap_time][:, None, None, None], partial_value, jnp.float32(0.0)
        )
    return running


def conv_kernel(keep_ref, *refs, layout, mode, per_step, firsts):
    sources = refs[: len(layout)]
    w_hbm, side_ref = refs[len(layout) : len(layout) + 2]
    o_ref, col_ref, w_ref, w_sem = refs[-4:]
    step = pl.program_id(0)
    steps = pl.num_programs(0)
    columns, channels = sources[0].shape[-2:]
    frame_count = keep_ref.shape[0] // 3
    cells = col_ref.shape[0]
    band = cells // per_step
    height = band // columns
    taps = 9 * channels

    outputs = w_ref.shape[-1] // 3

    def weight_copy(j, b):
        return pltpu.make_async_copy(
            w_hbm.at[pl.ds((j * 3 + b) * channels, channels)],
            w_ref.at[pl.ds(j * channels, channels), pl.ds(b * outputs, outputs)],
            w_sem.at[(j // 3) * 3 + b],
        )

    def weight_wait(k, b):
        pltpu.make_async_copy(
            w_hbm.at[pl.ds(0, 3 * channels)],
            w_ref.at[pl.ds(k * 3 * channels, 3 * channels), pl.ds(b * outputs, outputs)],
            w_sem.at[k * 3 + b],
        ).wait()

    @pl.when(step == 0)
    def _():
        for j in range(9):
            for b in range(3):
                weight_copy(j, b).start()

    def row_of(ext_frame, ext_row):
        for name, (frame_lo, frame_hi, row_lo, row_hi) in layout.items():
            if frame_lo <= ext_frame < frame_hi and row_lo <= ext_row < row_hi:
                return sources[list(layout).index(name)][ext_frame - frame_lo, ext_row - row_lo]
        raise ValueError("no source")

    for index, first in enumerate(firsts):

        @pl.when(step == index)
        def _():
            for fl in range(per_step):
                f = first + fl
                for k in range(3):
                    kept = keep_ref[k * frame_count + f] != 0
                    for a in range(3):
                        j = k * 3 + a
                        for i in range(height):
                            piece = row_of(f + k, a + i)
                            col_ref[
                                pl.ds(fl * band + i * columns, columns), pl.ds(j * channels, channels)
                            ] = jnp.where(kept, piece, jnp.zeros_like(piece))

    position = lax.broadcasted_iota(jnp.int32, (cells, outputs), 0) % columns

    product = None
    for k in range(3):

        @pl.when(step == 0)
        def _():
            for b in range(3):
                weight_wait(k, b)

        lanes = pl.ds(k * 3 * channels, 3 * channels)
        term = jnp.dot(col_ref[:, lanes], w_ref[lanes, :], preferred_element_type=jnp.float32)
        product = term if product is None else product + term
    running = None
    for b in (1, 0, 2):
        part = product[:, b * outputs : (b + 1) * outputs]
        if b == 0:
            part = jnp.where(position == 0, 0.0, pltpu.roll(part, 1, 0))
        elif b == 2:
            part = jnp.where(position == columns - 1, 0.0, pltpu.roll(part, cells - 1, 0))
        running = part if running is None else running + part
    if mode == "act":
        values_f = running.astype(jnp.bfloat16).astype(jnp.float32)
        inverse = lax.rsqrt(jnp.mean(values_f * values_f, axis=-1, keepdims=True) + EPSILON)
        scaled = values_f * inverse * side_ref[...]
        o_ref[...] = (scaled / (1.0 + jnp.exp(-scaled))).astype(o_ref.dtype)
    else:
        residual = side_ref[:, 1 : 1 + height]
        o_ref[...] = (residual.reshape(cells, outputs).astype(jnp.float32) + running).astype(
            o_ref.dtype
        )


def whole(x):
    return pl.BlockSpec(x.shape, lambda step: (0,) * x.ndim)


def conv_call(layout, sources, weight, keep, side, mode, per_step=2, firsts=None, into=None):
    columns, channels = sources[0].shape[-2:]
    frame_count = keep.shape[0] // 3
    rows_in = max(hi for (_, _, _, hi) in layout.values())
    band = (rows_in - 2) * columns
    cells = frame_count * band
    outputs = weight.shape[-1]
    weight_rows = weight.reshape(27 * channels, outputs)
    if firsts is None:
        firsts = tuple(range(0, frame_count, per_step))
    block_at = firsts[0] // per_step
    if mode == "act":
        side_spec = whole(side)
    else:
        side_spec = pl.BlockSpec(
            (per_step,) + side.shape[1:], lambda step: (1 + block_at + step, 0, 0, 0)
        )
    operands = [keep, *sources, weight_rows, side]
    extra_specs, aliases = [], {}
    if into is not None:
        extra_specs = [pl.BlockSpec(memory_space=pl.ANY)]
        aliases = {len(operands): 0}
        operands.append(into.reshape(cells, outputs))
    out = pl.pallas_call(
        functools.partial(conv_kernel, layout=layout, mode=mode, per_step=per_step, firsts=firsts),
        out_shape=jax.ShapeDtypeStruct((cells, outputs), jnp.bfloat16),
        in_specs=[pl.BlockSpec(memory_space=pltpu.SMEM)]
        + [whole(x) for x in sources]
        + [pl.BlockSpec(memory_space=pl.ANY), side_spec]
        + extra_specs,
        out_specs=pl.BlockSpec((per_step * band, outputs), lambda step: (step + block_at, 0)),
        grid=(len(firsts),),
        input_output_aliases=aliases,
        scratch_shapes=[
            pltpu.VMEM((per_step * band, 9 * channels), jnp.bfloat16),
            pltpu.VMEM((9 * channels, 3 * outputs), jnp.bfloat16),
            pltpu.SemaphoreType.DMA((9,)),
        ],
        cost_estimate=pl.CostEstimate(
            flops=2 * len(firsts) * per_step * band * 27 * channels * outputs,
            transcendentals=len(firsts) * per_step * band * outputs,
            bytes_accessed=2 * (27 * channels * outputs + 3 * len(firsts) * per_step * band * outputs),
        ),
        compiler_params=pltpu.CompilerParams(vmem_limit_bytes=60 * 1024 * 1024),
    )(*operands)
    return out.reshape(frame_count, rows_in - 2, columns, outputs)


def on_device(
    generator_latent_rows,
    slot_group_row,
    frame_clip_number,
    input_convolution_weight,
    first_norm_gain,
    first_convolution_weight,
    second_norm_gain,
    second_convolution_weight,
):
    frame_count = F_DEV
    slots_here = generator_latent_rows.shape[1]
    packed_rows = generator_latent_rows.shape[2]
    parts_count = lax.axis_size("rows")
    rows_here = slots_here // frame_count
    height = rows_here * parts_count
    columns = packed_rows // LATENT_CHANNELS
    band_index = lax.axis_index("rows")
    frame_group_index = lax.axis_index("tm")

    ids = jnp.broadcast_to(
        slot_group_row.astype(jnp.bfloat16)[:, :, None], (1, slots_here, ID_LANES)
    )
    packed = jnp.concatenate([generator_latent_rows, ids], axis=-1)
    parts_total = lax.axis_size("rows")
    pieces = [packed]
    for by in range(1, parts_total):
        ring = [(i, (i + by) % parts_total) for i in range(parts_total)]
        pieces.append(lax.ppermute(packed, "rows", ring))
    gathered = jnp.concatenate(pieces, axis=1)[0]
    values = gathered[:, :packed_rows]
    slot_ids = gathered[:, packed_rows].astype(jnp.int32)

    window_rows = rows_here + 4
    frame_of = jnp.arange(frame_count, dtype=jnp.int32)[:, None]
    row_of = band_index * rows_here - 2 + jnp.arange(window_rows, dtype=jnp.int32)[None, :]
    wanted = (frame_of * height + row_of).reshape(-1)
    valid = jnp.broadcast_to((row_of >= 0) & (row_of < height), (frame_count, window_rows)).reshape(-1)
    selector = ((wanted[:, None] == slot_ids[None, :]) & valid[:, None]).astype(jnp.bfloat16)
    own_window = jnp.dot(selector, values, preferred_element_type=jnp.float32).astype(jnp.bfloat16)
    prev_window = shifted(own_window, "tm", 1)
    latent = jnp.concatenate([prev_window, own_window], axis=0).reshape(
        2 * frame_count, window_rows, columns, LATENT_CHANNELS
    )

    padded_clips = jnp.concatenate([jnp.full((4,), -1, jnp.int32), frame_clip_number])
    window = lax.dynamic_slice_in_dim(padded_clips, frame_group_index * frame_count, frame_count + 4)
    current_ext = window[2:]
    keep_ext = [window[k : k + frame_count + 2] == current_ext for k in range(3)]
    current = window[4:]
    keep_own = jnp.stack(
        [(window[k + 2 : k + 2 + frame_count] == current) for k in range(3)]
    ).astype(jnp.int32).reshape(-1)

    base_ext = local_conv(latent, input_convolution_weight, keep_ext).astype(jnp.bfloat16)
    first_act = norm_act(base_ext, first_norm_gain)
    ext_rows = band_index * rows_here - 1 + jnp.arange(rows_here + 2, dtype=jnp.int32)
    row_ok = (ext_rows >= 0) & (ext_rows < height)
    first_act = jnp.where(row_ok[None, :, None, None], first_act, jnp.zeros((), jnp.bfloat16))

    gain = second_norm_gain.reshape(1, -1)
    ext_frames, ext_rows_n = first_act.shape[:2]
    second_act = conv_call(
        {"x": (0, ext_frames, 0, ext_rows_n)},
        [first_act],
        first_convolution_weight,
        keep_own,
        gain,
        "act",
    )

    last = second_act[frame_count - 2 :]
    from_above = shifted(second_act[:, rows_here - 1 :], "rows", 1)
    from_below = shifted(second_act[:, :1], "rows", -1)
    prev_mid = shifted(last, "tm", 1)
    prev_above = diagonal(last[:, rows_here - 1 :], 1, 1)
    prev_below = diagonal(last[:, :1], 1, -1)
    layout = {
        "own": (2, 2 + frame_count, 1, 1 + rows_here),
        "above": (2, 2 + frame_count, 0, 1),
        "below": (2, 2 + frame_count, 1 + rows_here, 2 + rows_here),
        "mid": (0, 2, 1, 1 + rows_here),
        "corner_above": (0, 2, 0, 1),
        "corner_below": (0, 2, 1 + rows_here, 2 + rows_here),
    }
    late_layout = {name: layout[name] for name in ("own", "above", "below")}
    late_sources = [second_act, from_above, from_below]
    decoded = conv_call(
        late_layout, late_sources, second_convolution_weight, keep_own, base_ext, "res",
        firsts=(frame_count - 2,),
    )
    return conv_call(
        layout,
        [second_act, from_above, from_below, prev_mid, prev_above, prev_below],
        second_convolution_weight,
        keep_own,
        base_ext,
        "res",
        firsts=(0,),
        into=decoded,
    )


def solution(mesh):
    in_specs = (P("tm", "rows", None), P("tm", "rows"), P(), P(), P(), P(), P(), P())
    out_specs = P("tm", "rows", None, None)
    return jax.shard_map(
        on_device, mesh=mesh, in_specs=in_specs, out_specs=out_specs, check_vma=False
    )
```

```python
import functools

import jax
import jax.numpy as jnp
from jax import lax
from jax.experimental import pallas as pl
from jax.experimental.pallas import tpu as pltpu
from jax.sharding import PartitionSpec as P

LATENT_CHANNELS = 16
F_DEV = 4
ID_LANES = 128

EPSILON = 1e-06


def shifted(x, axis, by):
    devices = lax.axis_size(axis)
    pairs = [(i, i + by) for i in range(devices) if 0 <= i + by < devices]
    return lax.ppermute(x, axis, pairs)


def diagonal(x, by_tm, by_rows):
    groups, parts = lax.axis_size("tm"), lax.axis_size("rows")
    pairs = []
    for g in range(groups):
        for r in range(parts):
            dg, dr = g + by_tm, r + by_rows
            if 0 <= dg < groups and 0 <= dr < parts:
                pairs.append((g * parts + r, dg * parts + dr))
    return lax.ppermute(x, ("tm", "rows"), pairs)


def norm_act(field, gain_vec):
    values_f = field.astype(jnp.float32)
    inverse = lax.rsqrt(jnp.mean(values_f * values_f, axis=-1, keepdims=True) + EPSILON)
    return jax.nn.silu(values_f * inverse * gain_vec).astype(jnp.bfloat16)


def local_conv(extended, weight, keep_masks):
    frame_count = extended.shape[0] - 2
    height = extended.shape[1] - 2
    columns = extended.shape[2]
    channels = extended.shape[3]
    outputs = weight.shape[-1]
    padded = jnp.pad(extended, ((0, 0), (0, 0), (1, 1), (0, 0)))
    running = jnp.zeros((frame_count, height, columns, outputs), jnp.float32)
    for tap_time in range(3):
        pieces = []
        for tap_row in range(3):
            for tap_col in range(3):
                pieces.append(
                    padded[
                        tap_time : tap_time + frame_count,
                        tap_row : tap_row + height,
                        tap_col : tap_col + columns,
                    ]
                )
        stacked = jnp.concatenate(pieces, axis=-1).reshape(-1, 9 * channels)
        partial_value = jnp.dot(
            stacked,
            weight[tap_time].reshape(9 * channels, outputs),
            preferred_element_type=jnp.float32,
        )
        partial_value = partial_value.reshape(frame_count, height, columns, outputs)
        running = running + jnp.where(
            keep_masks[tap_time][:, None, None, None], partial_value, jnp.float32(0.0)
        )
    return running


def conv_kernel(keep_ref, *refs, layout, mode, per_step, firsts, pre_act):
    sources = refs[: len(layout)]
    w_hbm, side_ref = refs[len(layout) : len(layout) + 2]
    if pre_act:
        gain_ref, row_keep_ref = refs[len(layout) + 2 : len(layout) + 4]
        o_ref, col_ref, w_ref, w_sem, act_ref = refs[-5:]
    else:
        o_ref, col_ref, w_ref, w_sem = refs[-4:]
    step = pl.program_id(0)
    steps = pl.num_programs(0)
    columns, channels = sources[0].shape[-2:]
    frame_count = keep_ref.shape[0] // 3
    cells = col_ref.shape[0]
    band = cells // per_step
    height = band // columns
    taps = 9 * channels

    outputs = w_ref.shape[-1] // 3

    def weight_copy(j, b):
        return pltpu.make_async_copy(
            w_hbm.at[pl.ds((j * 3 + b) * channels, channels)],
            w_ref.at[pl.ds(j * channels, channels), pl.ds(b * outputs, outputs)],
            w_sem.at[b],
        )

    def weight_wait(b):
        pltpu.make_async_copy(
            w_hbm.at[pl.ds(0, taps)], w_ref.at[:, pl.ds(b * outputs, outputs)], w_sem.at[b]
        ).wait()

    @pl.when(step == 0)
    def _():
        for b in (1, 0, 2):
            for j in range(9):
                weight_copy(j, b).start()

    if pre_act:
        source = sources[0]

        @pl.when(step == 0)
        def _():
            for e in range(source.shape[0]):
                for i in range(source.shape[1]):
                    values_f = source[e, i].astype(jnp.float32)
                    inverse = lax.rsqrt(
                        jnp.mean(values_f * values_f, axis=-1, keepdims=True) + EPSILON
                    )
                    scaled = values_f * inverse * gain_ref[...]
                    active = scaled / (1.0 + jnp.exp(-scaled))
                    act_ref[e, i] = jnp.where(
                        row_keep_ref[i] != 0, active, jnp.zeros_like(active)
                    ).astype(act_ref.dtype)

        sources = (act_ref,)

    def row_of(ext_frame, ext_row):
        for name, (frame_lo, frame_hi, row_lo, row_hi) in layout.items():
            if frame_lo <= ext_frame < frame_hi and row_lo <= ext_row < row_hi:
                return sources[list(layout).index(name)][ext_frame - frame_lo, ext_row - row_lo]
        raise ValueError("no source")

    for index, first in enumerate(firsts):

        @pl.when(step == index)
        def _():
            for fl in range(per_step):
                f = first + fl
                for k in range(3):
                    kept = keep_ref[k * frame_count + f] != 0
                    for a in range(3):
                        j = k * 3 + a
                        for i in range(height):
                            piece = row_of(f + k, a + i)
                            col_ref[
                                pl.ds(fl * band + i * columns, columns), pl.ds(j * channels, channels)
                            ] = jnp.where(kept, piece, jnp.zeros_like(piece))

    position = lax.broadcasted_iota(jnp.int32, (cells, outputs), 0) % columns

    @pl.when(step == 0)
    def _():
        for b in (1, 0, 2):
            weight_wait(b)

    product = jnp.dot(col_ref[...], w_ref[...], preferred_element_type=jnp.float32)
    running = None
    for b in (1, 0, 2):
        part = product[:, b * outputs : (b + 1) * outputs]
        if b == 0:
            part = jnp.where(position == 0, 0.0, pltpu.roll(part, 1, 0))
        elif b == 2:
            part = jnp.where(position == columns - 1, 0.0, pltpu.roll(part, cells - 1, 0))
        running = part if running is None else running + part
    if mode == "act":
        values_f = running.astype(jnp.bfloat16).astype(jnp.float32)
        inverse = lax.rsqrt(jnp.mean(values_f * values_f, axis=-1, keepdims=True) + EPSILON)
        scaled = values_f * inverse * side_ref[...]
        o_ref[...] = (scaled / (1.0 + jnp.exp(-scaled))).astype(o_ref.dtype)
    else:
        residual = side_ref[pl.ds(2 + firsts[0] + step * per_step, per_step), 1 : 1 + height]
        o_ref[...] = (residual.reshape(cells, outputs).astype(jnp.float32) + running).astype(
            o_ref.dtype
        )


def whole(x):
    return pl.BlockSpec(x.shape, lambda step: (0,) * x.ndim)


def conv_call(layout, sources, weight, keep, side, mode, per_step=2, firsts=None, into=None,
              pre_gain=None, row_keep=None):
    columns, channels = sources[0].shape[-2:]
    frame_count = keep.shape[0] // 3
    rows_in = max(hi for (_, _, _, hi) in layout.values())
    band = (rows_in - 2) * columns
    cells = frame_count * band
    outputs = weight.shape[-1]
    weight_rows = weight.reshape(27 * channels, outputs)
    if firsts is None:
        firsts = tuple(range(0, frame_count, per_step))
    block_at = firsts[0] // per_step
    operands = [keep, *sources, weight_rows, side]
    extra_specs, aliases = [], {}
    pre_act = pre_gain is not None
    scratch = []
    if pre_act:
        extra_specs = [whole(pre_gain), pl.BlockSpec(memory_space=pltpu.SMEM)]
        operands += [pre_gain, row_keep]
        scratch = [pltpu.VMEM(sources[0].shape, jnp.bfloat16)]
    if into is not None:
        extra_specs = extra_specs + [pl.BlockSpec(memory_space=pl.ANY)]
        aliases = {len(operands): 0}
        operands.append(into.reshape(cells, outputs))
    out = pl.pallas_call(
        functools.partial(
            conv_kernel, layout=layout, mode=mode, per_step=per_step, firsts=firsts,
            pre_act=pre_act,
        ),
        out_shape=jax.ShapeDtypeStruct((cells, outputs), jnp.bfloat16),
        in_specs=[pl.BlockSpec(memory_space=pltpu.SMEM)]
        + [whole(x) for x in sources]
        + [pl.BlockSpec(memory_space=pl.ANY), whole(side)]
        + extra_specs,
        out_specs=pl.BlockSpec((per_step * band, outputs), lambda step: (step + block_at, 0)),
        grid=(len(firsts),),
        input_output_aliases=aliases,
        scratch_shapes=[
            pltpu.VMEM((per_step * band, 9 * channels), jnp.bfloat16),
            pltpu.VMEM((9 * channels, 3 * outputs), jnp.bfloat16),
            pltpu.SemaphoreType.DMA((3,)),
        ] + scratch,
        cost_estimate=pl.CostEstimate(
            flops=2 * len(firsts) * per_step * band * 27 * channels * outputs,
            transcendentals=len(firsts) * per_step * band * outputs,
            bytes_accessed=2 * (27 * channels * outputs + 3 * len(firsts) * per_step * band * outputs),
        ),
        compiler_params=pltpu.CompilerParams(vmem_limit_bytes=60 * 1024 * 1024),
    )(*operands)
    return out.reshape(frame_count, rows_in - 2, columns, outputs)


def on_device(
    generator_latent_rows,
    slot_group_row,
    frame_clip_number,
    input_convolution_weight,
    first_norm_gain,
    first_convolution_weight,
    second_norm_gain,
    second_convolution_weight,
):
    frame_count = F_DEV
    slots_here = generator_latent_rows.shape[1]
    packed_rows = generator_latent_rows.shape[2]
    parts_count = lax.axis_size("rows")
    rows_here = slots_here // frame_count
    height = rows_here * parts_count
    columns = packed_rows // LATENT_CHANNELS
    band_index = lax.axis_index("rows")
    frame_group_index = lax.axis_index("tm")

    ids = jnp.broadcast_to(
        slot_group_row.astype(jnp.bfloat16)[:, :, None], (1, slots_here, ID_LANES)
    )
    packed = jnp.concatenate([generator_latent_rows, ids], axis=-1)
    parts_total = lax.axis_size("rows")
    pieces = [packed]
    for by in range(1, parts_total):
        ring = [(i, (i + by) % parts_total) for i in range(parts_total)]
        pieces.append(lax.ppermute(packed, "rows", ring))
    gathered = jnp.concatenate(pieces, axis=1)[0]
    values = gathered[:, :packed_rows]
    slot_ids = gathered[:, packed_rows].astype(jnp.int32)

    window_rows = rows_here + 4
    frame_of = jnp.arange(frame_count, dtype=jnp.int32)[:, None]
    row_of = band_index * rows_here - 2 + jnp.arange(window_rows, dtype=jnp.int32)[None, :]
    wanted = (frame_of * height + row_of).reshape(-1)
    valid = jnp.broadcast_to((row_of >= 0) & (row_of < height), (frame_count, window_rows)).reshape(-1)
    selector = ((wanted[:, None] == slot_ids[None, :]) & valid[:, None]).astype(jnp.bfloat16)
    own_window = jnp.dot(selector, values, preferred_element_type=jnp.float32).astype(jnp.bfloat16)
    prev_window = shifted(own_window, "tm", 1)
    latent = jnp.concatenate([prev_window, own_window], axis=0).reshape(
        2 * frame_count, window_rows, columns, LATENT_CHANNELS
    )

    padded_clips = jnp.concatenate([jnp.full((4,), -1, jnp.int32), frame_clip_number])
    window = lax.dynamic_slice_in_dim(padded_clips, frame_group_index * frame_count, frame_count + 4)
    current_ext = window[2:]
    keep_ext = [window[k : k + frame_count + 2] == current_ext for k in range(3)]
    current = window[4:]
    keep_own = jnp.stack(
        [(window[k + 2 : k + 2 + frame_count] == current) for k in range(3)]
    ).astype(jnp.int32).reshape(-1)

    base_ext = local_conv(latent, input_convolution_weight, keep_ext).astype(jnp.bfloat16)
    ext_rows = band_index * rows_here - 1 + jnp.arange(rows_here + 2, dtype=jnp.int32)
    row_ok = ((ext_rows >= 0) & (ext_rows < height)).astype(jnp.int32)

    gain = second_norm_gain.reshape(1, -1)
    ext_frames, ext_rows_n = base_ext.shape[:2]
    second_act = conv_call(
        {"x": (0, ext_frames, 0, ext_rows_n)},
        [base_ext],
        first_convolution_weight,
        keep_own,
        gain,
        "act",
        pre_gain=first_norm_gain.reshape(1, -1),
        row_keep=row_ok,
    )

    last = second_act[frame_count - 2 :]
    from_above = shifted(second_act[:, rows_here - 1 :], "rows", 1)
    from_below = shifted(second_act[:, :1], "rows", -1)
    prev_mid = shifted(last, "tm", 1)
    prev_above = diagonal(last[:, rows_here - 1 :], 1, 1)
    prev_below = diagonal(last[:, :1], 1, -1)
    layout = {
        "own": (2, 2 + frame_count, 1, 1 + rows_here),
        "above": (2, 2 + frame_count, 0, 1),
        "below": (2, 2 + frame_count, 1 + rows_here, 2 + rows_here),
        "mid": (0, 2, 1, 1 + rows_here),
        "corner_above": (0, 2, 0, 1),
        "corner_below": (0, 2, 1 + rows_here, 2 + rows_here),
    }
    late_layout = {name: layout[name] for name in ("own", "above", "below")}
    late_sources = [second_act, from_above, from_below]
    decoded = conv_call(
        late_layout, late_sources, second_convolution_weight, keep_own, base_ext, "res",
        firsts=(frame_count - 2,),
    )
    return conv_call(
        layout,
        [second_act, from_above, from_below, prev_mid, prev_above, prev_below],
        second_convolution_weight,
        keep_own,
        base_ext,
        "res",
        firsts=(0,),
        into=decoded,
    )


def solution(mesh):
    in_specs = (P("tm", "rows", None), P("tm", "rows"), P(), P(), P(), P(), P(), P())
    out_specs = P("tm", "rows", None, None)
    return jax.shard_map(
        on_device, mesh=mesh, in_specs=in_specs, out_specs=out_specs, check_vma=False
    )
```

```python
import functools

import jax
import jax.numpy as jnp
from jax import lax
from jax.experimental import pallas as pl
from jax.experimental.pallas import tpu as pltpu
from jax.sharding import PartitionSpec as P

LATENT_CHANNELS = 16
F_DEV = 4
ID_LANES = 128

EPSILON = 1e-06


def shifted(x, axis, by):
    devices = lax.axis_size(axis)
    pairs = [(i, i + by) for i in range(devices) if 0 <= i + by < devices]
    return lax.ppermute(x, axis, pairs)


def diagonal(x, by_tm, by_rows):
    groups, parts = lax.axis_size("tm"), lax.axis_size("rows")
    pairs = []
    for g in range(groups):
        for r in range(parts):
            dg, dr = g + by_tm, r + by_rows
            if 0 <= dg < groups and 0 <= dr < parts:
                pairs.append((g * parts + r, dg * parts + dr))
    return lax.ppermute(x, ("tm", "rows"), pairs)


def norm_act(field, gain_vec):
    values_f = field.astype(jnp.float32)
    inverse = lax.rsqrt(jnp.mean(values_f * values_f, axis=-1, keepdims=True) + EPSILON)
    return jax.nn.silu(values_f * inverse * gain_vec).astype(jnp.bfloat16)


def local_conv(extended, weight, keep_masks):
    frame_count = extended.shape[0] - 2
    height = extended.shape[1] - 2
    columns = extended.shape[2]
    channels = extended.shape[3]
    outputs = weight.shape[-1]
    padded = jnp.pad(extended, ((0, 0), (0, 0), (1, 1), (0, 0)))
    running = jnp.zeros((frame_count, height, columns, outputs), jnp.float32)
    for tap_time in range(3):
        pieces = []
        for tap_row in range(3):
            for tap_col in range(3):
                pieces.append(
                    padded[
                        tap_time : tap_time + frame_count,
                        tap_row : tap_row + height,
                        tap_col : tap_col + columns,
                    ]
                )
        stacked = jnp.concatenate(pieces, axis=-1).reshape(-1, 9 * channels)
        partial_value = jnp.dot(
            stacked,
            weight[tap_time].reshape(9 * channels, outputs),
            preferred_element_type=jnp.float32,
        )
        partial_value = partial_value.reshape(frame_count, height, columns, outputs)
        running = running + jnp.where(
            keep_masks[tap_time][:, None, None, None], partial_value, jnp.float32(0.0)
        )
    return running


def conv_kernel(keep_ref, *refs, layout, mode, per_step, firsts):
    sources = refs[: len(layout)]
    w_hbm, side_ref = refs[len(layout) : len(layout) + 2]
    o_ref, col_ref, w_ref, w_sem = refs[-4:]
    step = pl.program_id(0)
    steps = pl.num_programs(0)
    columns, channels = sources[0].shape[-2:]
    frame_count = keep_ref.shape[0] // 3
    cells = col_ref.shape[0]
    band = cells // per_step
    height = band // columns
    taps = 9 * channels

    outputs = w_ref.shape[-1] // 3

    def weight_copy(j, b):
        return pltpu.make_async_copy(
            w_hbm.at[pl.ds((j * 3 + b) * channels, channels)],
            w_ref.at[pl.ds(j * channels, channels), pl.ds(b * outputs, outputs)],
            w_sem.at[b],
        )

    def weight_wait(b):
        pltpu.make_async_copy(
            w_hbm.at[pl.ds(0, taps)], w_ref.at[:, pl.ds(b * outputs, outputs)], w_sem.at[b]
        ).wait()

    @pl.when(step == 0)
    def _():
        for b in (1, 0, 2):
            for j in range(9):
                weight_copy(j, b).start()

    def row_of(ext_frame, ext_row):
        for name, (frame_lo, frame_hi, row_lo, row_hi) in layout.items():
            if frame_lo <= ext_frame < frame_hi and row_lo <= ext_row < row_hi:
                return sources[list(layout).index(name)][ext_frame - frame_lo, ext_row - row_lo]
        raise ValueError("no source")

    for index, first in enumerate(firsts):

        @pl.when(step == index)
        def _():
            for fl in range(per_step):
                f = first + fl
                for k in range(3):
                    kept = keep_ref[k * frame_count + f] != 0
                    for a in range(3):
                        j = k * 3 + a
                        for i in range(height):
                            piece = row_of(f + k, a + i)
                            col_ref[
                                pl.ds(fl * band + i * columns, columns), pl.ds(j * channels, channels)
                            ] = jnp.where(kept, piece, jnp.zeros_like(piece))

    position = lax.broadcasted_iota(jnp.int32, (cells, outputs), 0) % columns

    @pl.when(step == 0)
    def _():
        for b in (1, 0, 2):
            weight_wait(b)

    product = jnp.dot(col_ref[...], w_ref[...], preferred_element_type=jnp.float32)
    running = None
    for b in (1, 0, 2):
        part = product[:, b * outputs : (b + 1) * outputs]
        if b == 0:
            part = jnp.where(position == 0, 0.0, pltpu.roll(part, 1, 0))
        elif b == 2:
            part = jnp.where(position == columns - 1, 0.0, pltpu.roll(part, cells - 1, 0))
        running = part if running is None else running + part
    if mode == "act":
        values_f = running.astype(jnp.bfloat16).astype(jnp.float32)
        inverse = lax.rsqrt(jnp.mean(values_f * values_f, axis=-1, keepdims=True) + EPSILON)
        scaled = values_f * inverse * side_ref[...]
        o_ref[...] = (scaled / (1.0 + jnp.exp(-scaled))).astype(o_ref.dtype)
    else:
        residual = side_ref[pl.ds(2 + firsts[0] + step * per_step, per_step), 1 : 1 + height]
        o_ref[...] = (residual.reshape(cells, outputs).astype(jnp.float32) + running).astype(
            o_ref.dtype
        )


def whole(x):
    return pl.BlockSpec(x.shape, lambda step: (0,) * x.ndim)


def conv_call(layout, sources, weight, keep, side, mode, per_step=2, firsts=None, into=None):
    columns, channels = sources[0].shape[-2:]
    frame_count = keep.shape[0] // 3
    rows_in = max(hi for (_, _, _, hi) in layout.values())
    band = (rows_in - 2) * columns
    cells = frame_count * band
    outputs = weight.shape[-1]
    weight_rows = weight.reshape(27 * channels, outputs)
    if firsts is None:
        firsts = tuple(range(0, frame_count, per_step))
    block_at = firsts[0] // per_step
    operands = [keep, *sources, weight_rows, side]
    extra_specs, aliases = [], {}
    if into is not None:
        extra_specs = [pl.BlockSpec(memory_space=pl.ANY)]
        aliases = {len(operands): 0}
        operands.append(into.reshape(cells, outputs))
    out = pl.pallas_call(
        functools.partial(conv_kernel, layout=layout, mode=mode, per_step=per_step, firsts=firsts),
        out_shape=jax.ShapeDtypeStruct((cells, outputs), jnp.bfloat16),
        in_specs=[pl.BlockSpec(memory_space=pltpu.SMEM)]
        + [whole(x) for x in sources]
        + [pl.BlockSpec(memory_space=pl.ANY), whole(side)]
        + extra_specs,
        out_specs=pl.BlockSpec((per_step * band, outputs), lambda step: (step + block_at, 0)),
        grid=(len(firsts),),
        input_output_aliases=aliases,
        scratch_shapes=[
            pltpu.VMEM((per_step * band, 9 * channels), jnp.bfloat16),
            pltpu.VMEM((9 * channels, 3 * outputs), jnp.bfloat16),
            pltpu.SemaphoreType.DMA((3,)),
        ],
        cost_estimate=pl.CostEstimate(
            flops=2 * len(firsts) * per_step * band * 27 * channels * outputs,
            transcendentals=len(firsts) * per_step * band * outputs,
            bytes_accessed=2 * (27 * channels * outputs + 3 * len(firsts) * per_step * band * outputs),
        ),
        compiler_params=pltpu.CompilerParams(vmem_limit_bytes=60 * 1024 * 1024),
    )(*operands)
    return out.reshape(frame_count, rows_in - 2, columns, outputs)


def on_device(
    generator_latent_rows,
    slot_group_row,
    frame_clip_number,
    input_convolution_weight,
    first_norm_gain,
    first_convolution_weight,
    second_norm_gain,
    second_convolution_weight,
):
    frame_count = F_DEV
    slots_here = generator_latent_rows.shape[1]
    packed_rows = generator_latent_rows.shape[2]
    parts_count = lax.axis_size("rows")
    rows_here = slots_here // frame_count
    height = rows_here * parts_count
    columns = packed_rows // LATENT_CHANNELS
    band_index = lax.axis_index("rows")
    frame_group_index = lax.axis_index("tm")

    ids = jnp.broadcast_to(
        slot_group_row.astype(jnp.bfloat16)[:, :, None], (1, slots_here, ID_LANES)
    )
    packed = jnp.concatenate([generator_latent_rows, ids], axis=-1)
    gathered = lax.all_gather(packed, "rows", axis=1, tiled=True)[0]
    values = gathered[:, :packed_rows]
    slot_ids = gathered[:, packed_rows].astype(jnp.int32)

    window_rows = rows_here + 4
    frame_of = jnp.arange(frame_count, dtype=jnp.int32)[:, None]
    row_of = band_index * rows_here - 2 + jnp.arange(window_rows, dtype=jnp.int32)[None, :]
    wanted = (frame_of * height + row_of).reshape(-1)
    valid = jnp.broadcast_to((row_of >= 0) & (row_of < height), (frame_count, window_rows)).reshape(-1)
    selector = ((wanted[:, None] == slot_ids[None, :]) & valid[:, None]).astype(jnp.bfloat16)
    own_window = jnp.dot(selector, values, preferred_element_type=jnp.float32).astype(jnp.bfloat16)
    prev_window = shifted(own_window, "tm", 1)
    latent = jnp.concatenate([prev_window, own_window], axis=0).reshape(
        2 * frame_count, window_rows, columns, LATENT_CHANNELS
    )

    padded_clips = jnp.concatenate([jnp.full((4,), -1, jnp.int32), frame_clip_number])
    window = lax.dynamic_slice_in_dim(padded_clips, frame_group_index * frame_count, frame_count + 4)
    current_ext = window[2:]
    keep_ext = [window[k : k + frame_count + 2] == current_ext for k in range(3)]
    current = window[4:]
    keep_own = jnp.stack(
        [(window[k + 2 : k + 2 + frame_count] == current) for k in range(3)]
    ).astype(jnp.int32).reshape(-1)

    base_ext = local_conv(latent, input_convolution_weight, keep_ext).astype(jnp.bfloat16)
    first_act = norm_act(base_ext, first_norm_gain)
    ext_rows = band_index * rows_here - 1 + jnp.arange(rows_here + 2, dtype=jnp.int32)
    row_ok = (ext_rows >= 0) & (ext_rows < height)
    first_act = jnp.where(row_ok[None, :, None, None], first_act, jnp.zeros((), jnp.bfloat16))

    gain = second_norm_gain.reshape(1, -1)
    ext_frames, ext_rows_n = first_act.shape[:2]
    second_act = conv_call(
        {"x": (0, ext_frames, 0, ext_rows_n)},
        [first_act],
        first_convolution_weight,
        keep_own,
        gain,
        "act",
    )

    last = second_act[frame_count - 2 :]
    from_above = shifted(second_act[:, rows_here - 1 :], "rows", 1)
    from_below = shifted(second_act[:, :1], "rows", -1)
    prev_mid = shifted(last, "tm", 1)
    prev_above = diagonal(last[:, rows_here - 1 :], 1, 1)
    prev_below = diagonal(last[:, :1], 1, -1)
    layout = {
        "own": (2, 2 + frame_count, 1, 1 + rows_here),
        "above": (2, 2 + frame_count, 0, 1),
        "below": (2, 2 + frame_count, 1 + rows_here, 2 + rows_here),
        "mid": (0, 2, 1, 1 + rows_here),
        "corner_above": (0, 2, 0, 1),
        "corner_below": (0, 2, 1 + rows_here, 2 + rows_here),
    }
    late_layout = {name: layout[name] for name in ("own", "above", "below")}
    late_sources = [second_act, from_above, from_below]
    decoded = conv_call(
        late_layout, late_sources, second_convolution_weight, keep_own, base_ext, "res",
        firsts=(frame_count - 2,),
    )
    return conv_call(
        layout,
        [second_act, from_above, from_below, prev_mid, prev_above, prev_below],
        second_convolution_weight,
        keep_own,
        base_ext,
        "res",
        firsts=(0,),
        into=decoded,
    )


def solution(mesh):
    in_specs = (P("tm", "rows", None), P("tm", "rows"), P(), P(), P(), P(), P(), P())
    out_specs = P("tm", "rows", None, None)
    return jax.shard_map(
        on_device, mesh=mesh, in_specs=in_specs, out_specs=out_specs, check_vma=False
    )
```

```python
import functools

import jax
import jax.numpy as jnp
from jax import lax
from jax.experimental import pallas as pl
from jax.experimental.pallas import tpu as pltpu
from jax.sharding import PartitionSpec as P

LATENT_CHANNELS = 16
F_DEV = 4
ID_LANES = 128

EPSILON = 1e-06


def shifted(x, axis, by):
    devices = lax.axis_size(axis)
    pairs = [(i, i + by) for i in range(devices) if 0 <= i + by < devices]
    return lax.ppermute(x, axis, pairs)


def diagonal(x, by_tm, by_rows):
    groups, parts = lax.axis_size("tm"), lax.axis_size("rows")
    pairs = []
    for g in range(groups):
        for r in range(parts):
            dg, dr = g + by_tm, r + by_rows
            if 0 <= dg < groups and 0 <= dr < parts:
                pairs.append((g * parts + r, dg * parts + dr))
    return lax.ppermute(x, ("tm", "rows"), pairs)


def norm_act(field, gain_vec):
    values_f = field.astype(jnp.float32)
    inverse = lax.rsqrt(jnp.mean(values_f * values_f, axis=-1, keepdims=True) + EPSILON)
    return jax.nn.silu(values_f * inverse * gain_vec).astype(jnp.bfloat16)


def local_conv(extended, weight, keep_masks):
    frame_count = extended.shape[0] - 2
    height = extended.shape[1] - 2
    columns = extended.shape[2]
    channels = extended.shape[3]
    outputs = weight.shape[-1]
    padded = jnp.pad(extended, ((0, 0), (0, 0), (1, 1), (0, 0)))
    running = jnp.zeros((frame_count, height, columns, outputs), jnp.float32)
    for tap_time in range(3):
        pieces = []
        for tap_row in range(3):
            for tap_col in range(3):
                pieces.append(
                    padded[
                        tap_time : tap_time + frame_count,
                        tap_row : tap_row + height,
                        tap_col : tap_col + columns,
                    ]
                )
        stacked = jnp.concatenate(pieces, axis=-1).reshape(-1, 9 * channels)
        partial_value = jnp.dot(
            stacked,
            weight[tap_time].reshape(9 * channels, outputs),
            preferred_element_type=jnp.float32,
        )
        partial_value = partial_value.reshape(frame_count, height, columns, outputs)
        running = running + jnp.where(
            keep_masks[tap_time][:, None, None, None], partial_value, jnp.float32(0.0)
        )
    return running


def conv_kernel(keep_ref, *refs, layout, mode, per_step, firsts):
    sources = refs[: len(layout)]
    w_hbm, side_ref = refs[len(layout) : len(layout) + 2]
    o_ref, col_ref, w_ref, w_sem = refs[-4:]
    step = pl.program_id(0)
    steps = pl.num_programs(0)
    columns, channels = sources[0].shape[-2:]
    frame_count = keep_ref.shape[0] // 3
    cells = col_ref.shape[0]
    band = cells // per_step
    height = band // columns
    taps = 9 * channels

    outputs = w_ref.shape[-1] // 3

    def weight_copy(j, b):
        return pltpu.make_async_copy(
            w_hbm.at[pl.ds((j * 3 + b) * channels, channels)],
            w_ref.at[pl.ds(j * channels, channels), pl.ds(b * outputs, outputs)],
            w_sem.at[b],
        )

    def weight_wait(b):
        pltpu.make_async_copy(
            w_hbm.at[pl.ds(0, taps)], w_ref.at[:, pl.ds(b * outputs, outputs)], w_sem.at[b]
        ).wait()

    @pl.when(step == 0)
    def _():
        for b in (1, 0, 2):
            for j in range(9):
                weight_copy(j, b).start()

    def row_of(ext_frame, ext_row):
        for name, (frame_lo, frame_hi, row_lo, row_hi) in layout.items():
            if frame_lo <= ext_frame < frame_hi and row_lo <= ext_row < row_hi:
                return sources[list(layout).index(name)][ext_frame - frame_lo, ext_row - row_lo]
        raise ValueError("no source")

    for index, first in enumerate(firsts):

        @pl.when(step == index)
        def _():
            for fl in range(per_step):
                f = first + fl
                for k in range(3):
                    kept = keep_ref[k * frame_count + f] != 0
                    for a in range(3):
                        j = k * 3 + a
                        for i in range(height):
                            piece = row_of(f + k, a + i)
                            col_ref[
                                pl.ds(fl * band + i * columns, columns), pl.ds(j * channels, channels)
                            ] = jnp.where(kept, piece, jnp.zeros_like(piece))

    position = lax.broadcasted_iota(jnp.int32, (cells, outputs), 0) % columns

    @pl.when(step == 0)
    def _():
        for b in (1, 0, 2):
            weight_wait(b)

    product = jnp.dot(col_ref[...], w_ref[...], preferred_element_type=jnp.float32)
    running = None
    for b in (1, 0, 2):
        part = product[:, b * outputs : (b + 1) * outputs]
        if b == 0:
            part = jnp.where(position == 0, 0.0, pltpu.roll(part, 1, 0))
        elif b == 2:
            part = jnp.where(position == columns - 1, 0.0, pltpu.roll(part, cells - 1, 0))
        running = part if running is None else running + part
    if mode == "act":
        values_f = running.astype(jnp.bfloat16).astype(jnp.float32)
        inverse = lax.rsqrt(jnp.mean(values_f * values_f, axis=-1, keepdims=True) + EPSILON)
        scaled = values_f * inverse * side_ref[...]
        o_ref[...] = (scaled / (1.0 + jnp.exp(-scaled))).astype(o_ref.dtype)
    else:
        residual = side_ref[pl.ds(2 + firsts[0] + step * per_step, per_step), 1 : 1 + height]
        o_ref[...] = (residual.reshape(cells, outputs).astype(jnp.float32) + running).astype(
            o_ref.dtype
        )


def whole(x):
    return pl.BlockSpec(x.shape, lambda step: (0,) * x.ndim)


def conv_call(layout, sources, weight, keep, side, mode, per_step=2, firsts=None, into=None):
    columns, channels = sources[0].shape[-2:]
    frame_count = keep.shape[0] // 3
    rows_in = max(hi for (_, _, _, hi) in layout.values())
    band = (rows_in - 2) * columns
    cells = frame_count * band
    outputs = weight.shape[-1]
    weight_rows = weight.reshape(27 * channels, outputs)
    if firsts is None:
        firsts = tuple(range(0, frame_count, per_step))
    block_at = firsts[0] // per_step
    operands = [keep, *sources, weight_rows, side]
    extra_specs, aliases = [], {}
    if into is not None:
        extra_specs = [pl.BlockSpec(memory_space=pl.ANY)]
        aliases = {len(operands): 0}
        operands.append(into.reshape(cells, outputs))
    out = pl.pallas_call(
        functools.partial(conv_kernel, layout=layout, mode=mode, per_step=per_step, firsts=firsts),
        out_shape=jax.ShapeDtypeStruct((cells, outputs), jnp.bfloat16),
        in_specs=[pl.BlockSpec(memory_space=pltpu.SMEM)]
        + [whole(x) for x in sources]
        + [pl.BlockSpec(memory_space=pl.ANY), whole(side)]
        + extra_specs,
        out_specs=pl.BlockSpec((per_step * band, outputs), lambda step: (step + block_at, 0)),
        grid=(len(firsts),),
        input_output_aliases=aliases,
        scratch_shapes=[
            pltpu.VMEM((per_step * band, 9 * channels), jnp.bfloat16),
            pltpu.VMEM((9 * channels, 3 * outputs), jnp.bfloat16),
            pltpu.SemaphoreType.DMA((3,)),
        ],
        cost_estimate=pl.CostEstimate(
            flops=2 * len(firsts) * per_step * band * 27 * channels * outputs,
            transcendentals=len(firsts) * per_step * band * outputs,
            bytes_accessed=2 * (27 * channels * outputs + 3 * len(firsts) * per_step * band * outputs),
        ),
        compiler_params=pltpu.CompilerParams(vmem_limit_bytes=60 * 1024 * 1024),
    )(*operands)
    return out.reshape(frame_count, rows_in - 2, columns, outputs)


def on_device(
    generator_latent_rows,
    slot_group_row,
    frame_clip_number,
    input_convolution_weight,
    first_norm_gain,
    first_convolution_weight,
    second_norm_gain,
    second_convolution_weight,
):
    frame_count = F_DEV
    slots_here = generator_latent_rows.shape[1]
    packed_rows = generator_latent_rows.shape[2]
    parts_count = lax.axis_size("rows")
    rows_here = slots_here // frame_count
    height = rows_here * parts_count
    columns = packed_rows // LATENT_CHANNELS
    band_index = lax.axis_index("rows")
    frame_group_index = lax.axis_index("tm")

    ids = jnp.broadcast_to(
        slot_group_row.astype(jnp.bfloat16)[:, :, None], (1, slots_here, ID_LANES)
    )
    packed = jnp.concatenate([generator_latent_rows, ids], axis=-1)
    parts_total = lax.axis_size("rows")
    pieces = [packed]
    for by in range(1, parts_total):
        ring = [(i, (i + by) % parts_total) for i in range(parts_total)]
        pieces.append(lax.ppermute(packed, "rows", ring))
    gathered = jnp.concatenate(pieces, axis=1)[0]
    values = gathered[:, :packed_rows]
    slot_ids = gathered[:, packed_rows].astype(jnp.int32)

    window_rows = rows_here + 4
    frame_of = jnp.arange(frame_count, dtype=jnp.int32)[:, None]
    row_of = band_index * rows_here - 2 + jnp.arange(window_rows, dtype=jnp.int32)[None, :]
    wanted = (frame_of * height + row_of).reshape(-1)
    valid = jnp.broadcast_to((row_of >= 0) & (row_of < height), (frame_count, window_rows)).reshape(-1)
    selector = ((wanted[:, None] == slot_ids[None, :]) & valid[:, None]).astype(jnp.bfloat16)
    own_window = jnp.dot(selector, values, preferred_element_type=jnp.float32).astype(jnp.bfloat16)
    prev_window = shifted(own_window, "tm", 1)
    latent = jnp.concatenate([prev_window, own_window], axis=0).reshape(
        2 * frame_count, window_rows, columns, LATENT_CHANNELS
    )

    padded_clips = jnp.concatenate([jnp.full((4,), -1, jnp.int32), frame_clip_number])
    window = lax.dynamic_slice_in_dim(padded_clips, frame_group_index * frame_count, frame_count + 4)
    current_ext = window[2:]
    keep_ext = [window[k : k + frame_count + 2] == current_ext for k in range(3)]
    current = window[4:]
    keep_own = jnp.stack(
        [(window[k + 2 : k + 2 + frame_count] == current) for k in range(3)]
    ).astype(jnp.int32).reshape(-1)

    base_ext = local_conv(latent, input_convolution_weight, keep_ext).astype(jnp.bfloat16)
    first_act = norm_act(base_ext, first_norm_gain)
    ext_rows = band_index * rows_here - 1 + jnp.arange(rows_here + 2, dtype=jnp.int32)
    row_ok = (ext_rows >= 0) & (ext_rows < height)
    first_act = jnp.where(row_ok[None, :, None, None], first_act, jnp.zeros((), jnp.bfloat16))

    gain = second_norm_gain.reshape(1, -1)
    ext_frames, ext_rows_n = first_act.shape[:2]
    second_act = conv_call(
        {"x": (0, ext_frames, 0, ext_rows_n)},
        [first_act],
        first_convolution_weight,
        keep_own,
        gain,
        "act",
        per_step=frame_count,
    )

    last = second_act[frame_count - 2 :]
    from_above = shifted(second_act[:, rows_here - 1 :], "rows", 1)
    from_below = shifted(second_act[:, :1], "rows", -1)
    prev_mid = shifted(last, "tm", 1)
    prev_above = diagonal(last[:, rows_here - 1 :], 1, 1)
    prev_below = diagonal(last[:, :1], 1, -1)
    layout = {
        "own": (2, 2 + frame_count, 1, 1 + rows_here),
        "above": (2, 2 + frame_count, 0, 1),
        "below": (2, 2 + frame_count, 1 + rows_here, 2 + rows_here),
        "mid": (0, 2, 1, 1 + rows_here),
        "corner_above": (0, 2, 0, 1),
        "corner_below": (0, 2, 1 + rows_here, 2 + rows_here),
    }
    late_layout = {name: layout[name] for name in ("own", "above", "below")}
    late_sources = [second_act, from_above, from_below]
    decoded = conv_call(
        late_layout, late_sources, second_convolution_weight, keep_own, base_ext, "res",
        firsts=(frame_count - 2,),
    )
    return conv_call(
        layout,
        [second_act, from_above, from_below, prev_mid, prev_above, prev_below],
        second_convolution_weight,
        keep_own,
        base_ext,
        "res",
        firsts=(0,),
        into=decoded,
    )


def solution(mesh):
    in_specs = (P("tm", "rows", None), P("tm", "rows"), P(), P(), P(), P(), P(), P())
    out_specs = P("tm", "rows", None, None)
    return jax.shard_map(
        on_device, mesh=mesh, in_specs=in_specs, out_specs=out_specs, check_vma=False
    )
```

```python
import functools

import jax
import jax.numpy as jnp
from jax import lax
from jax.experimental import pallas as pl
from jax.experimental.pallas import tpu as pltpu
from jax.sharding import PartitionSpec as P

LATENT_CHANNELS = 16
F_DEV = 4
ID_LANES = 128

EPSILON = 1e-06


def shifted(x, axis, by):
    devices = lax.axis_size(axis)
    pairs = [(i, i + by) for i in range(devices) if 0 <= i + by < devices]
    return lax.ppermute(x, axis, pairs)


def diagonal(x, by_tm, by_rows):
    groups, parts = lax.axis_size("tm"), lax.axis_size("rows")
    pairs = []
    for g in range(groups):
        for r in range(parts):
            dg, dr = g + by_tm, r + by_rows
            if 0 <= dg < groups and 0 <= dr < parts:
                pairs.append((g * parts + r, dg * parts + dr))
    return lax.ppermute(x, ("tm", "rows"), pairs)


def norm_act(field, gain_vec):
    values_f = field.astype(jnp.float32)
    inverse = lax.rsqrt(jnp.mean(values_f * values_f, axis=-1, keepdims=True) + EPSILON)
    return jax.nn.silu(values_f * inverse * gain_vec).astype(jnp.bfloat16)


def local_conv(extended, weight, keep_masks):
    frame_count = extended.shape[0] - 2
    height = extended.shape[1] - 2
    columns = extended.shape[2]
    channels = extended.shape[3]
    outputs = weight.shape[-1]
    padded = jnp.pad(extended, ((0, 0), (0, 0), (1, 1), (0, 0)))
    running = jnp.zeros((frame_count, height, columns, outputs), jnp.float32)
    for tap_time in range(3):
        pieces = []
        for tap_row in range(3):
            for tap_col in range(3):
                pieces.append(
                    padded[
                        tap_time : tap_time + frame_count,
                        tap_row : tap_row + height,
                        tap_col : tap_col + columns,
                    ]
                )
        stacked = jnp.concatenate(pieces, axis=-1).reshape(-1, 9 * channels)
        partial_value = jnp.dot(
            stacked,
            weight[tap_time].reshape(9 * channels, outputs),
            preferred_element_type=jnp.float32,
        )
        partial_value = partial_value.reshape(frame_count, height, columns, outputs)
        running = running + jnp.where(
            keep_masks[tap_time][:, None, None, None], partial_value, jnp.float32(0.0)
        )
    return running


def conv_kernel(keep_ref, *refs, layout, mode, per_step, firsts):
    sources = refs[: len(layout)]
    w_hbm, side_ref = refs[len(layout) : len(layout) + 2]
    o_ref, col_ref, w_ref, w_sem = refs[-4:]
    step = pl.program_id(0)
    steps = pl.num_programs(0)
    columns, channels = sources[0].shape[-2:]
    frame_count = keep_ref.shape[0] // 3
    cells = col_ref.shape[0]
    band = cells // per_step
    height = band // columns
    taps = 9 * channels

    outputs = w_ref.shape[-1] // 3

    def weight_copy(j, b):
        return pltpu.make_async_copy(
            w_hbm.at[pl.ds((j * 3 + b) * channels, channels)],
            w_ref.at[pl.ds(j * channels, channels), pl.ds(b * outputs, outputs)],
            w_sem.at[b],
        )

    def weight_wait(b):
        pltpu.make_async_copy(
            w_hbm.at[pl.ds(0, taps)], w_ref.at[:, pl.ds(b * outputs, outputs)], w_sem.at[b]
        ).wait()

    @pl.when(step == 0)
    def _():
        for b in (1, 0, 2):
            for j in range(9):
                weight_copy(j, b).start()

    def row_of(ext_frame, ext_row):
        for name, (frame_lo, frame_hi, row_lo, row_hi) in layout.items():
            if frame_lo <= ext_frame < frame_hi and row_lo <= ext_row < row_hi:
                return sources[list(layout).index(name)][ext_frame - frame_lo, ext_row - row_lo]
        raise ValueError("no source")

    for index, first in enumerate(firsts):

        @pl.when(step == index)
        def _():
            for fl in range(per_step):
                f = first + fl
                for k in range(3):
                    kept = keep_ref[k * frame_count + f] != 0
                    for a in range(3):
                        j = k * 3 + a
                        for i in range(height):
                            piece = row_of(f + k, a + i)
                            col_ref[
                                pl.ds(fl * band + i * columns, columns), pl.ds(j * channels, channels)
                            ] = jnp.where(kept, piece, jnp.zeros_like(piece))

    position = lax.broadcasted_iota(jnp.int32, (cells, outputs), 0) % columns

    @pl.when(step == 0)
    def _():
        for b in (1, 0, 2):
            weight_wait(b)

    product = jnp.dot(col_ref[...], w_ref[...], preferred_element_type=jnp.float32)
    running = None
    for b in (1, 0, 2):
        part = product[:, b * outputs : (b + 1) * outputs]
        if b == 0:
            part = jnp.where(position == 0, 0.0, pltpu.roll(part, 1, 0))
        elif b == 2:
            part = jnp.where(position == columns - 1, 0.0, pltpu.roll(part, cells - 1, 0))
        running = part if running is None else running + part
    if mode == "act":
        values_f = running.astype(jnp.bfloat16).astype(jnp.float32)
        inverse = lax.rsqrt(jnp.mean(values_f * values_f, axis=-1, keepdims=True) + EPSILON)
        scaled = values_f * inverse * side_ref[...]
        o_ref[...] = (scaled / (1.0 + jnp.exp(-scaled))).astype(o_ref.dtype)
    else:
        residual = side_ref[:, 1 : 1 + height]
        o_ref[...] = (residual.reshape(cells, outputs).astype(jnp.float32) + running).astype(
            o_ref.dtype
        )


def whole(x):
    return pl.BlockSpec(x.shape, lambda step: (0,) * x.ndim)


def conv_call(layout, sources, weight, keep, side, mode, per_step=2, firsts=None, into=None):
    columns, channels = sources[0].shape[-2:]
    frame_count = keep.shape[0] // 3
    rows_in = max(hi for (_, _, _, hi) in layout.values())
    band = (rows_in - 2) * columns
    cells = frame_count * band
    outputs = weight.shape[-1]
    weight_rows = weight.reshape(27 * channels, outputs)
    if firsts is None:
        firsts = tuple(range(0, frame_count, per_step))
    block_at = firsts[0] // per_step
    if mode == "act":
        side_spec = whole(side)
    else:
        side_spec = pl.BlockSpec(
            (per_step,) + side.shape[1:], lambda step: (1 + block_at + step, 0, 0, 0)
        )
    operands = [keep, *sources, weight_rows, side]
    extra_specs, aliases = [], {}
    if into is not None:
        extra_specs = [pl.BlockSpec(memory_space=pl.ANY)]
        aliases = {len(operands): 0}
        operands.append(into.reshape(cells, outputs))
    out = pl.pallas_call(
        functools.partial(conv_kernel, layout=layout, mode=mode, per_step=per_step, firsts=firsts),
        out_shape=jax.ShapeDtypeStruct((cells, outputs), jnp.bfloat16),
        in_specs=[pl.BlockSpec(memory_space=pltpu.SMEM)]
        + [whole(x) for x in sources]
        + [pl.BlockSpec(memory_space=pl.ANY), side_spec]
        + extra_specs,
        out_specs=pl.BlockSpec((per_step * band, outputs), lambda step: (step + block_at, 0)),
        grid=(len(firsts),),
        input_output_aliases=aliases,
        scratch_shapes=[
            pltpu.VMEM((per_step * band, 9 * channels), jnp.bfloat16),
            pltpu.VMEM((9 * channels, 3 * outputs), jnp.bfloat16),
            pltpu.SemaphoreType.DMA((3,)),
        ],
        cost_estimate=pl.CostEstimate(
            flops=2 * len(firsts) * per_step * band * 27 * channels * outputs,
            transcendentals=len(firsts) * per_step * band * outputs,
            bytes_accessed=2 * (27 * channels * outputs + 3 * len(firsts) * per_step * band * outputs),
        ),
        compiler_params=pltpu.CompilerParams(vmem_limit_bytes=60 * 1024 * 1024),
    )(*operands)
    return out.reshape(frame_count, rows_in - 2, columns, outputs)


def on_device(
    generator_latent_rows,
    slot_group_row,
    frame_clip_number,
    input_convolution_weight,
    first_norm_gain,
    first_convolution_weight,
    second_norm_gain,
    second_convolution_weight,
):
    frame_count = F_DEV
    slots_here = generator_latent_rows.shape[1]
    packed_rows = generator_latent_rows.shape[2]
    parts_count = lax.axis_size("rows")
    rows_here = slots_here // frame_count
    height = rows_here * parts_count
    columns = packed_rows // LATENT_CHANNELS
    band_index = lax.axis_index("rows")
    frame_group_index = lax.axis_index("tm")

    ids = jnp.broadcast_to(
        slot_group_row.astype(jnp.bfloat16)[:, :, None], (1, slots_here, ID_LANES)
    )
    packed = jnp.concatenate([generator_latent_rows, ids], axis=-1)
    parts_total = lax.axis_size("rows")
    pieces = [packed]
    for by in range(1, parts_total):
        ring = [(i, (i + by) % parts_total) for i in range(parts_total)]
        pieces.append(lax.ppermute(packed, "rows", ring))
    gathered = jnp.concatenate(pieces, axis=1)[0]
    values = gathered[:, :packed_rows]
    slot_ids = gathered[:, packed_rows].astype(jnp.int32)

    window_rows = rows_here + 4
    frame_of = jnp.arange(frame_count, dtype=jnp.int32)[:, None]
    row_of = band_index * rows_here - 2 + jnp.arange(window_rows, dtype=jnp.int32)[None, :]
    wanted = (frame_of * height + row_of).reshape(-1)
    valid = jnp.broadcast_to((row_of >= 0) & (row_of < height), (frame_count, window_rows)).reshape(-1)
    selector = ((wanted[:, None] == slot_ids[None, :]) & valid[:, None]).astype(jnp.bfloat16)
    own_window = jnp.dot(selector, values, preferred_element_type=jnp.float32).astype(jnp.bfloat16)
    prev_window = shifted(own_window, "tm", 1)
    latent = jnp.concatenate([prev_window, own_window], axis=0).reshape(
        2 * frame_count, window_rows, columns, LATENT_CHANNELS
    )

    padded_clips = jnp.concatenate([jnp.full((4,), -1, jnp.int32), frame_clip_number])
    window = lax.dynamic_slice_in_dim(padded_clips, frame_group_index * frame_count, frame_count + 4)
    current_ext = window[2:]
    keep_ext = [window[k : k + frame_count + 2] == current_ext for k in range(3)]
    current = window[4:]
    keep_own = jnp.stack(
        [(window[k + 2 : k + 2 + frame_count] == current) for k in range(3)]
    ).astype(jnp.int32).reshape(-1)

    base_ext = local_conv(latent, input_convolution_weight, keep_ext).astype(jnp.bfloat16)
    first_act = norm_act(base_ext, first_norm_gain)
    ext_rows = band_index * rows_here - 1 + jnp.arange(rows_here + 2, dtype=jnp.int32)
    row_ok = (ext_rows >= 0) & (ext_rows < height)
    first_act = jnp.where(row_ok[None, :, None, None], first_act, jnp.zeros((), jnp.bfloat16))

    gain = second_norm_gain.reshape(1, -1)
    ext_frames, ext_rows_n = first_act.shape[:2]
    second_act = conv_call(
        {"x": (0, ext_frames, 0, ext_rows_n)},
        [first_act],
        first_convolution_weight,
        keep_own,
        gain,
        "act",
        per_step=frame_count,
    )

    last = second_act[frame_count - 2 :]
    from_above = shifted(second_act[:, rows_here - 1 :], "rows", 1)
    from_below = shifted(second_act[:, :1], "rows", -1)
    prev_mid = shifted(last, "tm", 1)
    prev_above = diagonal(last[:, rows_here - 1 :], 1, 1)
    prev_below = diagonal(last[:, :1], 1, -1)
    layout = {
        "own": (2, 2 + frame_count, 1, 1 + rows_here),
        "above": (2, 2 + frame_count, 0, 1),
        "below": (2, 2 + frame_count, 1 + rows_here, 2 + rows_here),
        "mid": (0, 2, 1, 1 + rows_here),
        "corner_above": (0, 2, 0, 1),
        "corner_below": (0, 2, 1 + rows_here, 2 + rows_here),
    }
    late_layout = {name: layout[name] for name in ("own", "above", "below")}
    late_sources = [second_act, from_above, from_below]
    decoded = conv_call(
        late_layout, late_sources, second_convolution_weight, keep_own, base_ext, "res",
        firsts=(frame_count - 2,),
    )
    return conv_call(
        layout,
        [second_act, from_above, from_below, prev_mid, prev_above, prev_below],
        second_convolution_weight,
        keep_own,
        base_ext,
        "res",
        firsts=(0,),
        into=decoded,
    )


def solution(mesh):
    in_specs = (P("tm", "rows", None), P("tm", "rows"), P(), P(), P(), P(), P(), P())
    out_specs = P("tm", "rows", None, None)
    return jax.shard_map(
        on_device, mesh=mesh, in_specs=in_specs, out_specs=out_specs, check_vma=False
    )
```

```python
import functools

import jax
import jax.numpy as jnp
from jax import lax
from jax.experimental import pallas as pl
from jax.experimental.pallas import tpu as pltpu
from jax.sharding import PartitionSpec as P

LATENT_CHANNELS = 16
F_DEV = 4
ID_LANES = 128

EPSILON = 1e-06


def shifted(x, axis, by):
    devices = lax.axis_size(axis)
    pairs = [(i, i + by) for i in range(devices) if 0 <= i + by < devices]
    return lax.ppermute(x, axis, pairs)


def diagonal(x, by_tm, by_rows):
    groups, parts = lax.axis_size("tm"), lax.axis_size("rows")
    pairs = []
    for g in range(groups):
        for r in range(parts):
            dg, dr = g + by_tm, r + by_rows
            if 0 <= dg < groups and 0 <= dr < parts:
                pairs.append((g * parts + r, dg * parts + dr))
    return lax.ppermute(x, ("tm", "rows"), pairs)


def norm_act(field, gain_vec):
    values_f = field.astype(jnp.float32)
    inverse = lax.rsqrt(jnp.mean(values_f * values_f, axis=-1, keepdims=True) + EPSILON)
    return jax.nn.silu(values_f * inverse * gain_vec).astype(jnp.bfloat16)


def local_conv(extended, weight, keep_masks):
    frame_count = extended.shape[0] - 2
    height = extended.shape[1] - 2
    columns = extended.shape[2]
    channels = extended.shape[3]
    outputs = weight.shape[-1]
    padded = jnp.pad(extended, ((0, 0), (0, 0), (1, 1), (0, 0)))
    running = jnp.zeros((frame_count, height, columns, outputs), jnp.float32)
    for tap_time in range(3):
        pieces = []
        for tap_row in range(3):
            for tap_col in range(3):
                pieces.append(
                    padded[
                        tap_time : tap_time + frame_count,
                        tap_row : tap_row + height,
                        tap_col : tap_col + columns,
                    ]
                )
        stacked = jnp.concatenate(pieces, axis=-1).reshape(-1, 9 * channels)
        partial_value = jnp.dot(
            stacked,
            weight[tap_time].reshape(9 * channels, outputs),
            preferred_element_type=jnp.float32,
        )
        partial_value = partial_value.reshape(frame_count, height, columns, outputs)
        running = running + jnp.where(
            keep_masks[tap_time][:, None, None, None], partial_value, jnp.float32(0.0)
        )
    return running


def conv_kernel(keep_ref, *refs, layout, mode, per_step, firsts):
    sources = refs[: len(layout)]
    w_hbm, side_ref = refs[len(layout) : len(layout) + 2]
    o_ref, col_ref, w_ref, w_sem = refs[-4:]
    step = pl.program_id(0)
    steps = pl.num_programs(0)
    columns, channels = sources[0].shape[-2:]
    frame_count = keep_ref.shape[0] // 3
    cells = col_ref.shape[0]
    band = cells // per_step
    height = band // columns
    taps = 9 * channels

    outputs = w_ref.shape[-1] // 3

    def weight_copy(j, b):
        return pltpu.make_async_copy(
            w_hbm.at[pl.ds((j * 3 + b) * channels, channels)],
            w_ref.at[pl.ds(j * channels, channels), pl.ds(b * outputs, outputs)],
            w_sem.at[b],
        )

    def weight_wait(b):
        pltpu.make_async_copy(
            w_hbm.at[pl.ds(0, taps)], w_ref.at[:, pl.ds(b * outputs, outputs)], w_sem.at[b]
        ).wait()

    @pl.when(step == 0)
    def _():
        for b in (1, 0, 2):
            for j in range(9):
                weight_copy(j, b).start()

    def row_of(ext_frame, ext_row):
        for name, (frame_lo, frame_hi, row_lo, row_hi) in layout.items():
            if frame_lo <= ext_frame < frame_hi and row_lo <= ext_row < row_hi:
                return sources[list(layout).index(name)][ext_frame - frame_lo, ext_row - row_lo]
        raise ValueError("no source")

    for index, first in enumerate(firsts):

        @pl.when(step == index)
        def _():
            for fl in range(per_step):
                f = first + fl
                for k in range(3):
                    kept = keep_ref[k * frame_count + f] != 0
                    for a in range(3):
                        j = k * 3 + a
                        for i in range(height):
                            piece = row_of(f + k, a + i)
                            col_ref[
                                pl.ds(fl * band + i * columns, columns), pl.ds(j * channels, channels)
                            ] = jnp.where(kept, piece, jnp.zeros_like(piece))

    position = lax.broadcasted_iota(jnp.int32, (cells, outputs), 0) % columns

    @pl.when(step == 0)
    def _():
        for b in (1, 0, 2):
            weight_wait(b)

    product = jnp.dot(col_ref[...], w_ref[...], preferred_element_type=jnp.float32)
    running = None
    for b in (1, 0, 2):
        part = product[:, b * outputs : (b + 1) * outputs]
        if b == 0:
            part = jnp.where(position == 0, 0.0, pltpu.roll(part, 1, 0))
        elif b == 2:
            part = jnp.where(position == columns - 1, 0.0, pltpu.roll(part, cells - 1, 0))
        running = part if running is None else running + part
    if mode == "act":
        values_f = running.astype(jnp.bfloat16).astype(jnp.float32)
        inverse = lax.rsqrt(jnp.mean(values_f * values_f, axis=-1, keepdims=True) + EPSILON)
        scaled = values_f * inverse * side_ref[...]
        o_ref[...] = (scaled / (1.0 + jnp.exp(-scaled))).astype(o_ref.dtype)
    else:
        residual = side_ref[:, 1 : 1 + height]
        o_ref[...] = (residual.reshape(cells, outputs).astype(jnp.float32) + running).astype(
            o_ref.dtype
        )


def whole(x):
    return pl.BlockSpec(x.shape, lambda step: (0,) * x.ndim)


def conv_call(layout, sources, weight, keep, side, mode, per_step=2, firsts=None, into=None):
    columns, channels = sources[0].shape[-2:]
    frame_count = keep.shape[0] // 3
    rows_in = max(hi for (_, _, _, hi) in layout.values())
    band = (rows_in - 2) * columns
    cells = frame_count * band
    outputs = weight.shape[-1]
    weight_rows = weight.reshape(27 * channels, outputs)
    if firsts is None:
        firsts = tuple(range(0, frame_count, per_step))
    block_at = firsts[0] // per_step
    if mode == "act":
        side_spec = whole(side)
    else:
        side_spec = pl.BlockSpec(
            (per_step,) + side.shape[1:], lambda step: (1 + block_at + step, 0, 0, 0)
        )
    operands = [keep, *sources, weight_rows, side]
    extra_specs, aliases = [], {}
    if into is not None:
        extra_specs = [pl.BlockSpec(memory_space=pl.ANY)]
        aliases = {len(operands): 0}
        operands.append(into.reshape(cells, outputs))
    out = pl.pallas_call(
        functools.partial(conv_kernel, layout=layout, mode=mode, per_step=per_step, firsts=firsts),
        out_shape=jax.ShapeDtypeStruct((cells, outputs), jnp.bfloat16),
        in_specs=[pl.BlockSpec(memory_space=pltpu.SMEM)]
        + [
            pl.BlockSpec((hi - lo,) + x.shape[1:], lambda step: (0,) * x.ndim)
            for x, (lo, hi, _, _) in zip(sources, layout.values())
        ]
        + [pl.BlockSpec(memory_space=pl.ANY), side_spec]
        + extra_specs,
        out_specs=pl.BlockSpec((per_step * band, outputs), lambda step: (step + block_at, 0)),
        grid=(len(firsts),),
        input_output_aliases=aliases,
        scratch_shapes=[
            pltpu.VMEM((per_step * band, 9 * channels), jnp.bfloat16),
            pltpu.VMEM((9 * channels, 3 * outputs), jnp.bfloat16),
            pltpu.SemaphoreType.DMA((3,)),
        ],
        cost_estimate=pl.CostEstimate(
            flops=2 * len(firsts) * per_step * band * 27 * channels * outputs,
            transcendentals=len(firsts) * per_step * band * outputs,
            bytes_accessed=2 * (27 * channels * outputs + 3 * len(firsts) * per_step * band * outputs),
        ),
        compiler_params=pltpu.CompilerParams(vmem_limit_bytes=60 * 1024 * 1024),
    )(*operands)
    return out.reshape(frame_count, rows_in - 2, columns, outputs)


def on_device(
    generator_latent_rows,
    slot_group_row,
    frame_clip_number,
    input_convolution_weight,
    first_norm_gain,
    first_convolution_weight,
    second_norm_gain,
    second_convolution_weight,
):
    frame_count = F_DEV
    slots_here = generator_latent_rows.shape[1]
    packed_rows = generator_latent_rows.shape[2]
    parts_count = lax.axis_size("rows")
    rows_here = slots_here // frame_count
    height = rows_here * parts_count
    columns = packed_rows // LATENT_CHANNELS
    band_index = lax.axis_index("rows")
    frame_group_index = lax.axis_index("tm")

    ids = jnp.broadcast_to(
        slot_group_row.astype(jnp.bfloat16)[:, :, None], (1, slots_here, ID_LANES)
    )
    packed = jnp.concatenate([generator_latent_rows, ids], axis=-1)
    parts_total = lax.axis_size("rows")
    pieces = [packed]
    for by in range(1, parts_total):
        ring = [(i, (i + by) % parts_total) for i in range(parts_total)]
        pieces.append(lax.ppermute(packed, "rows", ring))
    gathered = jnp.concatenate(pieces, axis=1)[0]
    values = gathered[:, :packed_rows]
    slot_ids = gathered[:, packed_rows].astype(jnp.int32)

    window_rows = rows_here + 4
    frame_of = jnp.arange(frame_count, dtype=jnp.int32)[:, None]
    row_of = band_index * rows_here - 2 + jnp.arange(window_rows, dtype=jnp.int32)[None, :]
    wanted = (frame_of * height + row_of).reshape(-1)
    valid = jnp.broadcast_to((row_of >= 0) & (row_of < height), (frame_count, window_rows)).reshape(-1)
    selector = ((wanted[:, None] == slot_ids[None, :]) & valid[:, None]).astype(jnp.bfloat16)
    own_window = jnp.dot(selector, values, preferred_element_type=jnp.float32).astype(jnp.bfloat16)
    prev_window = shifted(own_window, "tm", 1)
    latent = jnp.concatenate([prev_window, own_window], axis=0).reshape(
        2 * frame_count, window_rows, columns, LATENT_CHANNELS
    )

    padded_clips = jnp.concatenate([jnp.full((4,), -1, jnp.int32), frame_clip_number])
    window = lax.dynamic_slice_in_dim(padded_clips, frame_group_index * frame_count, frame_count + 4)
    current_ext = window[2:]
    keep_ext = [window[k : k + frame_count + 2] == current_ext for k in range(3)]
    current = window[4:]
    keep_own = jnp.stack(
        [(window[k + 2 : k + 2 + frame_count] == current) for k in range(3)]
    ).astype(jnp.int32).reshape(-1)

    base_ext = local_conv(latent, input_convolution_weight, keep_ext).astype(jnp.bfloat16)
    first_act = norm_act(base_ext, first_norm_gain)
    ext_rows = band_index * rows_here - 1 + jnp.arange(rows_here + 2, dtype=jnp.int32)
    row_ok = (ext_rows >= 0) & (ext_rows < height)
    first_act = jnp.where(row_ok[None, :, None, None], first_act, jnp.zeros((), jnp.bfloat16))

    gain = second_norm_gain.reshape(1, -1)
    ext_frames, ext_rows_n = first_act.shape[:2]
    second_act = conv_call(
        {"x": (0, ext_frames, 0, ext_rows_n)},
        [first_act],
        first_convolution_weight,
        keep_own,
        gain,
        "act",
        per_step=frame_count,
    )

    last = second_act[frame_count - 2 :]
    from_above = shifted(second_act[:, rows_here - 1 :], "rows", 1)
    from_below = shifted(second_act[:, :1], "rows", -1)
    prev_mid = shifted(last, "tm", 1)
    prev_above = diagonal(last[:, rows_here - 1 :], 1, 1)
    prev_below = diagonal(last[:, :1], 1, -1)
    layout = {
        "own": (2, 2 + frame_count, 1, 1 + rows_here),
        "above": (2, 2 + frame_count, 0, 1),
        "below": (2, 2 + frame_count, 1 + rows_here, 2 + rows_here),
        "mid": (0, 2, 1, 1 + rows_here),
        "corner_above": (0, 2, 0, 1),
        "corner_below": (0, 2, 1 + rows_here, 2 + rows_here),
    }
    late_layout = {name: layout[name] for name in ("own", "above", "below")}
    late_sources = [second_act, from_above, from_below]
    decoded = conv_call(
        late_layout, late_sources, second_convolution_weight, keep_own, base_ext, "res",
        firsts=(frame_count - 2,),
    )
    early_layout = dict(layout)
    for name in ("own", "above", "below"):
        early_layout[name] = (2, 4) + layout[name][2:]
    return conv_call(
        early_layout,
        [second_act, from_above, from_below, prev_mid, prev_above, prev_below],
        second_convolution_weight,
        keep_own,
        base_ext,
        "res",
        firsts=(0,),
        into=decoded,
    )


def solution(mesh):
    in_specs = (P("tm", "rows", None), P("tm", "rows"), P(), P(), P(), P(), P(), P())
    out_specs = P("tm", "rows", None, None)
    return jax.shard_map(
        on_device, mesh=mesh, in_specs=in_specs, out_specs=out_specs, check_vma=False
    )
```

```python
import functools

import jax
import jax.numpy as jnp
from jax import lax
from jax.experimental import pallas as pl
from jax.experimental.pallas import tpu as pltpu
from jax.sharding import PartitionSpec as P

LATENT_CHANNELS = 16
F_DEV = 4
ID_LANES = 128

EPSILON = 1e-06


def shifted(x, axis, by):
    devices = lax.axis_size(axis)
    pairs = [(i, i + by) for i in range(devices) if 0 <= i + by < devices]
    return lax.ppermute(x, axis, pairs)


def diagonal(x, by_tm, by_rows):
    groups, parts = lax.axis_size("tm"), lax.axis_size("rows")
    pairs = []
    for g in range(groups):
        for r in range(parts):
            dg, dr = g + by_tm, r + by_rows
            if 0 <= dg < groups and 0 <= dr < parts:
                pairs.append((g * parts + r, dg * parts + dr))
    return lax.ppermute(x, ("tm", "rows"), pairs)


def norm_act(field, gain_vec):
    values_f = field.astype(jnp.float32)
    inverse = lax.rsqrt(jnp.mean(values_f * values_f, axis=-1, keepdims=True) + EPSILON)
    return jax.nn.silu(values_f * inverse * gain_vec).astype(jnp.bfloat16)


def local_conv(extended, weight, keep_masks):
    frame_count = extended.shape[0] - 2
    height = extended.shape[1] - 2
    columns = extended.shape[2]
    channels = extended.shape[3]
    outputs = weight.shape[-1]
    padded = jnp.pad(extended, ((0, 0), (0, 0), (1, 1), (0, 0)))
    running = jnp.zeros((frame_count, height, columns, outputs), jnp.float32)
    for tap_time in range(3):
        pieces = []
        for tap_row in range(3):
            for tap_col in range(3):
                pieces.append(
                    padded[
                        tap_time : tap_time + frame_count,
                        tap_row : tap_row + height,
                        tap_col : tap_col + columns,
                    ]
                )
        stacked = jnp.concatenate(pieces, axis=-1).reshape(-1, 9 * channels)
        partial_value = jnp.dot(
            stacked,
            weight[tap_time].reshape(9 * channels, outputs),
            preferred_element_type=jnp.float32,
        )
        partial_value = partial_value.reshape(frame_count, height, columns, outputs)
        running = running + jnp.where(
            keep_masks[tap_time][:, None, None, None], partial_value, jnp.float32(0.0)
        )
    return running


def conv_kernel(keep_ref, *refs, layout, mode, per_step, firsts):
    sources = refs[: len(layout)]
    w_hbm, side_ref = refs[len(layout) : len(layout) + 2]
    o_ref, col_ref, w_ref, w_sem = refs[-4:]
    step = pl.program_id(0)
    steps = pl.num_programs(0)
    columns, channels = sources[0].shape[-2:]
    frame_count = keep_ref.shape[0] // 3
    cells = col_ref.shape[0]
    band = cells // per_step
    height = band // columns
    taps = 9 * channels

    outputs = w_ref.shape[-1] // 3

    def weight_copy(j, b):
        return pltpu.make_async_copy(
            w_hbm.at[pl.ds((j * 3 + b) * channels, channels)],
            w_ref.at[pl.ds(j * channels, channels), pl.ds(b * outputs, outputs)],
            w_sem.at[b],
        )

    def weight_wait(b):
        pltpu.make_async_copy(
            w_hbm.at[pl.ds(0, taps)], w_ref.at[:, pl.ds(b * outputs, outputs)], w_sem.at[b]
        ).wait()

    @pl.when(step == 0)
    def _():
        for b in (1, 0, 2):
            for j in range(9):
                weight_copy(j, b).start()

    def row_of(ext_frame, ext_row):
        for name, (frame_lo, frame_hi, row_lo, row_hi) in layout.items():
            if frame_lo <= ext_frame < frame_hi and row_lo <= ext_row < row_hi:
                return sources[list(layout).index(name)][ext_frame - frame_lo, ext_row - row_lo]
        raise ValueError("no source")

    for index, first in enumerate(firsts):

        @pl.when(step == index)
        def _():
            for fl in range(per_step):
                f = first + fl
                for k in range(3):
                    kept = keep_ref[k * frame_count + f] != 0
                    for a in range(3):
                        j = k * 3 + a
                        for i in range(height):
                            piece = row_of(f + k, a + i)
                            col_ref[
                                pl.ds(fl * band + i * columns, columns), pl.ds(j * channels, channels)
                            ] = jnp.where(kept, piece, jnp.zeros_like(piece))

    position = lax.broadcasted_iota(jnp.int32, (cells, outputs), 0) % columns

    @pl.when(step == 0)
    def _():
        for b in (1, 0, 2):
            weight_wait(b)

    product = jnp.dot(col_ref[...], w_ref[...], preferred_element_type=jnp.float32)
    running = None
    for b in (1, 0, 2):
        part = product[:, b * outputs : (b + 1) * outputs]
        if b == 0:
            part = jnp.where(position == 0, 0.0, pltpu.roll(part, 1, 0))
        elif b == 2:
            part = jnp.where(position == columns - 1, 0.0, pltpu.roll(part, cells - 1, 0))
        running = part if running is None else running + part
    if mode == "act":
        values_f = running.astype(jnp.bfloat16).astype(jnp.float32)
        inverse = lax.rsqrt(jnp.mean(values_f * values_f, axis=-1, keepdims=True) + EPSILON)
        scaled = values_f * inverse * side_ref[...]
        o_ref[...] = (scaled / (1.0 + jnp.exp(-scaled))).astype(o_ref.dtype)
    else:
        residual = side_ref[:, 1 : 1 + height]
        o_ref[...] = (residual.reshape(cells, outputs).astype(jnp.float32) + running).astype(
            o_ref.dtype
        )


def whole(x):
    return pl.BlockSpec(x.shape, lambda step: (0,) * x.ndim)


def conv_call(layout, sources, weight, keep, side, mode, per_step=2, firsts=None, into=None):
    columns, channels = sources[0].shape[-2:]
    frame_count = keep.shape[0] // 3
    rows_in = max(hi for (_, _, _, hi) in layout.values())
    band = (rows_in - 2) * columns
    cells = frame_count * band
    outputs = weight.shape[-1]
    weight_rows = weight.reshape(27 * channels, outputs)
    if firsts is None:
        firsts = tuple(range(0, frame_count, per_step))
    block_at = firsts[0] // per_step
    if mode == "act":
        side_spec = whole(side)
    else:
        side_spec = pl.BlockSpec(
            (per_step,) + side.shape[1:], lambda step: (1 + block_at + step, 0, 0, 0)
        )
    operands = [keep, *sources, weight_rows, side]
    extra_specs, aliases = [], {}
    if into is not None:
        extra_specs = [pl.BlockSpec(memory_space=pl.ANY)]
        aliases = {len(operands): 0}
        operands.append(into.reshape(cells, outputs))
    out = pl.pallas_call(
        functools.partial(conv_kernel, layout=layout, mode=mode, per_step=per_step, firsts=firsts),
        out_shape=jax.ShapeDtypeStruct((cells, outputs), jnp.bfloat16),
        in_specs=[pl.BlockSpec(memory_space=pltpu.SMEM)]
        + [whole(x) for x in sources]
        + [pl.BlockSpec(memory_space=pl.ANY), side_spec]
        + extra_specs,
        out_specs=pl.BlockSpec((per_step * band, outputs), lambda step: (step + block_at, 0)),
        grid=(len(firsts),),
        input_output_aliases=aliases,
        scratch_shapes=[
            pltpu.VMEM((per_step * band, 9 * channels), jnp.bfloat16),
            pltpu.VMEM((9 * channels, 3 * outputs), jnp.bfloat16),
            pltpu.SemaphoreType.DMA((3,)),
        ],
        cost_estimate=pl.CostEstimate(
            flops=2 * len(firsts) * per_step * band * 27 * channels * outputs,
            transcendentals=len(firsts) * per_step * band * outputs,
            bytes_accessed=2 * (27 * channels * outputs + 3 * len(firsts) * per_step * band * outputs),
        ),
        compiler_params=pltpu.CompilerParams(vmem_limit_bytes=60 * 1024 * 1024),
    )(*operands)
    return out.reshape(frame_count, rows_in - 2, columns, outputs)


def on_device(
    generator_latent_rows,
    slot_group_row,
    frame_clip_number,
    input_convolution_weight,
    first_norm_gain,
    first_convolution_weight,
    second_norm_gain,
    second_convolution_weight,
):
    frame_count = F_DEV
    slots_here = generator_latent_rows.shape[1]
    packed_rows = generator_latent_rows.shape[2]
    parts_count = lax.axis_size("rows")
    rows_here = slots_here // frame_count
    height = rows_here * parts_count
    columns = packed_rows // LATENT_CHANNELS
    band_index = lax.axis_index("rows")
    frame_group_index = lax.axis_index("tm")

    ids = jnp.broadcast_to(
        slot_group_row.astype(jnp.bfloat16)[:, :, None], (1, slots_here, ID_LANES)
    )
    packed = jnp.concatenate([generator_latent_rows, ids], axis=-1)
    parts_total = lax.axis_size("rows")
    pieces = [packed]
    for by in range(1, parts_total):
        ring = [(i, (i + by) % parts_total) for i in range(parts_total)]
        pieces.append(lax.ppermute(packed, "rows", ring))
    gathered = jnp.concatenate(pieces, axis=1)[0]
    values = gathered[:, :packed_rows]
    slot_ids = gathered[:, packed_rows].astype(jnp.int32)

    window_rows = rows_here + 4
    frame_of = jnp.arange(frame_count, dtype=jnp.int32)[:, None]
    row_of = band_index * rows_here - 2 + jnp.arange(window_rows, dtype=jnp.int32)[None, :]
    wanted = (frame_of * height + row_of).reshape(-1)
    valid = jnp.broadcast_to((row_of >= 0) & (row_of < height), (frame_count, window_rows)).reshape(-1)
    selector = ((wanted[:, None] == slot_ids[None, :]) & valid[:, None]).astype(jnp.bfloat16)
    own_window = jnp.dot(selector, values, preferred_element_type=jnp.float32).astype(jnp.bfloat16)
    prev_window = shifted(own_window, "tm", 1)
    latent = jnp.concatenate([prev_window, own_window], axis=0).reshape(
        2 * frame_count, window_rows, columns, LATENT_CHANNELS
    )

    padded_clips = jnp.concatenate([jnp.full((4,), -1, jnp.int32), frame_clip_number])
    window = lax.dynamic_slice_in_dim(padded_clips, frame_group_index * frame_count, frame_count + 4)
    current_ext = window[2:]
    keep_ext = [window[k : k + frame_count + 2] == current_ext for k in range(3)]
    current = window[4:]
    keep_own = jnp.stack(
        [(window[k + 2 : k + 2 + frame_count] == current) for k in range(3)]
    ).astype(jnp.int32).reshape(-1)

    base_ext = local_conv(latent, input_convolution_weight, keep_ext).astype(jnp.bfloat16)
    first_act = norm_act(base_ext, first_norm_gain)
    ext_rows = band_index * rows_here - 1 + jnp.arange(rows_here + 2, dtype=jnp.int32)
    row_ok = (ext_rows >= 0) & (ext_rows < height)
    first_act = jnp.where(row_ok[None, :, None, None], first_act, jnp.zeros((), jnp.bfloat16))

    gain = second_norm_gain.reshape(1, -1)
    ext_frames, ext_rows_n = first_act.shape[:2]
    second_act = conv_call(
        {"x": (0, ext_frames, 0, ext_rows_n)},
        [first_act],
        first_convolution_weight,
        keep_own,
        gain,
        "act",
        per_step=frame_count,
    )

    last = second_act[frame_count - 2 :]
    from_above = shifted(second_act[:, rows_here - 1 :], "rows", 1)
    from_below = shifted(second_act[:, :1], "rows", -1)
    prev_mid = shifted(last, "tm", 1)
    prev_above = shifted(from_above[frame_count - 2 :], "tm", 1)
    prev_below = shifted(from_below[frame_count - 2 :], "tm", 1)
    layout = {
        "own": (2, 2 + frame_count, 1, 1 + rows_here),
        "above": (2, 2 + frame_count, 0, 1),
        "below": (2, 2 + frame_count, 1 + rows_here, 2 + rows_here),
        "mid": (0, 2, 1, 1 + rows_here),
        "corner_above": (0, 2, 0, 1),
        "corner_below": (0, 2, 1 + rows_here, 2 + rows_here),
    }
    late_layout = {name: layout[name] for name in ("own", "above", "below")}
    late_sources = [second_act, from_above, from_below]
    decoded = conv_call(
        late_layout, late_sources, second_convolution_weight, keep_own, base_ext, "res",
        firsts=(frame_count - 2,),
    )
    return conv_call(
        layout,
        [second_act, from_above, from_below, prev_mid, prev_above, prev_below],
        second_convolution_weight,
        keep_own,
        base_ext,
        "res",
        firsts=(0,),
        into=decoded,
    )


def solution(mesh):
    in_specs = (P("tm", "rows", None), P("tm", "rows"), P(), P(), P(), P(), P(), P())
    out_specs = P("tm", "rows", None, None)
    return jax.shard_map(
        on_device, mesh=mesh, in_specs=in_specs, out_specs=out_specs, check_vma=False
    )
```

```python
import functools

import jax
import jax.numpy as jnp
from jax import lax
from jax.experimental import pallas as pl
from jax.experimental.pallas import tpu as pltpu
from jax.sharding import PartitionSpec as P

LATENT_CHANNELS = 16
F_DEV = 4
ID_LANES = 128

EPSILON = 1e-06


def shifted(x, axis, by):
    devices = lax.axis_size(axis)
    pairs = [(i, i + by) for i in range(devices) if 0 <= i + by < devices]
    return lax.ppermute(x, axis, pairs)


def diagonal(x, by_tm, by_rows):
    groups, parts = lax.axis_size("tm"), lax.axis_size("rows")
    pairs = []
    for g in range(groups):
        for r in range(parts):
            dg, dr = g + by_tm, r + by_rows
            if 0 <= dg < groups and 0 <= dr < parts:
                pairs.append((g * parts + r, dg * parts + dr))
    return lax.ppermute(x, ("tm", "rows"), pairs)


def norm_act(field, gain_vec):
    values_f = field.astype(jnp.float32)
    inverse = lax.rsqrt(jnp.mean(values_f * values_f, axis=-1, keepdims=True) + EPSILON)
    return jax.nn.silu(values_f * inverse * gain_vec).astype(jnp.bfloat16)


def local_conv(extended, weight, keep_masks):
    frame_count = extended.shape[0] - 2
    height = extended.shape[1] - 2
    columns = extended.shape[2]
    channels = extended.shape[3]
    outputs = weight.shape[-1]
    padded = jnp.pad(extended, ((0, 0), (0, 0), (1, 1), (0, 0)))
    running = jnp.zeros((frame_count, height, columns, outputs), jnp.float32)
    for tap_time in range(3):
        pieces = []
        for tap_row in range(3):
            for tap_col in range(3):
                pieces.append(
                    padded[
                        tap_time : tap_time + frame_count,
                        tap_row : tap_row + height,
                        tap_col : tap_col + columns,
                    ]
                )
        stacked = jnp.concatenate(pieces, axis=-1).reshape(-1, 9 * channels)
        partial_value = jnp.dot(
            stacked,
            weight[tap_time].reshape(9 * channels, outputs),
            preferred_element_type=jnp.float32,
        )
        partial_value = partial_value.reshape(frame_count, height, columns, outputs)
        running = running + jnp.where(
            keep_masks[tap_time][:, None, None, None], partial_value, jnp.float32(0.0)
        )
    return running


def conv_kernel(keep_ref, *refs, layout, mode, per_step, firsts):
    sources = refs[: len(layout)]
    w_hbm, side_ref = refs[len(layout) : len(layout) + 2]
    o_ref, col_ref, w_ref, w_sem = refs[-4:]
    step = pl.program_id(0)
    steps = pl.num_programs(0)
    columns, channels = sources[0].shape[-2:]
    frame_count = keep_ref.shape[0] // 3
    cells = col_ref.shape[0]
    band = cells // per_step
    height = band // columns
    taps = 9 * channels

    outputs = w_ref.shape[-1] // 3

    def weight_copy(j, b):
        return pltpu.make_async_copy(
            w_hbm.at[pl.ds((j * 3 + b) * channels, channels)],
            w_ref.at[pl.ds(j * channels, channels), pl.ds(b * outputs, outputs)],
            w_sem.at[b],
        )

    def weight_wait(b):
        pltpu.make_async_copy(
            w_hbm.at[pl.ds(0, taps)], w_ref.at[:, pl.ds(b * outputs, outputs)], w_sem.at[b]
        ).wait()

    @pl.when(step == 0)
    def _():
        for b in (1, 0, 2):
            for j in range(9):
                weight_copy(j, b).start()

    def row_of(ext_frame, ext_row):
        for name, (frame_lo, frame_hi, row_lo, row_hi) in layout.items():
            if frame_lo <= ext_frame < frame_hi and row_lo <= ext_row < row_hi:
                return sources[list(layout).index(name)][ext_frame - frame_lo, ext_row - row_lo]
        raise ValueError("no source")

    for index, first in enumerate(firsts):

        @pl.when(step == index)
        def _():
            for fl in range(per_step):
                f = first + fl
                for k in range(3):
                    kept = keep_ref[k * frame_count + f] != 0
                    for a in range(3):
                        j = k * 3 + a
                        for i in range(height):
                            piece = row_of(f + k, a + i)
                            col_ref[
                                pl.ds(fl * band + i * columns, columns), pl.ds(j * channels, channels)
                            ] = jnp.where(kept, piece, jnp.zeros_like(piece))

    position = lax.broadcasted_iota(jnp.int32, (cells, outputs), 0) % columns

    @pl.when(step == 0)
    def _():
        for b in (1, 0, 2):
            weight_wait(b)

    product = jnp.dot(col_ref[...], w_ref[...], preferred_element_type=jnp.float32)
    running = None
    for b in (1, 0, 2):
        part = product[:, b * outputs : (b + 1) * outputs]
        if b == 0:
            part = jnp.where(position == 0, 0.0, pltpu.roll(part, 1, 0))
        elif b == 2:
            part = jnp.where(position == columns - 1, 0.0, pltpu.roll(part, cells - 1, 0))
        running = part if running is None else running + part
    if mode == "act":
        values_f = running.astype(jnp.bfloat16).astype(jnp.float32)
        inverse = lax.rsqrt(jnp.mean(values_f * values_f, axis=-1, keepdims=True) + EPSILON)
        scaled = values_f * inverse * side_ref[...]
        o_ref[...] = (scaled / (1.0 + jnp.exp(-scaled))).astype(o_ref.dtype)
    else:
        residual = side_ref[:, 1 : 1 + height]
        o_ref[...] = (residual.reshape(cells, outputs).astype(jnp.float32) + running).astype(
            o_ref.dtype
        )


def whole(x):
    return pl.BlockSpec(x.shape, lambda step: (0,) * x.ndim)


def conv_call(layout, sources, weight, keep, side, mode, per_step=2, firsts=None, into=None):
    columns, channels = sources[0].shape[-2:]
    frame_count = keep.shape[0] // 3
    rows_in = max(hi for (_, _, _, hi) in layout.values())
    band = (rows_in - 2) * columns
    cells = frame_count * band
    outputs = weight.shape[-1]
    weight_rows = weight.reshape(27 * channels, outputs)
    if firsts is None:
        firsts = tuple(range(0, frame_count, per_step))
    block_at = firsts[0] // per_step
    if mode == "act":
        side_spec = whole(side)
    else:
        side_spec = pl.BlockSpec(
            (per_step,) + side.shape[1:], lambda step: (1 + block_at + step, 0, 0, 0)
        )
    operands = [keep, *sources, weight_rows, side]
    extra_specs, aliases = [], {}
    if into is not None:
        extra_specs = [pl.BlockSpec(memory_space=pl.ANY)]
        aliases = {len(operands): 0}
        operands.append(into.reshape(cells, outputs))
    out = pl.pallas_call(
        functools.partial(conv_kernel, layout=layout, mode=mode, per_step=per_step, firsts=firsts),
        out_shape=jax.ShapeDtypeStruct((cells, outputs), jnp.bfloat16),
        in_specs=[pl.BlockSpec(memory_space=pltpu.SMEM)]
        + [whole(x) for x in sources]
        + [pl.BlockSpec(memory_space=pl.ANY), side_spec]
        + extra_specs,
        out_specs=pl.BlockSpec((per_step * band, outputs), lambda step: (step + block_at, 0)),
        grid=(len(firsts),),
        input_output_aliases=aliases,
        scratch_shapes=[
            pltpu.VMEM((per_step * band, 9 * channels), jnp.bfloat16),
            pltpu.VMEM((9 * channels, 3 * outputs), jnp.bfloat16),
            pltpu.SemaphoreType.DMA((3,)),
        ],
        cost_estimate=pl.CostEstimate(
            flops=2 * len(firsts) * per_step * band * 27 * channels * outputs,
            transcendentals=len(firsts) * per_step * band * outputs,
            bytes_accessed=2 * (27 * channels * outputs + 3 * len(firsts) * per_step * band * outputs),
        ),
        compiler_params=pltpu.CompilerParams(vmem_limit_bytes=60 * 1024 * 1024),
    )(*operands)
    return out.reshape(frame_count, rows_in - 2, columns, outputs)


def on_device(
    generator_latent_rows,
    slot_group_row,
    frame_clip_number,
    input_convolution_weight,
    first_norm_gain,
    first_convolution_weight,
    second_norm_gain,
    second_convolution_weight,
):
    frame_count = F_DEV
    slots_here = generator_latent_rows.shape[1]
    packed_rows = generator_latent_rows.shape[2]
    parts_count = lax.axis_size("rows")
    rows_here = slots_here // frame_count
    height = rows_here * parts_count
    columns = packed_rows // LATENT_CHANNELS
    band_index = lax.axis_index("rows")
    frame_group_index = lax.axis_index("tm")

    ids = jnp.broadcast_to(
        slot_group_row.astype(jnp.bfloat16)[:, :, None], (1, slots_here, ID_LANES)
    )
    packed = jnp.concatenate([generator_latent_rows, ids], axis=-1)
    parts_total = lax.axis_size("rows")
    pieces = [packed]
    for by in range(1, parts_total):
        ring = [(i, (i + by) % parts_total) for i in range(parts_total)]
        pieces.append(lax.ppermute(packed, "rows", ring))
    gathered = jnp.concatenate(pieces, axis=1)[0]
    values = gathered[:, :packed_rows]
    slot_ids = gathered[:, packed_rows].astype(jnp.int32)

    window_rows = rows_here + 4
    frame_of = jnp.arange(frame_count, dtype=jnp.int32)[:, None]
    row_of = band_index * rows_here - 2 + jnp.arange(window_rows, dtype=jnp.int32)[None, :]
    wanted = (frame_of * height + row_of).reshape(-1)
    valid = jnp.broadcast_to((row_of >= 0) & (row_of < height), (frame_count, window_rows)).reshape(-1)
    selector = ((wanted[:, None] == slot_ids[None, :]) & valid[:, None]).astype(jnp.bfloat16)
    own_window = jnp.dot(selector, values, preferred_element_type=jnp.float32).astype(jnp.bfloat16)
    prev_window = shifted(own_window, "tm", 1)
    latent = jnp.concatenate([prev_window, own_window], axis=0).reshape(
        2 * frame_count, window_rows, columns, LATENT_CHANNELS
    )

    padded_clips = jnp.concatenate([jnp.full((4,), -1, jnp.int32), frame_clip_number])
    window = lax.dynamic_slice_in_dim(padded_clips, frame_group_index * frame_count, frame_count + 4)
    current_ext = window[2:]
    keep_ext = [window[k : k + frame_count + 2] == current_ext for k in range(3)]
    current = window[4:]
    keep_own = jnp.stack(
        [(window[k + 2 : k + 2 + frame_count] == current) for k in range(3)]
    ).astype(jnp.int32).reshape(-1)

    base_ext = local_conv(latent, input_convolution_weight, keep_ext).astype(jnp.bfloat16)
    first_act = norm_act(base_ext, first_norm_gain)
    ext_rows = band_index * rows_here - 1 + jnp.arange(rows_here + 2, dtype=jnp.int32)
    row_ok = (ext_rows >= 0) & (ext_rows < height)
    first_act = jnp.where(row_ok[None, :, None, None], first_act, jnp.zeros((), jnp.bfloat16))

    gain = second_norm_gain.reshape(1, -1)
    ext_frames, ext_rows_n = first_act.shape[:2]
    second_act = conv_call(
        {"x": (0, ext_frames, 0, ext_rows_n)},
        [first_act],
        first_convolution_weight,
        keep_own,
        gain,
        "act",
        per_step=frame_count,
    )

    last = second_act[frame_count - 2 :]
    from_above = shifted(second_act[:, rows_here - 1 :], "rows", 1)
    from_below = shifted(second_act[:, :1], "rows", -1)
    last_ext = jnp.concatenate(
        [from_above[frame_count - 2 :], last, from_below[frame_count - 2 :]], axis=1
    )
    prev_ext = shifted(last_ext, "tm", 1)
    prev_above = prev_ext[:, :1]
    prev_mid = prev_ext[:, 1 : 1 + rows_here]
    prev_below = prev_ext[:, 1 + rows_here :]
    layout = {
        "own": (2, 2 + frame_count, 1, 1 + rows_here),
        "above": (2, 2 + frame_count, 0, 1),
        "below": (2, 2 + frame_count, 1 + rows_here, 2 + rows_here),
        "mid": (0, 2, 1, 1 + rows_here),
        "corner_above": (0, 2, 0, 1),
        "corner_below": (0, 2, 1 + rows_here, 2 + rows_here),
    }
    late_layout = {name: layout[name] for name in ("own", "above", "below")}
    late_sources = [second_act, from_above, from_below]
    decoded = conv_call(
        late_layout, late_sources, second_convolution_weight, keep_own, base_ext, "res",
        firsts=(frame_count - 2,),
    )
    return conv_call(
        layout,
        [second_act, from_above, from_below, prev_mid, prev_above, prev_below],
        second_convolution_weight,
        keep_own,
        base_ext,
        "res",
        firsts=(0,),
        into=decoded,
    )


def solution(mesh):
    in_specs = (P("tm", "rows", None), P("tm", "rows"), P(), P(), P(), P(), P(), P())
    out_specs = P("tm", "rows", None, None)
    return jax.shard_map(
        on_device, mesh=mesh, in_specs=in_specs, out_specs=out_specs, check_vma=False
    )
```

```python
import functools

import jax
import jax.numpy as jnp
from jax import lax
from jax.experimental import pallas as pl
from jax.experimental.pallas import tpu as pltpu
from jax.sharding import PartitionSpec as P

LATENT_CHANNELS = 16
F_DEV = 4
ID_LANES = 128

EPSILON = 1e-06


def shifted(x, axis, by):
    devices = lax.axis_size(axis)
    pairs = [(i, i + by) for i in range(devices) if 0 <= i + by < devices]
    return lax.ppermute(x, axis, pairs)


def diagonal(x, by_tm, by_rows):
    groups, parts = lax.axis_size("tm"), lax.axis_size("rows")
    pairs = []
    for g in range(groups):
        for r in range(parts):
            dg, dr = g + by_tm, r + by_rows
            if 0 <= dg < groups and 0 <= dr < parts:
                pairs.append((g * parts + r, dg * parts + dr))
    return lax.ppermute(x, ("tm", "rows"), pairs)


def norm_act(field, gain_vec):
    values_f = field.astype(jnp.float32)
    inverse = lax.rsqrt(jnp.mean(values_f * values_f, axis=-1, keepdims=True) + EPSILON)
    return jax.nn.silu(values_f * inverse * gain_vec).astype(jnp.bfloat16)


def local_conv(extended, weight, keep_masks):
    frame_count = extended.shape[0] - 2
    height = extended.shape[1] - 2
    columns = extended.shape[2]
    channels = extended.shape[3]
    outputs = weight.shape[-1]
    padded = jnp.pad(extended, ((0, 0), (0, 0), (1, 1), (0, 0)))
    running = jnp.zeros((frame_count, height, columns, outputs), jnp.float32)
    for tap_time in range(3):
        pieces = []
        for tap_row in range(3):
            for tap_col in range(3):
                pieces.append(
                    padded[
                        tap_time : tap_time + frame_count,
                        tap_row : tap_row + height,
                        tap_col : tap_col + columns,
                    ]
                )
        stacked = jnp.concatenate(pieces, axis=-1).reshape(-1, 9 * channels)
        partial_value = jnp.dot(
            stacked,
            weight[tap_time].reshape(9 * channels, outputs),
            preferred_element_type=jnp.float32,
        )
        partial_value = partial_value.reshape(frame_count, height, columns, outputs)
        running = running + jnp.where(
            keep_masks[tap_time][:, None, None, None], partial_value, jnp.float32(0.0)
        )
    return running


def conv_kernel(keep_ref, *refs, layout, mode, per_step, firsts):
    sources = refs[: len(layout)]
    w_hbm, side_ref = refs[len(layout) : len(layout) + 2]
    o_ref, col_ref, w_ref, w_sem = refs[-4:]
    step = pl.program_id(0)
    steps = pl.num_programs(0)
    columns, channels = sources[0].shape[-2:]
    frame_count = keep_ref.shape[0] // 3
    cells = col_ref.shape[0]
    band = cells // per_step
    height = band // columns
    taps = 9 * channels

    outputs = w_ref.shape[-1] // 3

    def weight_copy(j, b):
        return pltpu.make_async_copy(
            w_hbm.at[pl.ds((j * 3 + b) * channels, channels)],
            w_ref.at[pl.ds(j * channels, channels), pl.ds(b * outputs, outputs)],
            w_sem.at[b],
        )

    def weight_wait(b):
        pltpu.make_async_copy(
            w_hbm.at[pl.ds(0, taps)], w_ref.at[:, pl.ds(b * outputs, outputs)], w_sem.at[b]
        ).wait()

    @pl.when(step == 0)
    def _():
        for b in (1, 0, 2):
            for j in range(9):
                weight_copy(j, b).start()

    def row_of(ext_frame, ext_row):
        for name, (frame_lo, frame_hi, row_lo, row_hi) in layout.items():
            if frame_lo <= ext_frame < frame_hi and row_lo <= ext_row < row_hi:
                return sources[list(layout).index(name)][ext_frame - frame_lo, ext_row - row_lo]
        raise ValueError("no source")

    for index, first in enumerate(firsts):

        @pl.when(step == index)
        def _():
            for fl in range(per_step):
                f = first + fl
                for k in range(3):
                    kept = keep_ref[k * frame_count + f] != 0
                    for a in range(3):
                        j = k * 3 + a
                        for i in range(height):
                            piece = row_of(f + k, a + i)
                            if k == 2:
                                kept_piece = piece
                            else:
                                kept_piece = jnp.where(kept, piece, jnp.zeros_like(piece))
                            col_ref[
                                pl.ds(fl * band + i * columns, columns), pl.ds(j * channels, channels)
                            ] = kept_piece

    position = lax.broadcasted_iota(jnp.int32, (cells, outputs), 0) % columns

    @pl.when(step == 0)
    def _():
        for b in (1, 0, 2):
            weight_wait(b)

    product = jnp.dot(col_ref[...], w_ref[...], preferred_element_type=jnp.float32)
    running = None
    for b in (1, 0, 2):
        part = product[:, b * outputs : (b + 1) * outputs]
        if b == 0:
            part = jnp.where(position == 0, 0.0, pltpu.roll(part, 1, 0))
        elif b == 2:
            part = jnp.where(position == columns - 1, 0.0, pltpu.roll(part, cells - 1, 0))
        running = part if running is None else running + part
    if mode == "act":
        values_f = running.astype(jnp.bfloat16).astype(jnp.float32)
        inverse = lax.rsqrt(jnp.mean(values_f * values_f, axis=-1, keepdims=True) + EPSILON)
        scaled = values_f * inverse * side_ref[...]
        o_ref[...] = (scaled / (1.0 + jnp.exp(-scaled))).astype(o_ref.dtype)
    else:
        residual = side_ref[:, 1 : 1 + height]
        o_ref[...] = (residual.reshape(cells, outputs).astype(jnp.float32) + running).astype(
            o_ref.dtype
        )


def whole(x):
    return pl.BlockSpec(x.shape, lambda step: (0,) * x.ndim)


def conv_call(layout, sources, weight, keep, side, mode, per_step=2, firsts=None, into=None):
    columns, channels = sources[0].shape[-2:]
    frame_count = keep.shape[0] // 3
    rows_in = max(hi for (_, _, _, hi) in layout.values())
    band = (rows_in - 2) * columns
    cells = frame_count * band
    outputs = weight.shape[-1]
    weight_rows = weight.reshape(27 * channels, outputs)
    if firsts is None:
        firsts = tuple(range(0, frame_count, per_step))
    block_at = firsts[0] // per_step
    if mode == "act":
        side_spec = whole(side)
    else:
        side_spec = pl.BlockSpec(
            (per_step,) + side.shape[1:], lambda step: (1 + block_at + step, 0, 0, 0)
        )
    operands = [keep, *sources, weight_rows, side]
    extra_specs, aliases = [], {}
    if into is not None:
        extra_specs = [pl.BlockSpec(memory_space=pl.ANY)]
        aliases = {len(operands): 0}
        operands.append(into.reshape(cells, outputs))
    out = pl.pallas_call(
        functools.partial(conv_kernel, layout=layout, mode=mode, per_step=per_step, firsts=firsts),
        out_shape=jax.ShapeDtypeStruct((cells, outputs), jnp.bfloat16),
        in_specs=[pl.BlockSpec(memory_space=pltpu.SMEM)]
        + [whole(x) for x in sources]
        + [pl.BlockSpec(memory_space=pl.ANY), side_spec]
        + extra_specs,
        out_specs=pl.BlockSpec((per_step * band, outputs), lambda step: (step + block_at, 0)),
        grid=(len(firsts),),
        input_output_aliases=aliases,
        scratch_shapes=[
            pltpu.VMEM((per_step * band, 9 * channels), jnp.bfloat16),
            pltpu.VMEM((9 * channels, 3 * outputs), jnp.bfloat16),
            pltpu.SemaphoreType.DMA((3,)),
        ],
        cost_estimate=pl.CostEstimate(
            flops=2 * len(firsts) * per_step * band * 27 * channels * outputs,
            transcendentals=len(firsts) * per_step * band * outputs,
            bytes_accessed=2 * (27 * channels * outputs + 3 * len(firsts) * per_step * band * outputs),
        ),
        compiler_params=pltpu.CompilerParams(vmem_limit_bytes=60 * 1024 * 1024),
    )(*operands)
    return out.reshape(frame_count, rows_in - 2, columns, outputs)


def on_device(
    generator_latent_rows,
    slot_group_row,
    frame_clip_number,
    input_convolution_weight,
    first_norm_gain,
    first_convolution_weight,
    second_norm_gain,
    second_convolution_weight,
):
    frame_count = F_DEV
    slots_here = generator_latent_rows.shape[1]
    packed_rows = generator_latent_rows.shape[2]
    parts_count = lax.axis_size("rows")
    rows_here = slots_here // frame_count
    height = rows_here * parts_count
    columns = packed_rows // LATENT_CHANNELS
    band_index = lax.axis_index("rows")
    frame_group_index = lax.axis_index("tm")

    ids = jnp.broadcast_to(
        slot_group_row.astype(jnp.bfloat16)[:, :, None], (1, slots_here, ID_LANES)
    )
    packed = jnp.concatenate([generator_latent_rows, ids], axis=-1)
    parts_total = lax.axis_size("rows")
    pieces = [packed]
    for by in range(1, parts_total):
        ring = [(i, (i + by) % parts_total) for i in range(parts_total)]
        pieces.append(lax.ppermute(packed, "rows", ring))
    gathered = jnp.concatenate(pieces, axis=1)[0]
    values = gathered[:, :packed_rows]
    slot_ids = gathered[:, packed_rows].astype(jnp.int32)

    window_rows = rows_here + 4
    frame_of = jnp.arange(frame_count, dtype=jnp.int32)[:, None]
    row_of = band_index * rows_here - 2 + jnp.arange(window_rows, dtype=jnp.int32)[None, :]
    wanted = (frame_of * height + row_of).reshape(-1)
    valid = jnp.broadcast_to((row_of >= 0) & (row_of < height), (frame_count, window_rows)).reshape(-1)
    selector = ((wanted[:, None] == slot_ids[None, :]) & valid[:, None]).astype(jnp.bfloat16)
    own_window = jnp.dot(selector, values, preferred_element_type=jnp.float32).astype(jnp.bfloat16)
    prev_window = shifted(own_window, "tm", 1)
    latent = jnp.concatenate([prev_window, own_window], axis=0).reshape(
        2 * frame_count, window_rows, columns, LATENT_CHANNELS
    )

    padded_clips = jnp.concatenate([jnp.full((4,), -1, jnp.int32), frame_clip_number])
    window = lax.dynamic_slice_in_dim(padded_clips, frame_group_index * frame_count, frame_count + 4)
    current_ext = window[2:]
    keep_ext = [window[k : k + frame_count + 2] == current_ext for k in range(3)]
    current = window[4:]
    keep_own = jnp.stack(
        [(window[k + 2 : k + 2 + frame_count] == current) for k in range(3)]
    ).astype(jnp.int32).reshape(-1)

    base_ext = local_conv(latent, input_convolution_weight, keep_ext).astype(jnp.bfloat16)
    first_act = norm_act(base_ext, first_norm_gain)
    ext_rows = band_index * rows_here - 1 + jnp.arange(rows_here + 2, dtype=jnp.int32)
    row_ok = (ext_rows >= 0) & (ext_rows < height)
    first_act = jnp.where(row_ok[None, :, None, None], first_act, jnp.zeros((), jnp.bfloat16))

    gain = second_norm_gain.reshape(1, -1)
    ext_frames, ext_rows_n = first_act.shape[:2]
    second_act = conv_call(
        {"x": (0, ext_frames, 0, ext_rows_n)},
        [first_act],
        first_convolution_weight,
        keep_own,
        gain,
        "act",
        per_step=frame_count,
    )

    last = second_act[frame_count - 2 :]
    from_above = shifted(second_act[:, rows_here - 1 :], "rows", 1)
    from_below = shifted(second_act[:, :1], "rows", -1)
    prev_mid = shifted(last, "tm", 1)
    prev_above = shifted(from_above[frame_count - 2 :], "tm", 1)
    prev_below = shifted(from_below[frame_count - 2 :], "tm", 1)
    layout = {
        "own": (2, 2 + frame_count, 1, 1 + rows_here),
        "above": (2, 2 + frame_count, 0, 1),
        "below": (2, 2 + frame_count, 1 + rows_here, 2 + rows_here),
        "mid": (0, 2, 1, 1 + rows_here),
        "corner_above": (0, 2, 0, 1),
        "corner_below": (0, 2, 1 + rows_here, 2 + rows_here),
    }
    late_layout = {name: layout[name] for name in ("own", "above", "below")}
    late_sources = [second_act, from_above, from_below]
    decoded = conv_call(
        late_layout, late_sources, second_convolution_weight, keep_own, base_ext, "res",
        firsts=(frame_count - 2,),
    )
    return conv_call(
        layout,
        [second_act, from_above, from_below, prev_mid, prev_above, prev_below],
        second_convolution_weight,
        keep_own,
        base_ext,
        "res",
        firsts=(0,),
        into=decoded,
    )


def solution(mesh):
    in_specs = (P("tm", "rows", None), P("tm", "rows"), P(), P(), P(), P(), P(), P())
    out_specs = P("tm", "rows", None, None)
    return jax.shard_map(
        on_device, mesh=mesh, in_specs=in_specs, out_specs=out_specs, check_vma=False
    )
```
